32 devices in a mesh: ctx: 4 (over y, x), pair: 4 (over z), dp: 2 (over core).
Axes of the slice: x: 2, y: 2, z: 4, core: 2. Of those that a mesh axis runs over, the one named last changes fastest.
Arguments:
- queries: bfloat16 [8, 4, 128, 2048], P(('dp', 'ctx'), 'pair'), parts along dimension 0, may hold values from -8 to 8
- resp_keys: bfloat16 [8, 4, 128, 1024], P(('dp', 'ctx'), 'pair'), parts along dimension 0, may hold values from -6 to 6
- resp_values: bfloat16 [8, 4, 128, 1024], P(('dp', 'ctx'), 'pair'), parts along dimension 0, may hold values from -6 to 6
- d_out: bfloat16 [8, 4, 128, 2048], P(('dp', 'ctx'), 'pair'), parts along dimension 0, may hold values from -6 to 6
- prefix_kv: bfloat16 [4, 512, 2, 1024], P('dp', 'ctx', None, 'pair'), parts along dimension 0, may hold values from -8 to 8
- prefix_blocks: int32 [8, 4, 4], P(('dp', 'ctx'), 'pair'), parts along dimension 0, may hold values 0 or 1
- resp_lengths: int32 [8, 4], P(('dp', 'ctx'), 'pair'), parts along dimension 0, may hold values from 32 to 128, as said below
- pair_prompt: int32 [8], P('dp'), parts along dimension 0, may hold values from 0 to 1, as said below
Outputs:
- d_queries: bfloat16 [8, 4, 128, 2048], P(('dp', 'ctx'), 'pair'), parts along dimension 0
- d_resp_keys: bfloat16 [8, 4, 128, 1024], P(('dp', 'ctx'), 'pair'), parts along dimension 0
- d_resp_values: bfloat16 [8, 4, 128, 1024], P(('dp', 'ctx'), 'pair'), parts along dimension 0
- d_prefix: float32 [4, 512, 2, 1024], P('dp', 'ctx', None, 'pair'), parts along dimension 0
The draws below stay inside these ranges and needn't reach their ends.
There are 2 independent parts, one for each index of `dp`. The reference program is written for one: setup_inputs(seed, part) draws one part's arguments, and reference() takes and returns one part's arrays. A program takes and returns all parts, laid end to end along the dimension named above; each array names one. Nothing has to cross between parts.
Inputs may be any that keep to these rules, and one draw needn't show every extreme that they name: `pair_prompt`: each prompt is answered by exactly two indices of pair, one chosen and one rejected response. `resp_lengths`: some response fills all 128 slots.
All inputs are finite; a program needn't handle non-finite values. No bound on the sum of `prefix_blocks` on one device may be relied on, other than what follows from the above.
Results may differ from the reference program's by a relative error of at most 0.012.
The reference program's roundings to bfloat16 on the way count: a program that leaves them out, or rounds other values in their place, can miss the bound.
Values may be sent and summed in bfloat16 or wider, within the bound.
No kernel may reach another device: no remote copies, remote signals or barrier semaphores. Data moves between devices by JAX's collectives and lax.ppermute only.
A program may use at most 128 MiB of HBM per device.

```python
import jax
import jax.numpy as jnp
from jax import lax

KV_HEADS = 8
GROUP = 2
HEAD_DIM = 128
BLOCK = 128
RESP = 128
Q_WIDTH = 2048
KV_WIDTH = 1024
PRE = 512
BLOCKS = 4
PROMPTS = 2
N_CTX = 4
N_PAIR = 4


def draw_queries(key, part):
    drawn = jax.random.truncated_normal(jax.random.fold_in(key, 3), -8.0, 8.0, (N_CTX, N_PAIR, RESP, Q_WIDTH), jnp.float32)
    return drawn.astype(jnp.bfloat16)


def draw_prefix_kv(key, part):
    drawn = jax.random.truncated_normal(jax.random.fold_in(key, 5), -8.0, 8.0, (PROMPTS, PRE, 2, KV_WIDTH), jnp.float32)
    return drawn.astype(jnp.bfloat16)


def draw_resp_lengths(key, part):
    drawn = jax.random.randint(jax.random.fold_in(key, 11), (N_CTX * N_PAIR,), RESP // 4, RESP + 1, jnp.int32)
    fullest = jax.random.randint(jax.random.fold_in(key, 13), (), 0, N_CTX * N_PAIR, jnp.int32)
    drawn = jnp.where(jnp.arange(N_CTX * N_PAIR) == fullest, RESP, drawn).astype(jnp.int32)
    return drawn.reshape(N_CTX, N_PAIR)


def draw_pair_prompt(key, part):
    order = jax.random.permutation(jax.random.fold_in(key, 17), N_PAIR)
    labels = (jnp.arange(N_PAIR) // 2).astype(jnp.int32)
    return jnp.zeros((N_PAIR,), jnp.int32).at[order].set(labels)


def plant(values, rng, least, top_value):
    longest = values.shape.index(max(values.shape))
    spots = []
    for shift in (0, 1):
        where = [jax.random.randint(jax.random.fold_in(rng, axis), (), 0, length) for axis, length in enumerate(values.shape)]
        where[longest] = (where[longest] + shift) % values.shape[longest]
        spots.append(tuple(where))
    return values.at[spots[0]].set(least).at[spots[1]].set(top_value)


def shard_levels(stream_key, dims, split, smallest, largest):
    def one(position, shards_of):
        steps = jax.random.uniform(jax.random.fold_in(jax.random.fold_in(stream_key, 6), position), (shards_of,), jnp.float32, smallest / len(split), largest / len(split))
        return jnp.repeat(jnp.exp(steps), dims[position] // shards_of).reshape((-1,) + (1,) * (len(dims) - position - 1))

    gain = one(*split[0])
    for cut in split[1:]:
        gain = gain * one(*cut)
    return gain


def scatter_about(rng, extent, width, limit, shards=(), held_as=jnp.bfloat16):
    loudness = shard_levels(rng, extent, shards, -0.22, 0.18) if shards else 1.0
    values = jax.random.normal(rng, extent, jnp.float32) * width * loudness
    return jnp.minimum(jnp.maximum(values, -limit), limit).astype(held_as)


def setup_inputs(seed: int = 0, part: int = 0) -> dict:
    keys = jax.random.split(jax.random.key(seed), 9)
    part_keys = jax.random.split(jax.random.fold_in(keys[8], part), 9)
    queries = draw_queries(jax.random.fold_in(jax.random.fold_in(keys[8], part), 71), part)
    resp_keys = scatter_about(part_keys[1], (N_CTX, N_PAIR, RESP, KV_WIDTH), 1.0, 6.0, ((0, 4), (1, 4)))
    resp_values = scatter_about(part_keys[2], (N_CTX, N_PAIR, RESP, KV_WIDTH), 1.0, 6.0, ((0, 4), (1, 4)))
    d_out = scatter_about(part_keys[3], (N_CTX, N_PAIR, RESP, Q_WIDTH), 1.0, 6.0, ((0, 4), (1, 4)))
    prefix_kv = draw_prefix_kv(jax.random.fold_in(jax.random.fold_in(keys[8], part), 71), part)
    prefix_blocks = plant((jax.random.randint(part_keys[5], (N_CTX, N_PAIR, BLOCKS), 0, 4) < 3).astype(jnp.int32), jax.random.fold_in(part_keys[5], 1), 0, 1)
    resp_lengths = draw_resp_lengths(jax.random.fold_in(jax.random.fold_in(keys[8], part), 71), part)
    pair_prompt = draw_pair_prompt(jax.random.fold_in(jax.random.fold_in(keys[8], part), 71), part)
    return {"queries": queries, "resp_keys": resp_keys, "resp_values": resp_values, "d_out": d_out, "prefix_kv": prefix_kv, "prefix_blocks": prefix_blocks, "resp_lengths": resp_lengths, "pair_prompt": pair_prompt}


scale_factor = 144.0 ** -0.5
neg_big = -1.0e30


def response_grads(query_rows, own_keys, own_values, grad_in, prefix_keys, prefix_values, visible, length):
    resp_rows = query_rows.shape[0]
    pre_rows = prefix_keys.shape[0]
    keys_three = jnp.concatenate([prefix_keys, own_keys], 0).reshape(pre_rows + resp_rows, KV_HEADS, HEAD_DIM).astype(jnp.float32)
    values_three = jnp.concatenate([prefix_values, own_values], 0).reshape(pre_rows + resp_rows, KV_HEADS, HEAD_DIM).astype(jnp.float32)
    query_four = query_rows.reshape(resp_rows, KV_HEADS, GROUP, HEAD_DIM).astype(jnp.float32)
    positions = jnp.arange(resp_rows, dtype=jnp.int32)
    live_rows = positions < length
    grad_rows = jnp.where(live_rows[:, None], grad_in, jnp.zeros_like(grad_in))
    grad_four = grad_rows.reshape(resp_rows, KV_HEADS, GROUP, HEAD_DIM).astype(jnp.float32)
    prefix_mask = jnp.broadcast_to((visible > 0)[:, None], (pre_rows // BLOCK, BLOCK)).reshape(pre_rows)
    causal = positions[:, None] >= positions[None, :]
    allowed = jnp.concatenate([jnp.broadcast_to(prefix_mask[None, :], (resp_rows, pre_rows)), causal], 1)
    scores = jnp.einsum('qgjd,kgd->gjqk', query_four, keys_three) * scale_factor
    scores = jnp.where(allowed[None, None], scores, neg_big)
    row_peak = jnp.max(scores, axis=-1, keepdims=True)
    raised = jnp.exp(scores - row_peak)
    weights = raised / jnp.sum(raised, axis=-1, keepdims=True)
    probs_low = lax.optimization_barrier(weights.astype(jnp.bfloat16)).astype(jnp.float32)
    attended = jnp.einsum('gjqk,kgd->qgjd', probs_low, values_three)
    attended = lax.optimization_barrier(attended.astype(jnp.bfloat16)).astype(jnp.float32)
    row_delta = jnp.transpose(jnp.sum(grad_four * attended, axis=-1), (1, 2, 0))
    d_probs = jnp.einsum('qgjd,kgd->gjqk', grad_four, values_three)
    d_scores = weights * (d_probs - row_delta[..., None])
    ds_low = lax.optimization_barrier(d_scores.astype(jnp.bfloat16)).astype(jnp.float32)
    query_grad = (jnp.einsum('gjqk,kgd->qgjd', ds_low, keys_three) * scale_factor).astype(jnp.bfloat16)
    key_grad = jnp.einsum('gjqk,qgjd->kgd', ds_low, query_four) * scale_factor
    value_grad = jnp.einsum('gjqk,qgjd->kgd', probs_low, grad_four)
    key_grad = key_grad.reshape(pre_rows + resp_rows, KV_HEADS * HEAD_DIM)
    value_grad = value_grad.reshape(pre_rows + resp_rows, KV_HEADS * HEAD_DIM)
    own_key_grad = key_grad[pre_rows:].astype(jnp.bfloat16)
    own_value_grad = value_grad[pre_rows:].astype(jnp.bfloat16)
    prefix_part = jnp.stack([key_grad[:pre_rows], value_grad[:pre_rows]], 1)
    prefix_part = lax.optimization_barrier(prefix_part.astype(jnp.bfloat16)).astype(jnp.float32)
    return query_grad.reshape(resp_rows, -1), own_key_grad, own_value_grad, prefix_part


def reference(queries, resp_keys, resp_values, d_out, prefix_kv, prefix_blocks, resp_lengths, pair_prompt):
    holders = N_CTX * N_PAIR
    holder_prompt = jnp.broadcast_to(pair_prompt[None, :], (N_CTX, N_PAIR)).reshape(holders).astype(jnp.int32)
    holder_pair = jnp.broadcast_to(jnp.arange(N_PAIR, dtype=jnp.int32)[None, :], (N_CTX, N_PAIR)).reshape(holders).astype(jnp.int32)
    scan_items = (queries.reshape(holders, RESP, Q_WIDTH), resp_keys.reshape(holders, RESP, KV_WIDTH),
                  resp_values.reshape(holders, RESP, KV_WIDTH), d_out.reshape(holders, RESP, Q_WIDTH),
                  prefix_blocks.reshape(holders, BLOCKS), resp_lengths.reshape(holders), holder_prompt, holder_pair)

    def per_holder(totals, items):
        query_rows, own_keys, own_values, grad_in, visible, length, prompt, slot = items
        prefix_panel = lax.dynamic_index_in_dim(prefix_kv, prompt, 0, keepdims=False)
        query_grad, own_key_grad, own_value_grad, prefix_part = response_grads(
            query_rows, own_keys, own_values, grad_in, prefix_panel[:, 0], prefix_panel[:, 1], visible, length)
        totals = totals.at[slot].add(prefix_part)
        return totals, (query_grad, own_key_grad, own_value_grad)

    zeros_start = jnp.zeros((N_PAIR, PRE, 2, KV_WIDTH), jnp.float32)
    ctx_total, outputs = lax.scan(per_holder, zeros_start, scan_items)
    ctx_total = lax.optimization_barrier(ctx_total.astype(jnp.bfloat16)).astype(jnp.float32)
    prompt_hits = (pair_prompt[:, None] == jnp.arange(PROMPTS, dtype=jnp.int32)[None, :]).astype(jnp.float32)
    d_prefix = jnp.sum(prompt_hits[:, :, None, None, None] * ctx_total[:, None], axis=0)
    query_grads, key_grads, value_grads = outputs
    return (query_grads.reshape(N_CTX, N_PAIR, RESP, Q_WIDTH),
            key_grads.reshape(N_CTX, N_PAIR, RESP, KV_WIDTH),
            value_grads.reshape(N_CTX, N_PAIR, RESP, KV_WIDTH),
            d_prefix)
```

```python
import functools

import jax
import jax.numpy as jnp
from jax import lax
from jax.experimental import pallas as pl
from jax.experimental.pallas import tpu as pltpu
from jax.sharding import PartitionSpec as P

KV_HEADS = 8
GROUP = 2
HEAD_DIM = 128
BLOCK = 128


scale_factor = 144.0 ** (-0.5)
neg_big = -1e30

NT = (((1,), (1,)), ((), ()))
TN = (((0,), (0,)), ((), ()))


def attention_grad_kernel(blocks_ref, length_ref, q_ref, do_ref, kp_ref, vp_ref, kr_ref, vr_ref,
                          dq_ref, dkr_ref, dvr_ref, dpre_ref):
    resp_rows = q_ref.shape[0]
    pre_rows = kp_ref.shape[0]
    n_blocks = pre_rows // BLOCK
    kp = kp_ref[...]
    vp = vp_ref[...]
    kr = kr_ref[...]
    vr = vr_ref[...]

    col_block = lax.broadcasted_iota(jnp.int32, (1, pre_rows), 1) // BLOCK
    flag = jnp.zeros((1, pre_rows), jnp.int32)
    for b in range(n_blocks):
        flag = jnp.where(col_block == b, blocks_ref[b], flag)
    pre_ok = flag > 0
    row_i = lax.broadcasted_iota(jnp.int32, (resp_rows, resp_rows), 0)
    col_i = lax.broadcasted_iota(jnp.int32, (resp_rows, resp_rows), 1)
    causal = row_i >= col_i
    live = lax.broadcasted_iota(jnp.int32, (resp_rows, 1), 0) < length_ref[0]

    dkp = jnp.zeros((pre_rows, HEAD_DIM), jnp.float32)
    dvp = jnp.zeros((pre_rows, HEAD_DIM), jnp.float32)
    dkr = jnp.zeros((resp_rows, HEAD_DIM), jnp.float32)
    dvr = jnp.zeros((resp_rows, HEAD_DIM), jnp.float32)
    for j in range(GROUP):
        cols = slice(j * HEAD_DIM, (j + 1) * HEAD_DIM)
        qj = q_ref[:, cols]
        doj = jnp.where(live, do_ref[:, cols], jnp.zeros_like(do_ref[:, cols]))
        sp = lax.dot_general(qj, kp, NT, preferred_element_type=jnp.float32) * scale_factor
        sr = lax.dot_general(qj, kr, NT, preferred_element_type=jnp.float32) * scale_factor
        sp = jnp.where(pre_ok, sp, neg_big)
        sr = jnp.where(causal, sr, neg_big)
        peak = jnp.maximum(jnp.max(sp, axis=-1, keepdims=True), jnp.max(sr, axis=-1, keepdims=True))
        ep = jnp.exp(sp - peak)
        er = jnp.exp(sr - peak)
        total = jnp.sum(ep, axis=-1, keepdims=True) + jnp.sum(er, axis=-1, keepdims=True)
        wp = ep / total
        wr = er / total
        pp = wp.astype(jnp.bfloat16)
        pr = wr.astype(jnp.bfloat16)
        att = jnp.dot(pp, vp, preferred_element_type=jnp.float32) + jnp.dot(
            pr, vr, preferred_element_type=jnp.float32)
        att = att.astype(jnp.bfloat16).astype(jnp.float32)
        delta = jnp.sum(doj.astype(jnp.float32) * att, axis=-1, keepdims=True)
        dpp = lax.dot_general(doj, vp, NT, preferred_element_type=jnp.float32)
        dpr = lax.dot_general(doj, vr, NT, preferred_element_type=jnp.float32)
        dsp = (wp * (dpp - delta)).astype(jnp.bfloat16)
        dsr = (wr * (dpr - delta)).astype(jnp.bfloat16)
        dq = (jnp.dot(dsp, kp, preferred_element_type=jnp.float32) + jnp.dot(
            dsr, kr, preferred_element_type=jnp.float32)) * scale_factor
        dq_ref[:, cols] = dq.astype(dq_ref.dtype)
        dkp = dkp + lax.dot_general(dsp, qj, TN, preferred_element_type=jnp.float32)
        dkr = dkr + lax.dot_general(dsr, qj, TN, preferred_element_type=jnp.float32)
        dvp = dvp + lax.dot_general(pp, doj, TN, preferred_element_type=jnp.float32)
        dvr = dvr + lax.dot_general(pr, doj, TN, preferred_element_type=jnp.float32)
    dkr_ref[...] = (dkr * scale_factor).astype(dkr_ref.dtype)
    dvr_ref[...] = dvr.astype(dvr_ref.dtype)
    dpre_ref[0] = (dkp * scale_factor).astype(dpre_ref.dtype)
    dpre_ref[1] = dvp.astype(dpre_ref.dtype)


def attention_grads(blocks, length, q, do, kp, vp, kr, vr):
    resp_rows, q_width = q.shape
    pre_rows, kv_width = kp.shape
    heads = kv_width // HEAD_DIM
    qspec = pl.BlockSpec((resp_rows, GROUP * HEAD_DIM), lambda g, b, n: (0, g))
    pspec = pl.BlockSpec((pre_rows, HEAD_DIM), lambda g, b, n: (0, g))
    rspec = pl.BlockSpec((resp_rows, HEAD_DIM), lambda g, b, n: (0, g))
    flops = 2 * 6 * resp_rows * GROUP * heads * (pre_rows + resp_rows) * HEAD_DIM
    return pl.pallas_call(
        attention_grad_kernel,
        out_shape=(
            jax.ShapeDtypeStruct((resp_rows, q_width), jnp.bfloat16),
            jax.ShapeDtypeStruct((resp_rows, kv_width), jnp.bfloat16),
            jax.ShapeDtypeStruct((resp_rows, kv_width), jnp.bfloat16),
            jax.ShapeDtypeStruct((2, pre_rows, kv_width), jnp.bfloat16),
        ),
        grid_spec=pltpu.PrefetchScalarGridSpec(
            num_scalar_prefetch=2,
            grid=(heads,),
            in_specs=[qspec, qspec, pspec, pspec, rspec, rspec],
            out_specs=[qspec, rspec, rspec,
                       pl.BlockSpec((2, pre_rows, HEAD_DIM), lambda g, b, n: (0, 0, g))],
        ),
        cost_estimate=pl.CostEstimate(
            flops=flops,
            transcendentals=resp_rows * GROUP * heads * (pre_rows + resp_rows),
            bytes_accessed=2 * (2 * resp_rows * q_width + 4 * pre_rows * kv_width + 4 * resp_rows * kv_width),
        ),
    )(blocks, length, q, do, kp, vp, kr, vr)


def shards(
    queries, resp_keys, resp_values, d_out, prefix_kv, prefix_blocks, resp_lengths, pair_prompt
):
    n_prompts = prefix_kv.shape[0]
    kv_planes = jnp.transpose(prefix_kv, (0, 2, 1, 3))
    outgoing = jnp.take(kv_planes, pair_prompt, axis=0)
    mine = lax.all_to_all(outgoing, "pair", split_axis=0, concat_axis=3, tiled=True)
    panel = lax.all_gather(mine, "ctx", axis=2, tiled=True)[0]
    kp = panel[0]
    vp = panel[1]
    pre_rows = kp.shape[0]

    dq, dkr, dvr, dpre = attention_grads(
        prefix_blocks[0, 0], resp_lengths[0, 0].reshape(1), queries[0, 0], d_out[0, 0],
        kp, vp, resp_keys[0, 0], resp_values[0, 0])
    d_queries = dq[None, None]
    d_resp_keys = dkr[None, None]
    d_resp_values = dvr[None, None]

    n_ctx = lax.axis_size("ctx")
    n_pair = lax.axis_size("pair")
    kv_width = dpre.shape[-1]
    pieces = dpre.reshape(2, n_ctx, pre_rows // n_ctx, kv_width)
    pieces = lax.all_to_all(pieces, "ctx", split_axis=1, concat_axis=1, tiled=True)
    ctx_total = jnp.sum(pieces.astype(jnp.float32), axis=1).astype(jnp.bfloat16)
    ctx_total = ctx_total.reshape(2, pre_rows // n_ctx, n_pair, kv_width // n_pair)
    arrived = lax.all_to_all(ctx_total, "pair", split_axis=2, concat_axis=2, tiled=True)
    prompt_hits = (pair_prompt[:, None] == jnp.arange(n_prompts, dtype=jnp.int32)[None, :]).astype(
        jnp.float32
    )
    arrived = jnp.transpose(arrived.astype(jnp.float32), (2, 1, 0, 3))
    d_prefix = jnp.sum(prompt_hits[:, :, None, None, None] * arrived[:, None], axis=0)
    return (d_queries, d_resp_keys, d_resp_values, d_prefix)


def solution(mesh):
    placed = (
        P(("dp", "ctx"), "pair", None, None),
        P(("dp", "ctx"), "pair", None, None),
        P(("dp", "ctx"), "pair", None, None),
        P(("dp", "ctx"), "pair", None, None),
        P("dp", "ctx", None, "pair"),
        P(("dp", "ctx"), "pair", None),
        P(("dp", "ctx"), "pair"),
        P("dp"),
    )
    return jax.shard_map(
        shards,
        mesh=mesh,
        in_specs=placed,
        out_specs=(
            P(("dp", "ctx"), "pair", None, None),
            P(("dp", "ctx"), "pair", None, None),
            P(("dp", "ctx"), "pair", None, None),
            P("dp", "ctx", None, "pair"),
        ),
        check_vma=False,
    )
```

```python
import functools

import jax
import jax.numpy as jnp
from jax import lax
from jax.experimental import pallas as pl
from jax.experimental.pallas import tpu as pltpu
from jax.sharding import PartitionSpec as P

KV_HEADS = 8
GROUP = 2
HEAD_DIM = 128
BLOCK = 128


scale_factor = 144.0 ** (-0.5)
neg_big = -1e30

NT = (((1,), (1,)), ((), ()))
TN = (((0,), (0,)), ((), ()))


def attention_grad_kernel(blocks_ref, length_ref, q_ref, do_ref, kp_ref, vp_ref, kr_ref, vr_ref,
                          dq_ref, dkr_ref, dvr_ref, dpre_ref):
    resp_rows = q_ref.shape[0]
    n_ctx, chunk_rows, _ = kp_ref.shape
    pre_rows = n_ctx * chunk_rows
    n_blocks = pre_rows // BLOCK
    kp = kp_ref[...].reshape(pre_rows, HEAD_DIM)
    vp = vp_ref[...].reshape(pre_rows, HEAD_DIM)
    kr = kr_ref[...]
    vr = vr_ref[...]

    col_block = lax.broadcasted_iota(jnp.int32, (1, pre_rows), 1) // BLOCK
    flag = jnp.zeros((1, pre_rows), jnp.int32)
    for b in range(n_blocks):
        flag = jnp.where(col_block == b, blocks_ref[b], flag)
    pre_ok = flag > 0
    row_i = lax.broadcasted_iota(jnp.int32, (resp_rows, resp_rows), 0)
    col_i = lax.broadcasted_iota(jnp.int32, (resp_rows, resp_rows), 1)
    causal = row_i >= col_i
    live = lax.broadcasted_iota(jnp.int32, (resp_rows, 1), 0) < length_ref[0]

    dkp = jnp.zeros((pre_rows, HEAD_DIM), jnp.float32)
    dvp = jnp.zeros((pre_rows, HEAD_DIM), jnp.float32)
    dkr = jnp.zeros((resp_rows, HEAD_DIM), jnp.float32)
    dvr = jnp.zeros((resp_rows, HEAD_DIM), jnp.float32)
    for j in range(GROUP):
        cols = slice(j * HEAD_DIM, (j + 1) * HEAD_DIM)
        qj = q_ref[:, cols]
        doj = jnp.where(live, do_ref[:, cols], jnp.zeros_like(do_ref[:, cols]))
        sp = lax.dot_general(qj, kp, NT, preferred_element_type=jnp.float32) * scale_factor
        sr = lax.dot_general(qj, kr, NT, preferred_element_type=jnp.float32) * scale_factor
        sp = jnp.where(pre_ok, sp, neg_big)
        sr = jnp.where(causal, sr, neg_big)
        peak = jnp.maximum(jnp.max(sp, axis=-1, keepdims=True), jnp.max(sr, axis=-1, keepdims=True))
        ep = jnp.exp(sp - peak)
        er = jnp.exp(sr - peak)
        total = jnp.sum(ep, axis=-1, keepdims=True) + jnp.sum(er, axis=-1, keepdims=True)
        wp = ep / total
        wr = er / total
        pp = wp.astype(jnp.bfloat16)
        pr = wr.astype(jnp.bfloat16)
        att = jnp.dot(pp, vp, preferred_element_type=jnp.float32) + jnp.dot(
            pr, vr, preferred_element_type=jnp.float32)
        att = att.astype(jnp.bfloat16).astype(jnp.float32)
        delta = jnp.sum(doj.astype(jnp.float32) * att, axis=-1, keepdims=True)
        dpp = lax.dot_general(doj, vp, NT, preferred_element_type=jnp.float32)
        dpr = lax.dot_general(doj, vr, NT, preferred_element_type=jnp.float32)
        dsp = (wp * (dpp - delta)).astype(jnp.bfloat16)
        dsr = (wr * (dpr - delta)).astype(jnp.bfloat16)
        dq = (jnp.dot(dsp, kp, preferred_element_type=jnp.float32) + jnp.dot(
            dsr, kr, preferred_element_type=jnp.float32)) * scale_factor
        dq_ref[:, cols] = dq.astype(dq_ref.dtype)
        dkp = dkp + lax.dot_general(dsp, qj, TN, preferred_element_type=jnp.float32)
        dkr = dkr + lax.dot_general(dsr, qj, TN, preferred_element_type=jnp.float32)
        dvp = dvp + lax.dot_general(pp, doj, TN, preferred_element_type=jnp.float32)
        dvr = dvr + lax.dot_general(pr, doj, TN, preferred_element_type=jnp.float32)
    dkr_ref[...] = (dkr * scale_factor).astype(dkr_ref.dtype)
    dvr_ref[...] = dvr.astype(dvr_ref.dtype)
    dpre_ref[:, 0] = (dkp * scale_factor).astype(dpre_ref.dtype).reshape(n_ctx, chunk_rows, HEAD_DIM)
    dpre_ref[:, 1] = dvp.astype(dpre_ref.dtype).reshape(n_ctx, chunk_rows, HEAD_DIM)


def attention_grads(blocks, length, q, do, panel, kr, vr):
    resp_rows, q_width = q.shape
    n_ctx, n_pair, _, chunk_rows, chunk_feats = panel.shape
    kv_width = kr.shape[1]
    pre_rows = n_ctx * chunk_rows
    heads = kv_width // HEAD_DIM
    per_chunk = chunk_feats // HEAD_DIM
    qspec = pl.BlockSpec((resp_rows, GROUP * HEAD_DIM), lambda g, b, n: (0, g))
    kspec = pl.BlockSpec((n_ctx, None, None, chunk_rows, HEAD_DIM),
                         lambda g, b, n: (0, g // per_chunk, 0, 0, g % per_chunk))
    vspec = pl.BlockSpec((n_ctx, None, None, chunk_rows, HEAD_DIM),
                         lambda g, b, n: (0, g // per_chunk, 1, 0, g % per_chunk))
    rspec = pl.BlockSpec((resp_rows, HEAD_DIM), lambda g, b, n: (0, g))
    dspec = pl.BlockSpec((n_ctx, None, 2, chunk_rows, HEAD_DIM),
                         lambda g, b, n: (0, g // per_chunk, 0, 0, g % per_chunk))
    flops = 2 * 6 * resp_rows * GROUP * heads * (pre_rows + resp_rows) * HEAD_DIM
    return pl.pallas_call(
        attention_grad_kernel,
        out_shape=(
            jax.ShapeDtypeStruct((resp_rows, q_width), jnp.bfloat16),
            jax.ShapeDtypeStruct((resp_rows, kv_width), jnp.bfloat16),
            jax.ShapeDtypeStruct((resp_rows, kv_width), jnp.bfloat16),
            jax.ShapeDtypeStruct(panel.shape, jnp.bfloat16),
        ),
        grid_spec=pltpu.PrefetchScalarGridSpec(
            num_scalar_prefetch=2,
            grid=(heads,),
            in_specs=[qspec, qspec, kspec, vspec, rspec, rspec],
            out_specs=[qspec, rspec, rspec, dspec],
        ),
        cost_estimate=pl.CostEstimate(
            flops=flops,
            transcendentals=resp_rows * GROUP * heads * (pre_rows + resp_rows),
            bytes_accessed=2 * (2 * resp_rows * q_width + 4 * pre_rows * kv_width + 4 * resp_rows * kv_width),
        ),
    )(blocks, length, q, do, panel, panel, kr, vr)


def ring_shift(x, axis, n, d):
    return lax.ppermute(x, axis, [(i, (i + d) % n) for i in range(n)])


def pair_gather(planes, pair_prompt):
    n = lax.axis_size("pair")
    r = lax.axis_index("pair")
    held = [lax.dynamic_index_in_dim(planes, pair_prompt[r], 0, keepdims=False)]
    for d in range(1, n):
        chunk = lax.dynamic_index_in_dim(planes, pair_prompt[(r + d) % n], 0, keepdims=False)
        held.append(ring_shift(chunk, "pair", n, d))
    held = jnp.stack(held)
    return jnp.take(held, (r - jnp.arange(n)) % n, axis=0)


def ctx_gather(x):
    n = lax.axis_size("ctx")
    if n != 4:
        return lax.all_gather(x, "ctx", axis=0, tiled=False)
    c = lax.axis_index("ctx")
    along_x = [(i, i ^ 1) for i in range(n)]
    along_y = [(i, i ^ 2) for i in range(n)]
    from_x = lax.ppermute(x, "ctx", along_x)
    from_y = lax.ppermute(x, "ctx", along_y)
    half = x.shape[-2] // 2
    far_a = lax.ppermute(from_y[..., :half, :], "ctx", along_x)
    far_b = lax.ppermute(from_x[..., half:, :], "ctx", along_y)
    held = jnp.stack([x, from_x, from_y, jnp.concatenate([far_a, far_b], -2)])
    return jnp.take(held, jnp.bitwise_xor(jnp.arange(n), c), axis=0)


def ctx_reduce(pieces):
    n = lax.axis_size("ctx")
    if n != 4:
        got = lax.all_to_all(pieces, "ctx", split_axis=0, concat_axis=0, tiled=True)
        return jnp.sum(got.astype(jnp.float32), axis=0).astype(jnp.bfloat16)
    c = lax.axis_index("ctx")
    along_x = [(i, i ^ 1) for i in range(n)]
    along_y = [(i, i ^ 2) for i in range(n)]
    mine = lax.dynamic_index_in_dim(pieces, c, 0, keepdims=False)
    to_x = lax.dynamic_index_in_dim(pieces, jnp.bitwise_xor(c, 1), 0, keepdims=False)
    to_y = lax.dynamic_index_in_dim(pieces, jnp.bitwise_xor(c, 2), 0, keepdims=False)
    to_far = lax.dynamic_index_in_dim(pieces, jnp.bitwise_xor(c, 3), 0, keepdims=False)
    half = to_far.shape[-2] // 2
    own_x, pass_y = lax.ppermute((to_x, to_far[..., :half, :]), "ctx", along_x)
    own_y, pass_x = lax.ppermute((to_y, to_far[..., half:, :]), "ctx", along_y)
    far_a = lax.ppermute(pass_y, "ctx", along_y)
    far_b = lax.ppermute(pass_x, "ctx", along_x)
    far = jnp.concatenate([far_a, far_b], -2)
    total = (mine.astype(jnp.float32) + own_x.astype(jnp.float32)) + (
        own_y.astype(jnp.float32) + far.astype(jnp.float32))
    return total.astype(jnp.bfloat16)


def pair_reduce(totals, pair_prompt, n_prompts):
    n = lax.axis_size("pair")
    r = lax.axis_index("pair")
    out = None
    for d in range(n):
        chunk = lax.dynamic_index_in_dim(totals, (r + d) % n, 0, keepdims=False)
        got = chunk if d == 0 else ring_shift(chunk, "pair", n, d)
        source = (r - d) % n
        hits = (pair_prompt[source] == jnp.arange(n_prompts, dtype=jnp.int32)).astype(jnp.float32)
        term = hits[:, None, None, None] * jnp.transpose(got.astype(jnp.float32), (1, 0, 2))[None]
        out = term if out is None else out + term
    return out


def shards(
    queries, resp_keys, resp_values, d_out, prefix_kv, prefix_blocks, resp_lengths, pair_prompt
):
    n_prompts = prefix_kv.shape[0]
    planes = jnp.transpose(prefix_kv, (0, 2, 1, 3))
    panel = ctx_gather(pair_gather(planes, pair_prompt))

    dq, dkr, dvr, dpre = attention_grads(
        prefix_blocks[0, 0], resp_lengths[0, 0].reshape(1), queries[0, 0], d_out[0, 0],
        panel, resp_keys[0, 0], resp_values[0, 0])
    d_queries = dq[None, None]
    d_resp_keys = dkr[None, None]
    d_resp_values = dvr[None, None]

    ctx_total = ctx_reduce(dpre)
    d_prefix = pair_reduce(ctx_total, pair_prompt, n_prompts)
    return (d_queries, d_resp_keys, d_resp_values, d_prefix)


def solution(mesh):
    placed = (
        P(("dp", "ctx"), "pair", None, None),
        P(("dp", "ctx"), "pair", None, None),
        P(("dp", "ctx"), "pair", None, None),
        P(("dp", "ctx"), "pair", None, None),
        P("dp", "ctx", None, "pair"),
        P(("dp", "ctx"), "pair", None),
        P(("dp", "ctx"), "pair"),
        P("dp"),
    )
    return jax.shard_map(
        shards,
        mesh=mesh,
        in_specs=placed,
        out_specs=(
            P(("dp", "ctx"), "pair", None, None),
            P(("dp", "ctx"), "pair", None, None),
            P(("dp", "ctx"), "pair", None, None),
            P("dp", "ctx", None, "pair"),
        ),
        check_vma=False,
    )
```

```python
import functools

import jax
import jax.numpy as jnp
from jax import lax
from jax.experimental import pallas as pl
from jax.experimental.pallas import tpu as pltpu
from jax.sharding import PartitionSpec as P

KV_HEADS = 8
GROUP = 2
HEAD_DIM = 128
BLOCK = 128


scale_factor = 144.0 ** (-0.5)
neg_big = -1e30

NT = (((1,), (1,)), ((), ()))
TN = (((0,), (0,)), ((), ()))


def attention_grad_kernel(blocks_ref, length_ref, pair_ref, q_ref, do_ref, kp_ref, vp_ref, kr_ref, vr_ref,
                          dq_ref, dkr_ref, dvr_ref, dpre_ref):
    resp_rows = q_ref.shape[0]
    n_ctx, chunk_rows, _ = kp_ref.shape
    pre_rows = n_ctx * chunk_rows
    n_blocks = pre_rows // BLOCK
    kp = kp_ref[...].reshape(pre_rows, HEAD_DIM)
    vp = vp_ref[...].reshape(pre_rows, HEAD_DIM)
    kr = kr_ref[...]
    vr = vr_ref[...]

    col_block = lax.broadcasted_iota(jnp.int32, (1, pre_rows), 1) // BLOCK
    flag = jnp.zeros((1, pre_rows), jnp.int32)
    for b in range(n_blocks):
        flag = jnp.where(col_block == b, blocks_ref[b], flag)
    pre_ok = flag > 0
    row_i = lax.broadcasted_iota(jnp.int32, (resp_rows, resp_rows), 0)
    col_i = lax.broadcasted_iota(jnp.int32, (resp_rows, resp_rows), 1)
    causal = row_i >= col_i
    live = lax.broadcasted_iota(jnp.int32, (resp_rows, 1), 0) < length_ref[0]

    dkp = jnp.zeros((pre_rows, HEAD_DIM), jnp.float32)
    dvp = jnp.zeros((pre_rows, HEAD_DIM), jnp.float32)
    dkr = jnp.zeros((resp_rows, HEAD_DIM), jnp.float32)
    dvr = jnp.zeros((resp_rows, HEAD_DIM), jnp.float32)
    for j in range(GROUP):
        cols = slice(j * HEAD_DIM, (j + 1) * HEAD_DIM)
        qj = q_ref[:, cols]
        doj = jnp.where(live, do_ref[:, cols], jnp.zeros_like(do_ref[:, cols]))
        sp = lax.dot_general(qj, kp, NT, preferred_element_type=jnp.float32) * scale_factor
        sr = lax.dot_general(qj, kr, NT, preferred_element_type=jnp.float32) * scale_factor
        sp = jnp.where(pre_ok, sp, neg_big)
        sr = jnp.where(causal, sr, neg_big)
        peak = jnp.maximum(jnp.max(sp, axis=-1, keepdims=True), jnp.max(sr, axis=-1, keepdims=True))
        ep = jnp.exp(sp - peak)
        er = jnp.exp(sr - peak)
        total = jnp.sum(ep, axis=-1, keepdims=True) + jnp.sum(er, axis=-1, keepdims=True)
        wp = ep / total
        wr = er / total
        pp = wp.astype(jnp.bfloat16)
        pr = wr.astype(jnp.bfloat16)
        att = jnp.dot(pp, vp, preferred_element_type=jnp.float32) + jnp.dot(
            pr, vr, preferred_element_type=jnp.float32)
        att = att.astype(jnp.bfloat16).astype(jnp.float32)
        delta = jnp.sum(doj.astype(jnp.float32) * att, axis=-1, keepdims=True)
        dpp = lax.dot_general(doj, vp, NT, preferred_element_type=jnp.float32)
        dpr = lax.dot_general(doj, vr, NT, preferred_element_type=jnp.float32)
        dsp = (wp * (dpp - delta)).astype(jnp.bfloat16)
        dsr = (wr * (dpr - delta)).astype(jnp.bfloat16)
        dq = (jnp.dot(dsp, kp, preferred_element_type=jnp.float32) + jnp.dot(
            dsr, kr, preferred_element_type=jnp.float32)) * scale_factor
        dq_ref[:, cols] = dq.astype(dq_ref.dtype)
        dkp = dkp + lax.dot_general(dsp, qj, TN, preferred_element_type=jnp.float32)
        dkr = dkr + lax.dot_general(dsr, qj, TN, preferred_element_type=jnp.float32)
        dvp = dvp + lax.dot_general(pp, doj, TN, preferred_element_type=jnp.float32)
        dvr = dvr + lax.dot_general(pr, doj, TN, preferred_element_type=jnp.float32)
    dkr_ref[...] = (dkr * scale_factor).astype(dkr_ref.dtype)
    dvr_ref[...] = dvr.astype(dvr_ref.dtype)
    dpre_ref[:, 0] = (dkp * scale_factor).astype(dpre_ref.dtype).reshape(n_ctx, chunk_rows, HEAD_DIM)
    dpre_ref[:, 1] = dvp.astype(dpre_ref.dtype).reshape(n_ctx, chunk_rows, HEAD_DIM)


def attention_grads(blocks, length, pair_index, q, do, panel, kr, vr):
    resp_rows, q_width = q.shape
    n_ctx, n_pair, _, chunk_rows, chunk_feats = panel.shape
    kv_width = kr.shape[1]
    pre_rows = n_ctx * chunk_rows
    heads = kv_width // HEAD_DIM
    per_chunk = chunk_feats // HEAD_DIM

    def head(g, r):
        return ((r[0] + n_pair - g // per_chunk) % n_pair) * per_chunk + g % per_chunk

    qspec = pl.BlockSpec((resp_rows, GROUP * HEAD_DIM), lambda g, b, n, r: (0, head(g, r)))
    kspec = pl.BlockSpec((n_ctx, None, None, chunk_rows, HEAD_DIM),
                         lambda g, b, n, r: (0, g // per_chunk, 0, 0, g % per_chunk))
    vspec = pl.BlockSpec((n_ctx, None, None, chunk_rows, HEAD_DIM),
                         lambda g, b, n, r: (0, g // per_chunk, 1, 0, g % per_chunk))
    rspec = pl.BlockSpec((resp_rows, HEAD_DIM), lambda g, b, n, r: (0, head(g, r)))
    dspec = pl.BlockSpec((n_ctx, None, 2, chunk_rows, HEAD_DIM),
                         lambda g, b, n, r: (0, g // per_chunk, 0, 0, g % per_chunk))
    flops = 2 * 6 * resp_rows * GROUP * heads * (pre_rows + resp_rows) * HEAD_DIM
    return pl.pallas_call(
        attention_grad_kernel,
        out_shape=(
            jax.ShapeDtypeStruct((resp_rows, q_width), jnp.bfloat16),
            jax.ShapeDtypeStruct((resp_rows, kv_width), jnp.bfloat16),
            jax.ShapeDtypeStruct((resp_rows, kv_width), jnp.bfloat16),
            jax.ShapeDtypeStruct(panel.shape, jnp.bfloat16),
        ),
        grid_spec=pltpu.PrefetchScalarGridSpec(
            num_scalar_prefetch=3,
            grid=(heads,),
            in_specs=[qspec, qspec, kspec, vspec, rspec, rspec],
            out_specs=[qspec, rspec, rspec, dspec],
        ),
        cost_estimate=pl.CostEstimate(
            flops=flops,
            transcendentals=resp_rows * GROUP * heads * (pre_rows + resp_rows),
            bytes_accessed=2 * (2 * resp_rows * q_width + 4 * pre_rows * kv_width + 4 * resp_rows * kv_width),
        ),
    )(blocks, length, pair_index, q, do, panel, panel, kr, vr)


def ring_shift(x, axis, n, d):
    return lax.ppermute(x, axis, [(i, (i + d) % n) for i in range(n)])


def pair_gather(planes, pair_prompt):
    n = lax.axis_size("pair")
    r = lax.axis_index("pair")
    held = [lax.dynamic_index_in_dim(planes, pair_prompt[r], 0, keepdims=False)]
    for d in range(1, n):
        chunk = lax.dynamic_index_in_dim(planes, pair_prompt[(r + d) % n], 0, keepdims=False)
        held.append(ring_shift(chunk, "pair", n, d))
    return jnp.stack(held)


def ctx_gather(x):
    n = lax.axis_size("ctx")
    if n != 4:
        return lax.all_gather(x, "ctx", axis=0, tiled=False), jnp.arange(n, dtype=jnp.int32)
    c = lax.axis_index("ctx")
    along_x = [(i, i ^ 1) for i in range(n)]
    along_y = [(i, i ^ 2) for i in range(n)]
    from_x = lax.ppermute(x, "ctx", along_x)
    from_y = lax.ppermute(x, "ctx", along_y)
    half = x.shape[-2] // 2
    far_a = lax.ppermute(from_y[..., :half, :], "ctx", along_x)
    far_b = lax.ppermute(from_x[..., half:, :], "ctx", along_y)
    held = jnp.stack([x, from_x, from_y, jnp.concatenate([far_a, far_b], -2)])
    return held, jnp.bitwise_xor(jnp.arange(n, dtype=jnp.int32), c)


def ctx_reduce(pieces):
    n = lax.axis_size("ctx")
    if n != 4:
        got = lax.all_to_all(pieces, "ctx", split_axis=0, concat_axis=0, tiled=True)
        return jnp.sum(got.astype(jnp.float32), axis=0).astype(jnp.bfloat16)
    along_x = [(i, i ^ 1) for i in range(n)]
    along_y = [(i, i ^ 2) for i in range(n)]
    mine, to_x, to_y, to_far = pieces[0], pieces[1], pieces[2], pieces[3]
    half = to_far.shape[-2] // 2
    own_x, pass_y = lax.ppermute((to_x, to_far[..., :half, :]), "ctx", along_x)
    own_y, pass_x = lax.ppermute((to_y, to_far[..., half:, :]), "ctx", along_y)
    far_a = lax.ppermute(pass_y, "ctx", along_y)
    far_b = lax.ppermute(pass_x, "ctx", along_x)
    far = jnp.concatenate([far_a, far_b], -2)
    total = (mine.astype(jnp.float32) + own_x.astype(jnp.float32)) + (
        own_y.astype(jnp.float32) + far.astype(jnp.float32))
    return total.astype(jnp.bfloat16)


def pair_reduce(totals, pair_prompt, n_prompts):
    n = lax.axis_size("pair")
    r = lax.axis_index("pair")
    out = None
    for d in range(n):
        chunk = totals[(n - d) % n]
        got = chunk if d == 0 else ring_shift(chunk, "pair", n, d)
        source = (r - d) % n
        hits = (pair_prompt[source] == jnp.arange(n_prompts, dtype=jnp.int32)).astype(jnp.float32)
        term = hits[:, None, None, None] * jnp.transpose(got.astype(jnp.float32), (1, 0, 2))[None]
        out = term if out is None else out + term
    return out


def shards(
    queries, resp_keys, resp_values, d_out, prefix_kv, prefix_blocks, resp_lengths, pair_prompt
):
    n_prompts = prefix_kv.shape[0]
    planes = jnp.transpose(prefix_kv, (0, 2, 1, 3))
    panel, sources = ctx_gather(pair_gather(planes, pair_prompt))
    chunk_blocks = panel.shape[3] // BLOCK
    flags = prefix_blocks[0, 0].reshape(-1, chunk_blocks)[sources].reshape(-1)

    dq, dkr, dvr, dpre = attention_grads(
        flags, resp_lengths[0, 0].reshape(1), lax.axis_index("pair").reshape(1).astype(jnp.int32),
        queries[0, 0], d_out[0, 0], panel, resp_keys[0, 0], resp_values[0, 0])
    d_queries = dq[None, None]
    d_resp_keys = dkr[None, None]
    d_resp_values = dvr[None, None]

    ctx_total = ctx_reduce(dpre)
    d_prefix = pair_reduce(ctx_total, pair_prompt, n_prompts)
    return (d_queries, d_resp_keys, d_resp_values, d_prefix)


def solution(mesh):
    placed = (
        P(("dp", "ctx"), "pair", None, None),
        P(("dp", "ctx"), "pair", None, None),
        P(("dp", "ctx"), "pair", None, None),
        P(("dp", "ctx"), "pair", None, None),
        P("dp", "ctx", None, "pair"),
        P(("dp", "ctx"), "pair", None),
        P(("dp", "ctx"), "pair"),
        P("dp"),
    )
    return jax.shard_map(
        shards,
        mesh=mesh,
        in_specs=placed,
        out_specs=(
            P(("dp", "ctx"), "pair", None, None),
            P(("dp", "ctx"), "pair", None, None),
            P(("dp", "ctx"), "pair", None, None),
            P("dp", "ctx", None, "pair"),
        ),
        check_vma=False,
    )
```

```python
import functools

import jax
import jax.numpy as jnp
from jax import lax
from jax.experimental import pallas as pl
from jax.experimental.pallas import tpu as pltpu
from jax.sharding import PartitionSpec as P

KV_HEADS = 8
GROUP = 2
HEAD_DIM = 128
BLOCK = 128
HEAD_GROUPS = 2


scale_factor = 144.0 ** (-0.5)
neg_big = -1e30

NT = (((1,), (1,)), ((), ()))
TN = (((0,), (0,)), ((), ()))


def attention_grad_kernel(aliased, blocks_ref, length_ref, pair_ref, q_ref, do_ref, kp_ref, vp_ref, kr_ref, vr_ref,
                          *refs):
    dq_ref, dkr_ref, dvr_ref, dpre_ref = refs[3:] if aliased else refs
    resp_rows = q_ref.shape[0]
    n_ctx, chunk_rows, _ = kp_ref.shape
    pre_rows = n_ctx * chunk_rows
    n_blocks = pre_rows // BLOCK
    kp = kp_ref[...].reshape(pre_rows, HEAD_DIM)
    vp = vp_ref[...].reshape(pre_rows, HEAD_DIM)
    kr = kr_ref[...]
    vr = vr_ref[...]

    col_block = lax.broadcasted_iota(jnp.int32, (1, pre_rows), 1) // BLOCK
    flag = jnp.zeros((1, pre_rows), jnp.int32)
    for b in range(n_blocks):
        flag = jnp.where(col_block == b, blocks_ref[b], flag)
    pre_ok = flag > 0
    row_i = lax.broadcasted_iota(jnp.int32, (resp_rows, resp_rows), 0)
    col_i = lax.broadcasted_iota(jnp.int32, (resp_rows, resp_rows), 1)
    causal = row_i >= col_i
    live = lax.broadcasted_iota(jnp.int32, (resp_rows, 1), 0) < length_ref[0]

    dkp = jnp.zeros((pre_rows, HEAD_DIM), jnp.float32)
    dvp = jnp.zeros((pre_rows, HEAD_DIM), jnp.float32)
    dkr = jnp.zeros((resp_rows, HEAD_DIM), jnp.float32)
    dvr = jnp.zeros((resp_rows, HEAD_DIM), jnp.float32)
    for j in range(GROUP):
        cols = slice(j * HEAD_DIM, (j + 1) * HEAD_DIM)
        qj = q_ref[:, cols]
        doj = jnp.where(live, do_ref[:, cols], jnp.zeros_like(do_ref[:, cols]))
        sp = lax.dot_general(qj, kp, NT, preferred_element_type=jnp.float32) * scale_factor
        sr = lax.dot_general(qj, kr, NT, preferred_element_type=jnp.float32) * scale_factor
        sp = jnp.where(pre_ok, sp, neg_big)
        sr = jnp.where(causal, sr, neg_big)
        peak = jnp.maximum(jnp.max(sp, axis=-1, keepdims=True), jnp.max(sr, axis=-1, keepdims=True))
        ep = jnp.exp(sp - peak)
        er = jnp.exp(sr - peak)
        total = jnp.sum(ep, axis=-1, keepdims=True) + jnp.sum(er, axis=-1, keepdims=True)
        wp = ep / total
        wr = er / total
        pp = wp.astype(jnp.bfloat16)
        pr = wr.astype(jnp.bfloat16)
        att = jnp.dot(pp, vp, preferred_element_type=jnp.float32) + jnp.dot(
            pr, vr, preferred_element_type=jnp.float32)
        att = att.astype(jnp.bfloat16).astype(jnp.float32)
        delta = jnp.sum(doj.astype(jnp.float32) * att, axis=-1, keepdims=True)
        dpp = lax.dot_general(doj, vp, NT, preferred_element_type=jnp.float32)
        dpr = lax.dot_general(doj, vr, NT, preferred_element_type=jnp.float32)
        dsp = (wp * (dpp - delta)).astype(jnp.bfloat16)
        dsr = (wr * (dpr - delta)).astype(jnp.bfloat16)
        dq = (jnp.dot(dsp, kp, preferred_element_type=jnp.float32) + jnp.dot(
            dsr, kr, preferred_element_type=jnp.float32)) * scale_factor
        dq_ref[:, cols] = dq.astype(dq_ref.dtype)
        dkp = dkp + lax.dot_general(dsp, qj, TN, preferred_element_type=jnp.float32)
        dkr = dkr + lax.dot_general(dsr, qj, TN, preferred_element_type=jnp.float32)
        dvp = dvp + lax.dot_general(pp, doj, TN, preferred_element_type=jnp.float32)
        dvr = dvr + lax.dot_general(pr, doj, TN, preferred_element_type=jnp.float32)
    dkr_ref[...] = (dkr * scale_factor).astype(dkr_ref.dtype)
    dvr_ref[...] = dvr.astype(dvr_ref.dtype)
    dpre_ref[:, 0] = (dkp * scale_factor).astype(dpre_ref.dtype).reshape(n_ctx, chunk_rows, HEAD_DIM)
    dpre_ref[:, 1] = dvp.astype(dpre_ref.dtype).reshape(n_ctx, chunk_rows, HEAD_DIM)


def attention_grads(blocks, length, pair_index, q, do, panel, kr, vr, first_head, earlier):
    resp_rows, q_width = q.shape
    n_ctx, n_pair, _, chunk_rows, chunk_feats = panel.shape
    kv_width = kr.shape[1]
    pre_rows = n_ctx * chunk_rows
    chunk_heads = kv_width // n_pair // HEAD_DIM
    per_chunk = chunk_feats // HEAD_DIM
    heads = n_pair * per_chunk

    def head(g, r):
        return ((r[0] + n_pair - g // per_chunk) % n_pair) * chunk_heads + first_head + g % per_chunk

    qspec = pl.BlockSpec((resp_rows, GROUP * HEAD_DIM), lambda g, b, n, r: (0, head(g, r)))
    kspec = pl.BlockSpec((n_ctx, None, None, chunk_rows, HEAD_DIM),
                         lambda g, b, n, r: (0, g // per_chunk, 0, 0, g % per_chunk))
    vspec = pl.BlockSpec((n_ctx, None, None, chunk_rows, HEAD_DIM),
                         lambda g, b, n, r: (0, g // per_chunk, 1, 0, g % per_chunk))
    rspec = pl.BlockSpec((resp_rows, HEAD_DIM), lambda g, b, n, r: (0, head(g, r)))
    dspec = pl.BlockSpec((n_ctx, None, 2, chunk_rows, HEAD_DIM),
                         lambda g, b, n, r: (0, g // per_chunk, 0, 0, g % per_chunk))
    flops = 2 * 6 * resp_rows * GROUP * heads * (pre_rows + resp_rows) * HEAD_DIM
    in_specs = [qspec, qspec, kspec, vspec, rspec, rspec]
    operands = [blocks, length, pair_index, q, do, panel, panel, kr, vr]
    aliases = {}
    if earlier is not None:
        in_specs += [pl.BlockSpec(memory_space=pl.ANY)] * 3
        aliases = {len(operands) + i: i for i in range(3)}
        operands += list(earlier)
    return pl.pallas_call(
        functools.partial(attention_grad_kernel, earlier is not None),
        out_shape=(
            jax.ShapeDtypeStruct((resp_rows, q_width), jnp.bfloat16),
            jax.ShapeDtypeStruct((resp_rows, kv_width), jnp.bfloat16),
            jax.ShapeDtypeStruct((resp_rows, kv_width), jnp.bfloat16),
            jax.ShapeDtypeStruct(panel.shape, jnp.bfloat16),
        ),
        grid_spec=pltpu.PrefetchScalarGridSpec(
            num_scalar_prefetch=3,
            grid=(heads,),
            in_specs=in_specs,
            out_specs=[qspec, rspec, rspec, dspec],
        ),
        input_output_aliases=aliases,
        cost_estimate=pl.CostEstimate(
            flops=flops,
            transcendentals=resp_rows * GROUP * heads * (pre_rows + resp_rows),
            bytes_accessed=2 * heads * HEAD_DIM * (4 * resp_rows * GROUP + 4 * pre_rows + 4 * resp_rows),
        ),
    )(*operands)


def ring_shift(x, axis, n, d):
    return lax.ppermute(x, axis, [(i, (i + d) % n) for i in range(n)])


def pair_gather(planes, pair_prompt):
    n = lax.axis_size("pair")
    r = lax.axis_index("pair")
    held = [lax.dynamic_index_in_dim(planes, pair_prompt[r], 0, keepdims=False)]
    for d in range(1, n):
        chunk = lax.dynamic_index_in_dim(planes, pair_prompt[(r + d) % n], 0, keepdims=False)
        held.append(ring_shift(chunk, "pair", n, d))
    return jnp.stack(held)


def ctx_gather(x):
    n = lax.axis_size("ctx")
    if n != 4:
        return lax.all_gather(x, "ctx", axis=0, tiled=False), jnp.arange(n, dtype=jnp.int32)
    c = lax.axis_index("ctx")
    along_x = [(i, i ^ 1) for i in range(n)]
    along_y = [(i, i ^ 2) for i in range(n)]
    from_x = lax.ppermute(x, "ctx", along_x)
    from_y = lax.ppermute(x, "ctx", along_y)
    half = x.shape[-2] // 2
    far_a = lax.ppermute(from_y[..., :half, :], "ctx", along_x)
    far_b = lax.ppermute(from_x[..., half:, :], "ctx", along_y)
    held = jnp.stack([x, from_x, from_y, jnp.concatenate([far_a, far_b], -2)])
    return held, jnp.bitwise_xor(jnp.arange(n, dtype=jnp.int32), c)


def ctx_reduce(pieces):
    n = lax.axis_size("ctx")
    if n != 4:
        got = lax.all_to_all(pieces, "ctx", split_axis=0, concat_axis=0, tiled=True)
        return jnp.sum(got.astype(jnp.float32), axis=0).astype(jnp.bfloat16)
    along_x = [(i, i ^ 1) for i in range(n)]
    along_y = [(i, i ^ 2) for i in range(n)]
    mine, to_x, to_y, to_far = pieces[0], pieces[1], pieces[2], pieces[3]
    half = to_far.shape[-2] // 2
    own_x, pass_y = lax.ppermute((to_x, to_far[..., :half, :]), "ctx", along_x)
    own_y, pass_x = lax.ppermute((to_y, to_far[..., half:, :]), "ctx", along_y)
    far_a = lax.ppermute(pass_y, "ctx", along_y)
    far_b = lax.ppermute(pass_x, "ctx", along_x)
    far = jnp.concatenate([far_a, far_b], -2)
    total = (mine.astype(jnp.float32) + own_x.astype(jnp.float32)) + (
        own_y.astype(jnp.float32) + far.astype(jnp.float32))
    return total.astype(jnp.bfloat16)


def pair_reduce(totals, pair_prompt, n_prompts):
    n = lax.axis_size("pair")
    r = lax.axis_index("pair")
    out = None
    for d in range(n):
        chunk = totals[(n - d) % n]
        got = chunk if d == 0 else ring_shift(chunk, "pair", n, d)
        source = (r - d) % n
        hits = (pair_prompt[source] == jnp.arange(n_prompts, dtype=jnp.int32)).astype(jnp.float32)
        term = hits[:, None, None, None] * jnp.transpose(got.astype(jnp.float32), (1, 0, 2))[None]
        out = term if out is None else out + term
    return out


def shards(
    queries, resp_keys, resp_values, d_out, prefix_kv, prefix_blocks, resp_lengths, pair_prompt
):
    n_prompts = prefix_kv.shape[0]
    planes = jnp.transpose(prefix_kv, (0, 2, 1, 3))
    chunk_feats = planes.shape[-1]
    n_groups = HEAD_GROUPS if chunk_feats % (HEAD_GROUPS * HEAD_DIM) == 0 else 1
    group_feats = chunk_feats // n_groups
    pair_index = lax.axis_index("pair").reshape(1).astype(jnp.int32)
    earlier = None
    parts = []
    for k in range(n_groups):
        cols = slice(k * group_feats, (k + 1) * group_feats)
        panel, sources = ctx_gather(pair_gather(planes[..., cols], pair_prompt))
        chunk_blocks = panel.shape[3] // BLOCK
        flags = prefix_blocks[0, 0].reshape(-1, chunk_blocks)[sources].reshape(-1)
        dq, dkr, dvr, dpre = attention_grads(
            flags, resp_lengths[0, 0].reshape(1), pair_index, queries[0, 0], d_out[0, 0], panel,
            resp_keys[0, 0], resp_values[0, 0], k * (group_feats // HEAD_DIM), earlier)
        earlier = (dq, dkr, dvr)
        parts.append(pair_reduce(ctx_reduce(dpre), pair_prompt, n_prompts))
    d_prefix = parts[0] if n_groups == 1 else jnp.concatenate(parts, -1)
    return (dq[None, None], dkr[None, None], dvr[None, None], d_prefix)


def solution(mesh):
    placed = (
        P(("dp", "ctx"), "pair", None, None),
        P(("dp", "ctx"), "pair", None, None),
        P(("dp", "ctx"), "pair", None, None),
        P(("dp", "ctx"), "pair", None, None),
        P("dp", "ctx", None, "pair"),
        P(("dp", "ctx"), "pair", None),
        P(("dp", "ctx"), "pair"),
        P("dp"),
    )
    return jax.shard_map(
        shards,
        mesh=mesh,
        in_specs=placed,
        out_specs=(
            P(("dp", "ctx"), "pair", None, None),
            P(("dp", "ctx"), "pair", None, None),
            P(("dp", "ctx"), "pair", None, None),
            P("dp", "ctx", None, "pair"),
        ),
        check_vma=False,
    )
```

```python
import functools

import jax
import jax.numpy as jnp
from jax import lax
from jax.experimental import pallas as pl
from jax.experimental.pallas import tpu as pltpu
from jax.sharding import PartitionSpec as P

KV_HEADS = 8
GROUP = 2
HEAD_DIM = 128
BLOCK = 128
HEAD_GROUPS = 2


scale_factor = 144.0 ** (-0.5)
neg_big = -1e30

NT = (((1,), (1,)), ((), ()))
TN = (((0,), (0,)), ((), ()))


def attention_grad_kernel(layout, blocks_ref, length_ref, place_ref, q_ref, do_ref, *refs):
    n_in, n_slots, slot_rows, xor_slots, out_ranges, aliased = layout
    kp_refs, vp_refs = refs[:n_in], refs[n_in:2 * n_in]
    kr_ref, vr_ref = refs[2 * n_in:2 * n_in + 2]
    outs = refs[2 * n_in + 2 + (3 if aliased else 0):]
    dq_ref, dkr_ref, dvr_ref = outs[:3]
    piece_refs = outs[3:]
    resp_rows = q_ref.shape[0]
    kp = jnp.concatenate([r[...] for r in kp_refs], 0)
    vp = jnp.concatenate([r[...] for r in vp_refs], 0)
    pre_rows = kp.shape[0]
    kr = kr_ref[...]
    vr = vr_ref[...]

    slot_blocks = slot_rows // BLOCK
    c = place_ref[1]
    col_block = lax.broadcasted_iota(jnp.int32, (1, pre_rows), 1) // BLOCK
    flag = jnp.zeros((1, pre_rows), jnp.int32)
    for b in range(n_slots * slot_blocks):
        slot, sub = b // slot_blocks, b % slot_blocks
        source = jnp.bitwise_xor(c, slot) if xor_slots else slot
        flag = jnp.where(col_block == b, blocks_ref[source * slot_blocks + sub], flag)
    pre_ok = flag > 0
    row_i = lax.broadcasted_iota(jnp.int32, (resp_rows, resp_rows), 0)
    col_i = lax.broadcasted_iota(jnp.int32, (resp_rows, resp_rows), 1)
    causal = row_i >= col_i
    live = lax.broadcasted_iota(jnp.int32, (resp_rows, 1), 0) < length_ref[0]

    dkp = jnp.zeros((pre_rows, HEAD_DIM), jnp.float32)
    dvp = jnp.zeros((pre_rows, HEAD_DIM), jnp.float32)
    dkr = jnp.zeros((resp_rows, HEAD_DIM), jnp.float32)
    dvr = jnp.zeros((resp_rows, HEAD_DIM), jnp.float32)
    for j in range(GROUP):
        cols = slice(j * HEAD_DIM, (j + 1) * HEAD_DIM)
        qj = q_ref[:, cols]
        doj = jnp.where(live, do_ref[:, cols], jnp.zeros_like(do_ref[:, cols]))
        sp = lax.dot_general(qj, kp, NT, preferred_element_type=jnp.float32) * scale_factor
        sr = lax.dot_general(qj, kr, NT, preferred_element_type=jnp.float32) * scale_factor
        sp = jnp.where(pre_ok, sp, neg_big)
        sr = jnp.where(causal, sr, neg_big)
        peak = jnp.maximum(jnp.max(sp, axis=-1, keepdims=True), jnp.max(sr, axis=-1, keepdims=True))
        ep = jnp.exp(sp - peak)
        er = jnp.exp(sr - peak)
        total = jnp.sum(ep, axis=-1, keepdims=True) + jnp.sum(er, axis=-1, keepdims=True)
        wp = ep / total
        wr = er / total
        pp = wp.astype(jnp.bfloat16)
        pr = wr.astype(jnp.bfloat16)
        att = jnp.dot(pp, vp, preferred_element_type=jnp.float32) + jnp.dot(
            pr, vr, preferred_element_type=jnp.float32)
        att = att.astype(jnp.bfloat16).astype(jnp.float32)
        delta = jnp.sum(doj.astype(jnp.float32) * att, axis=-1, keepdims=True)
        dpp = lax.dot_general(doj, vp, NT, preferred_element_type=jnp.float32)
        dpr = lax.dot_general(doj, vr, NT, preferred_element_type=jnp.float32)
        dsp = (wp * (dpp - delta)).astype(jnp.bfloat16)
        dsr = (wr * (dpr - delta)).astype(jnp.bfloat16)
        dq = (jnp.dot(dsp, kp, preferred_element_type=jnp.float32) + jnp.dot(
            dsr, kr, preferred_element_type=jnp.float32)) * scale_factor
        dq_ref[:, cols] = dq.astype(dq_ref.dtype)
        dkp = dkp + lax.dot_general(dsp, qj, TN, preferred_element_type=jnp.float32)
        dkr = dkr + lax.dot_general(dsr, qj, TN, preferred_element_type=jnp.float32)
        dvp = dvp + lax.dot_general(pp, doj, TN, preferred_element_type=jnp.float32)
        dvr = dvr + lax.dot_general(pr, doj, TN, preferred_element_type=jnp.float32)
    dkr_ref[...] = (dkr * scale_factor).astype(dkr_ref.dtype)
    dvr_ref[...] = dvr.astype(dvr_ref.dtype)
    dkp = (dkp * scale_factor).astype(jnp.bfloat16)
    dvp = dvp.astype(jnp.bfloat16)
    for ref, ranges in zip(piece_refs, out_ranges):
        at = 0
        for start, rows in ranges:
            ref[0, at:at + rows] = dkp[start:start + rows]
            ref[1, at:at + rows] = dvp[start:start + rows]
            at += rows


def attention_grads(blocks, length, place, q, do, pieces, xor_slots, out_ranges, kr, vr, first_head, earlier):
    resp_rows, q_width = q.shape
    n_pair, _, _, chunk_feats = pieces[0].shape
    kv_width = kr.shape[1]
    pre_rows = sum(p.shape[2] for p in pieces)
    chunk_heads = kv_width // n_pair // HEAD_DIM
    per_chunk = chunk_feats // HEAD_DIM
    heads = n_pair * per_chunk
    n_slots = lax.axis_size("ctx")
    slot_rows = pre_rows // n_slots

    def head(g, r):
        return ((r[0] + n_pair - g // per_chunk) % n_pair) * chunk_heads + first_head + g % per_chunk

    def piece_spec(rows, kv):
        return pl.BlockSpec((None, None, rows, HEAD_DIM), lambda g, b, n, r: (g // per_chunk, kv, 0, g % per_chunk))

    qspec = pl.BlockSpec((resp_rows, GROUP * HEAD_DIM), lambda g, b, n, r: (0, head(g, r)))
    rspec = pl.BlockSpec((resp_rows, HEAD_DIM), lambda g, b, n, r: (0, head(g, r)))
    in_specs = [qspec, qspec]
    in_specs += [piece_spec(p.shape[2], 0) for p in pieces] + [piece_spec(p.shape[2], 1) for p in pieces]
    in_specs += [rspec, rspec]
    operands = [blocks, length, place, q, do] + list(pieces) + list(pieces) + [kr, vr]
    aliases = {}
    if earlier is not None:
        in_specs += [pl.BlockSpec(memory_space=pl.ANY)] * 3
        aliases = {len(operands) + i: i for i in range(3)}
        operands += list(earlier)
    out_rows = [sum(rows for _, rows in ranges) for ranges in out_ranges]
    out_specs = [qspec, rspec, rspec] + [
        pl.BlockSpec((None, 2, rows, HEAD_DIM), lambda g, b, n, r: (g // per_chunk, 0, 0, g % per_chunk))
        for rows in out_rows]
    out_shape = [
        jax.ShapeDtypeStruct((resp_rows, q_width), jnp.bfloat16),
        jax.ShapeDtypeStruct((resp_rows, kv_width), jnp.bfloat16),
        jax.ShapeDtypeStruct((resp_rows, kv_width), jnp.bfloat16),
    ] + [jax.ShapeDtypeStruct((n_pair, 2, rows, chunk_feats), jnp.bfloat16) for rows in out_rows]
    layout = (len(pieces), n_slots, slot_rows, xor_slots, tuple(tuple(r) for r in out_ranges), earlier is not None)
    flops = 2 * 6 * resp_rows * GROUP * heads * (pre_rows + resp_rows) * HEAD_DIM
    return pl.pallas_call(
        functools.partial(attention_grad_kernel, layout),
        out_shape=tuple(out_shape),
        grid_spec=pltpu.PrefetchScalarGridSpec(
            num_scalar_prefetch=3,
            grid=(heads,),
            in_specs=in_specs,
            out_specs=out_specs,
        ),
        input_output_aliases=aliases,
        cost_estimate=pl.CostEstimate(
            flops=flops,
            transcendentals=resp_rows * GROUP * heads * (pre_rows + resp_rows),
            bytes_accessed=2 * heads * HEAD_DIM * (4 * resp_rows * GROUP + 4 * pre_rows + 4 * resp_rows),
        ),
    )(*operands)


def ring_shift(x, axis, n, d):
    return lax.ppermute(x, axis, [(i, (i + d) % n) for i in range(n)])


def pair_gather(planes, pair_prompt):
    n = lax.axis_size("pair")
    r = lax.axis_index("pair")
    held = [lax.dynamic_index_in_dim(planes, pair_prompt[r], 0, keepdims=False)]
    for d in range(1, n):
        chunk = lax.dynamic_index_in_dim(planes, pair_prompt[(r + d) % n], 0, keepdims=False)
        held.append(ring_shift(chunk, "pair", n, d))
    return jnp.stack(held)


def tree_ctx():
    return lax.axis_size("ctx") == 4


def ctx_gather(x):
    n = lax.axis_size("ctx")
    if not tree_ctx():
        got = lax.all_gather(x, "ctx", axis=0, tiled=False)
        return [got[j] for j in range(n)]
    along_x = [(i, i ^ 1) for i in range(n)]
    along_y = [(i, i ^ 2) for i in range(n)]
    from_x = lax.ppermute(x, "ctx", along_x)
    from_y = lax.ppermute(x, "ctx", along_y)
    half = x.shape[2] // 2
    far_a = lax.ppermute(from_y[:, :, :half], "ctx", along_x)
    far_b = lax.ppermute(from_x[:, :, half:], "ctx", along_y)
    return [x, from_x, from_y, far_a, far_b]


def ctx_out_ranges(slot_rows):
    n = lax.axis_size("ctx")
    if not tree_ctx():
        return [[(j * slot_rows, slot_rows)] for j in range(n)]
    half = slot_rows // 2
    return [[(0, slot_rows)],
            [(slot_rows, slot_rows), (3 * slot_rows, half)],
            [(2 * slot_rows, slot_rows), (3 * slot_rows + half, half)]]


def ctx_reduce(pieces):
    if not tree_ctx():
        got = lax.all_to_all(jnp.stack(pieces), "ctx", split_axis=0, concat_axis=0, tiled=True)
        return jnp.sum(got.astype(jnp.float32), axis=0).astype(jnp.bfloat16)
    n = lax.axis_size("ctx")
    along_x = [(i, i ^ 1) for i in range(n)]
    along_y = [(i, i ^ 2) for i in range(n)]
    mine, send_x, send_y = pieces
    rows = mine.shape[2]
    got_x = lax.ppermute(send_x, "ctx", along_x)
    got_y = lax.ppermute(send_y, "ctx", along_y)
    far_a = lax.ppermute(got_x[:, :, rows:], "ctx", along_y)
    far_b = lax.ppermute(got_y[:, :, rows:], "ctx", along_x)
    far = jnp.concatenate([far_a, far_b], 2)
    total = (mine.astype(jnp.float32) + got_x[:, :, :rows].astype(jnp.float32)) + (
        got_y[:, :, :rows].astype(jnp.float32) + far.astype(jnp.float32))
    return total.astype(jnp.bfloat16)


def pair_reduce(totals, pair_prompt, n_prompts):
    n = lax.axis_size("pair")
    r = lax.axis_index("pair")
    out = None
    for d in range(n):
        chunk = totals[(n - d) % n]
        got = chunk if d == 0 else ring_shift(chunk, "pair", n, d)
        source = (r - d) % n
        hits = (pair_prompt[source] == jnp.arange(n_prompts, dtype=jnp.int32)).astype(jnp.float32)
        term = hits[:, None, None, None] * jnp.transpose(got.astype(jnp.float32), (1, 0, 2))[None]
        out = term if out is None else out + term
    return out


def shards(
    queries, resp_keys, resp_values, d_out, prefix_kv, prefix_blocks, resp_lengths, pair_prompt
):
    n_prompts = prefix_kv.shape[0]
    planes = jnp.transpose(prefix_kv, (0, 2, 1, 3))
    slot_rows = planes.shape[2]
    chunk_feats = planes.shape[-1]
    n_groups = HEAD_GROUPS if chunk_feats % (HEAD_GROUPS * HEAD_DIM) == 0 else 1
    group_feats = chunk_feats // n_groups
    place = jnp.stack([lax.axis_index("pair"), lax.axis_index("ctx")]).astype(jnp.int32)
    earlier = None
    parts = []
    for k in range(n_groups):
        cols = slice(k * group_feats, (k + 1) * group_feats)
        pieces = ctx_gather(pair_gather(planes[..., cols], pair_prompt))
        outs = attention_grads(
            prefix_blocks[0, 0], resp_lengths[0, 0].reshape(1), place, queries[0, 0], d_out[0, 0], pieces,
            tree_ctx(), ctx_out_ranges(slot_rows), resp_keys[0, 0], resp_values[0, 0],
            k * (group_feats // HEAD_DIM), earlier)
        earlier = outs[:3]
        parts.append(pair_reduce(ctx_reduce(list(outs[3:])), pair_prompt, n_prompts))
    dq, dkr, dvr = earlier
    d_prefix = parts[0] if n_groups == 1 else jnp.concatenate(parts, -1)
    return (dq[None, None], dkr[None, None], dvr[None, None], d_prefix)


def solution(mesh):
    placed = (
        P(("dp", "ctx"), "pair", None, None),
        P(("dp", "ctx"), "pair", None, None),
        P(("dp", "ctx"), "pair", None, None),
        P(("dp", "ctx"), "pair", None, None),
        P("dp", "ctx", None, "pair"),
        P(("dp", "ctx"), "pair", None),
        P(("dp", "ctx"), "pair"),
        P("dp"),
    )
    return jax.shard_map(
        shards,
        mesh=mesh,
        in_specs=placed,
        out_specs=(
            P(("dp", "ctx"), "pair", None, None),
            P(("dp", "ctx"), "pair", None, None),
            P(("dp", "ctx"), "pair", None, None),
            P("dp", "ctx", None, "pair"),
        ),
        check_vma=False,
    )
```

```python
import functools

import jax
import jax.numpy as jnp
from jax import lax
from jax.experimental import pallas as pl
from jax.experimental.pallas import tpu as pltpu
from jax.sharding import PartitionSpec as P

KV_HEADS = 8
GROUP = 2
HEAD_DIM = 128
BLOCK = 128
HEAD_GROUPS = 2


scale_factor = 144.0 ** (-0.5)
neg_big = -1e30

NT = (((1,), (1,)), ((), ()))
TN = (((0,), (0,)), ((), ()))


def attention_grad_kernel(layout, blocks_ref, length_ref, place_ref, q_ref, do_ref, *refs):
    n_in, n_slots, slot_rows, xor_slots, out_ranges, aliased = layout
    kp_refs, vp_refs = refs[:n_in], refs[n_in:2 * n_in]
    kr_ref, vr_ref = refs[2 * n_in:2 * n_in + 2]
    outs = refs[2 * n_in + 2 + (3 if aliased else 0):]
    dq_ref, dkr_ref, dvr_ref = outs[:3]
    piece_refs = outs[3:]
    resp_rows = q_ref.shape[0]
    kp = jnp.concatenate([r[...] for r in kp_refs], 0)
    vp = jnp.concatenate([r[...] for r in vp_refs], 0)
    pre_rows = kp.shape[0]
    kr = kr_ref[...]
    vr = vr_ref[...]

    slot_blocks = slot_rows // BLOCK
    c = place_ref[1]
    col_block = lax.broadcasted_iota(jnp.int32, (1, pre_rows), 1) // BLOCK
    flag = jnp.zeros((1, pre_rows), jnp.int32)
    for b in range(n_slots * slot_blocks):
        slot, sub = b // slot_blocks, b % slot_blocks
        source = jnp.bitwise_xor(c, slot) if xor_slots else slot
        flag = jnp.where(col_block == b, blocks_ref[source * slot_blocks + sub], flag)
    pre_ok = flag > 0
    row_i = lax.broadcasted_iota(jnp.int32, (resp_rows, resp_rows), 0)
    col_i = lax.broadcasted_iota(jnp.int32, (resp_rows, resp_rows), 1)
    causal = row_i >= col_i
    live = lax.broadcasted_iota(jnp.int32, (resp_rows, 1), 0) < length_ref[0]

    dkp = jnp.zeros((pre_rows, HEAD_DIM), jnp.float32)
    dvp = jnp.zeros((pre_rows, HEAD_DIM), jnp.float32)
    dkr = jnp.zeros((resp_rows, HEAD_DIM), jnp.float32)
    dvr = jnp.zeros((resp_rows, HEAD_DIM), jnp.float32)
    for j in range(GROUP):
        cols = slice(j * HEAD_DIM, (j + 1) * HEAD_DIM)
        qj = q_ref[:, cols]
        doj = jnp.where(live, do_ref[:, cols], jnp.zeros_like(do_ref[:, cols]))
        sp = lax.dot_general(qj, kp, NT, preferred_element_type=jnp.float32) * scale_factor
        sr = lax.dot_general(qj, kr, NT, preferred_element_type=jnp.float32) * scale_factor
        sp = jnp.where(pre_ok, sp, neg_big)
        sr = jnp.where(causal, sr, neg_big)
        peak = jnp.maximum(jnp.max(sp, axis=-1, keepdims=True), jnp.max(sr, axis=-1, keepdims=True))
        ep = jnp.exp(sp - peak)
        er = jnp.exp(sr - peak)
        total = jnp.sum(ep, axis=-1, keepdims=True) + jnp.sum(er, axis=-1, keepdims=True)
        wp = ep / total
        wr = er / total
        pp = wp.astype(jnp.bfloat16)
        pr = wr.astype(jnp.bfloat16)
        att = jnp.dot(pp, vp, preferred_element_type=jnp.float32) + jnp.dot(
            pr, vr, preferred_element_type=jnp.float32)
        att = att.astype(jnp.bfloat16).astype(jnp.float32)
        delta = jnp.sum(doj.astype(jnp.float32) * att, axis=-1, keepdims=True)
        dpp = lax.dot_general(doj, vp, NT, preferred_element_type=jnp.float32)
        dpr = lax.dot_general(doj, vr, NT, preferred_element_type=jnp.float32)
        dsp = (wp * (dpp - delta)).astype(jnp.bfloat16)
        dsr = (wr * (dpr - delta)).astype(jnp.bfloat16)
        dq = (jnp.dot(dsp, kp, preferred_element_type=jnp.float32) + jnp.dot(
            dsr, kr, preferred_element_type=jnp.float32)) * scale_factor
        dq_ref[:, cols] = dq.astype(dq_ref.dtype)
        dkp = dkp + lax.dot_general(dsp, qj, TN, preferred_element_type=jnp.float32)
        dkr = dkr + lax.dot_general(dsr, qj, TN, preferred_element_type=jnp.float32)
        dvp = dvp + lax.dot_general(pp, doj, TN, preferred_element_type=jnp.float32)
        dvr = dvr + lax.dot_general(pr, doj, TN, preferred_element_type=jnp.float32)
    dkr_ref[...] = (dkr * scale_factor).astype(dkr_ref.dtype)
    dvr_ref[...] = dvr.astype(dvr_ref.dtype)
    dkp = (dkp * scale_factor).astype(jnp.bfloat16)
    dvp = dvp.astype(jnp.bfloat16)
    for ref, ranges in zip(piece_refs, out_ranges):
        at = 0
        for start, rows in ranges:
            ref[0, at:at + rows] = dkp[start:start + rows]
            ref[1, at:at + rows] = dvp[start:start + rows]
            at += rows


def attention_grads(blocks, length, place, q, do, pieces, xor_slots, out_ranges, kr, vr, first_head, earlier):
    resp_rows, q_width = q.shape
    n_pair, _, _, chunk_feats = pieces[0].shape
    kv_width = kr.shape[1]
    pre_rows = sum(p.shape[2] for p in pieces)
    chunk_heads = kv_width // n_pair // HEAD_DIM
    per_chunk = chunk_feats // HEAD_DIM
    heads = n_pair * per_chunk
    n_slots = lax.axis_size("ctx")
    slot_rows = pre_rows // n_slots

    def head(g, r):
        return ((r[0] + n_pair - g // per_chunk) % n_pair) * chunk_heads + first_head + g % per_chunk

    def piece_spec(rows, kv):
        return pl.BlockSpec((None, None, rows, HEAD_DIM), lambda g, b, n, r: (g // per_chunk, kv, 0, g % per_chunk))

    qspec = pl.BlockSpec((resp_rows, GROUP * HEAD_DIM), lambda g, b, n, r: (0, head(g, r)))
    rspec = pl.BlockSpec((resp_rows, HEAD_DIM), lambda g, b, n, r: (0, head(g, r)))
    in_specs = [qspec, qspec]
    in_specs += [piece_spec(p.shape[2], 0) for p in pieces] + [piece_spec(p.shape[2], 1) for p in pieces]
    in_specs += [rspec, rspec]
    operands = [blocks, length, place, q, do] + list(pieces) + list(pieces) + [kr, vr]
    aliases = {}
    if earlier is not None:
        in_specs += [pl.BlockSpec(memory_space=pl.ANY)] * 3
        aliases = {len(operands) + i: i for i in range(3)}
        operands += list(earlier)
    out_rows = [sum(rows for _, rows in ranges) for ranges in out_ranges]
    out_specs = [qspec, rspec, rspec] + [
        pl.BlockSpec((None, 2, rows, HEAD_DIM), lambda g, b, n, r: (g // per_chunk, 0, 0, g % per_chunk))
        for rows in out_rows]
    out_shape = [
        jax.ShapeDtypeStruct((resp_rows, q_width), jnp.bfloat16),
        jax.ShapeDtypeStruct((resp_rows, kv_width), jnp.bfloat16),
        jax.ShapeDtypeStruct((resp_rows, kv_width), jnp.bfloat16),
    ] + [jax.ShapeDtypeStruct((n_pair, 2, rows, chunk_feats), jnp.bfloat16) for rows in out_rows]
    layout = (len(pieces), n_slots, slot_rows, xor_slots, tuple(tuple(r) for r in out_ranges), earlier is not None)
    flops = 2 * 6 * resp_rows * GROUP * heads * (pre_rows + resp_rows) * HEAD_DIM
    return pl.pallas_call(
        functools.partial(attention_grad_kernel, layout),
        out_shape=tuple(out_shape),
        grid_spec=pltpu.PrefetchScalarGridSpec(
            num_scalar_prefetch=3,
            grid=(heads,),
            in_specs=in_specs,
            out_specs=out_specs,
        ),
        input_output_aliases=aliases,
        cost_estimate=pl.CostEstimate(
            flops=flops,
            transcendentals=resp_rows * GROUP * heads * (pre_rows + resp_rows),
            bytes_accessed=2 * heads * HEAD_DIM * (4 * resp_rows * GROUP + 4 * pre_rows + 4 * resp_rows),
        ),
    )(*operands)


def ring_shift(x, axis, n, d):
    return lax.ppermute(x, axis, [(i, (i + d) % n) for i in range(n)])


def pair_gather(planes, pair_prompt):
    n = lax.axis_size("pair")
    r = lax.axis_index("pair")
    held = [lax.dynamic_index_in_dim(planes, pair_prompt[r], 0, keepdims=False)]
    for d in range(1, n):
        chunk = lax.dynamic_index_in_dim(planes, pair_prompt[(r + d) % n], 0, keepdims=False)
        held.append(ring_shift(chunk, "pair", n, d))
    return jnp.stack(held)


def tree_ctx():
    return lax.axis_size("ctx") == 4


def ctx_gather(x):
    n = lax.axis_size("ctx")
    if not tree_ctx():
        got = lax.all_gather(x, "ctx", axis=0, tiled=False)
        return [got[j] for j in range(n)]
    along_x = [(i, i ^ 1) for i in range(n)]
    along_y = [(i, i ^ 2) for i in range(n)]
    from_x = lax.ppermute(x, "ctx", along_x)
    from_y = lax.ppermute(x, "ctx", along_y)
    half = x.shape[2] // 2
    far_a = lax.ppermute(from_y[:, :, :half], "ctx", along_x)
    far_b = lax.ppermute(from_x[:, :, half:], "ctx", along_y)
    return [x, from_x, from_y, far_a, far_b]


def ctx_out_ranges(slot_rows):
    n = lax.axis_size("ctx")
    if not tree_ctx():
        return [[(j * slot_rows, slot_rows)] for j in range(n)]
    half = slot_rows // 2
    return [[(0, slot_rows)],
            [(slot_rows, slot_rows), (3 * slot_rows, half)],
            [(2 * slot_rows, slot_rows), (3 * slot_rows + half, half)]]


def ctx_reduce(pieces):
    if not tree_ctx():
        got = lax.all_to_all(jnp.stack(pieces), "ctx", split_axis=0, concat_axis=0, tiled=True)
        return jnp.sum(got.astype(jnp.float32), axis=0).astype(jnp.bfloat16)
    n = lax.axis_size("ctx")
    along_x = [(i, i ^ 1) for i in range(n)]
    along_y = [(i, i ^ 2) for i in range(n)]
    mine, send_x, send_y = pieces
    rows = mine.shape[2]
    got_x = lax.ppermute(send_x, "ctx", along_x)
    got_y = lax.ppermute(send_y, "ctx", along_y)
    far_a = lax.ppermute(got_x[:, :, rows:], "ctx", along_y)
    far_b = lax.ppermute(got_y[:, :, rows:], "ctx", along_x)
    far = jnp.concatenate([far_a, far_b], 2)
    total = (mine.astype(jnp.float32) + got_x[:, :, :rows].astype(jnp.float32)) + (
        got_y[:, :, :rows].astype(jnp.float32) + far.astype(jnp.float32))
    return total.astype(jnp.bfloat16)


def pair_reduce(totals, pair_prompt, n_prompts):
    n = lax.axis_size("pair")
    r = lax.axis_index("pair")
    out = None
    for d in range(n):
        chunk = totals[(n - d) % n]
        got = chunk if d == 0 else ring_shift(chunk, "pair", n, d)
        source = (r - d) % n
        hits = (pair_prompt[source] == jnp.arange(n_prompts, dtype=jnp.int32)).astype(jnp.float32)
        term = hits[:, None, None, None] * jnp.transpose(got.astype(jnp.float32), (1, 0, 2))[None]
        out = term if out is None else out + term
    return out


def in_group(width, kv_heads, chunk_heads, group_heads, k):
    head = jnp.arange(width) // (width // kv_heads)
    return ((head % chunk_heads) // group_heads == k)[None]


def shards(
    queries, resp_keys, resp_values, d_out, prefix_kv, prefix_blocks, resp_lengths, pair_prompt
):
    n_prompts = prefix_kv.shape[0]
    planes = jnp.transpose(prefix_kv, (0, 2, 1, 3))
    slot_rows = planes.shape[2]
    chunk_feats = planes.shape[-1]
    n_groups = HEAD_GROUPS if chunk_feats % (HEAD_GROUPS * HEAD_DIM) == 0 else 1
    group_feats = chunk_feats // n_groups
    place = jnp.stack([lax.axis_index("pair"), lax.axis_index("ctx")]).astype(jnp.int32)
    kv_heads = resp_keys.shape[-1] // HEAD_DIM
    chunk_heads = chunk_feats // HEAD_DIM
    group_heads = group_feats // HEAD_DIM
    earlier = None
    parts = []
    for k in range(n_groups):
        cols = slice(k * group_feats, (k + 1) * group_feats)
        pieces = ctx_gather(pair_gather(planes[..., cols], pair_prompt))
        outs = attention_grads(
            prefix_blocks[0, 0], resp_lengths[0, 0].reshape(1), place, queries[0, 0], d_out[0, 0], pieces,
            tree_ctx(), ctx_out_ranges(slot_rows), resp_keys[0, 0], resp_values[0, 0],
            k * (group_feats // HEAD_DIM), None)
        if earlier is None:
            earlier = outs[:3]
        else:
            earlier = tuple(jnp.where(in_group(o.shape[1], kv_heads, chunk_heads, group_heads, k), o, e)
                            for o, e in zip(outs[:3], earlier))
        parts.append(pair_reduce(ctx_reduce(list(outs[3:])), pair_prompt, n_prompts))
    dq, dkr, dvr = earlier
    d_prefix = parts[0] if n_groups == 1 else jnp.concatenate(parts, -1)
    return (dq[None, None], dkr[None, None], dvr[None, None], d_prefix)


def solution(mesh):
    placed = (
        P(("dp", "ctx"), "pair", None, None),
        P(("dp", "ctx"), "pair", None, None),
        P(("dp", "ctx"), "pair", None, None),
        P(("dp", "ctx"), "pair", None, None),
        P("dp", "ctx", None, "pair"),
        P(("dp", "ctx"), "pair", None),
        P(("dp", "ctx"), "pair"),
        P("dp"),
    )
    return jax.shard_map(
        shards,
        mesh=mesh,
        in_specs=placed,
        out_specs=(
            P(("dp", "ctx"), "pair", None, None),
            P(("dp", "ctx"), "pair", None, None),
            P(("dp", "ctx"), "pair", None, None),
            P("dp", "ctx", None, "pair"),
        ),
        check_vma=False,
    )
```

```python
import functools

import jax
import jax.numpy as jnp
from jax import lax
from jax.experimental import pallas as pl
from jax.experimental.pallas import tpu as pltpu
from jax.sharding import PartitionSpec as P

KV_HEADS = 8
GROUP = 2
HEAD_DIM = 128
BLOCK = 128
HEAD_GROUPS = 2


scale_factor = 144.0 ** (-0.5)
neg_big = -1e30

NT = (((1,), (1,)), ((), ()))
TN = (((0,), (0,)), ((), ()))


def attention_grad_kernel(layout, blocks_ref, length_ref, place_ref, q_ref, do_ref, *refs):
    n_in, n_slots, slot_rows, xor_slots, out_ranges, aliased = layout
    kp_refs, vp_refs = refs[:n_in], refs[n_in:2 * n_in]
    kr_ref, vr_ref = refs[2 * n_in:2 * n_in + 2]
    outs = refs[2 * n_in + 2 + (3 if aliased else 0):]
    dq_ref, dkr_ref, dvr_ref = outs[:3]
    piece_refs = outs[3:]
    resp_rows = q_ref.shape[0]
    kp = jnp.concatenate([r[...] for r in kp_refs], 0)
    vp = jnp.concatenate([r[...] for r in vp_refs], 0)
    pre_rows = kp.shape[0]
    kr = kr_ref[...]
    vr = vr_ref[...]

    slot_blocks = slot_rows // BLOCK
    c = place_ref[1]
    col_block = lax.broadcasted_iota(jnp.int32, (1, pre_rows), 1) // BLOCK
    flag = jnp.zeros((1, pre_rows), jnp.int32)
    for b in range(n_slots * slot_blocks):
        slot, sub = b // slot_blocks, b % slot_blocks
        source = jnp.bitwise_xor(c, slot) if xor_slots else slot
        flag = jnp.where(col_block == b, blocks_ref[source * slot_blocks + sub], flag)
    pre_ok = flag > 0
    rows = GROUP * resp_rows
    row_i = lax.broadcasted_iota(jnp.int32, (rows, resp_rows), 0) % resp_rows
    col_i = lax.broadcasted_iota(jnp.int32, (rows, resp_rows), 1)
    causal = row_i >= col_i
    live = lax.broadcasted_iota(jnp.int32, (rows, 1), 0) % resp_rows < length_ref[0]
    heads = [slice(j * HEAD_DIM, (j + 1) * HEAD_DIM) for j in range(GROUP)]
    q2 = jnp.concatenate([q_ref[:, cols] for cols in heads], 0)
    do2 = jnp.concatenate([do_ref[:, cols] for cols in heads], 0)
    do2 = jnp.where(live, do2, jnp.zeros_like(do2))

    sp = lax.dot_general(q2, kp, NT, preferred_element_type=jnp.float32) * scale_factor
    sr = lax.dot_general(q2, kr, NT, preferred_element_type=jnp.float32) * scale_factor
    sp = jnp.where(pre_ok, sp, neg_big)
    sr = jnp.where(causal, sr, neg_big)
    peak = jnp.maximum(jnp.max(sp, axis=-1, keepdims=True), jnp.max(sr, axis=-1, keepdims=True))
    ep = jnp.exp(sp - peak)
    er = jnp.exp(sr - peak)
    inv = 1.0 / (jnp.sum(ep, axis=-1, keepdims=True) + jnp.sum(er, axis=-1, keepdims=True))
    wp = ep * inv
    wr = er * inv
    pp = wp.astype(jnp.bfloat16)
    pr = wr.astype(jnp.bfloat16)
    att = jnp.dot(pp, vp, preferred_element_type=jnp.float32) + jnp.dot(pr, vr, preferred_element_type=jnp.float32)
    att = att.astype(jnp.bfloat16).astype(jnp.float32)
    delta = jnp.sum(do2.astype(jnp.float32) * att, axis=-1, keepdims=True)
    dpp = lax.dot_general(do2, vp, NT, preferred_element_type=jnp.float32)
    dpr = lax.dot_general(do2, vr, NT, preferred_element_type=jnp.float32)
    dsp = (wp * (dpp - delta)).astype(jnp.bfloat16)
    dsr = (wr * (dpr - delta)).astype(jnp.bfloat16)
    dq = (jnp.dot(dsp, kp, preferred_element_type=jnp.float32) + jnp.dot(
        dsr, kr, preferred_element_type=jnp.float32)) * scale_factor
    dq = dq.astype(dq_ref.dtype)
    for j, cols in enumerate(heads):
        dq_ref[:, cols] = dq[j * resp_rows:(j + 1) * resp_rows]
    dkp = lax.dot_general(dsp, q2, TN, preferred_element_type=jnp.float32)
    dkr = lax.dot_general(dsr, q2, TN, preferred_element_type=jnp.float32)
    dvp = lax.dot_general(pp, do2, TN, preferred_element_type=jnp.float32)
    dvr = lax.dot_general(pr, do2, TN, preferred_element_type=jnp.float32)
    dkr_ref[...] = (dkr * scale_factor).astype(dkr_ref.dtype)
    dvr_ref[...] = dvr.astype(dvr_ref.dtype)
    dkp = (dkp * scale_factor).astype(jnp.bfloat16)
    dvp = dvp.astype(jnp.bfloat16)
    for ref, ranges in zip(piece_refs, out_ranges):
        at = 0
        for start, rows in ranges:
            ref[0, at:at + rows] = dkp[start:start + rows]
            ref[1, at:at + rows] = dvp[start:start + rows]
            at += rows


def attention_grads(blocks, length, place, q, do, pieces, xor_slots, out_ranges, kr, vr, first_head, earlier):
    resp_rows, q_width = q.shape
    n_pair, _, _, chunk_feats = pieces[0].shape
    kv_width = kr.shape[1]
    pre_rows = sum(p.shape[2] for p in pieces)
    chunk_heads = kv_width // n_pair // HEAD_DIM
    per_chunk = chunk_feats // HEAD_DIM
    heads = n_pair * per_chunk
    n_slots = lax.axis_size("ctx")
    slot_rows = pre_rows // n_slots

    def head(g, r):
        return ((r[0] + n_pair - g // per_chunk) % n_pair) * chunk_heads + first_head + g % per_chunk

    def piece_spec(rows, kv):
        return pl.BlockSpec((None, None, rows, HEAD_DIM), lambda g, b, n, r: (g // per_chunk, kv, 0, g % per_chunk))

    qspec = pl.BlockSpec((resp_rows, GROUP * HEAD_DIM), lambda g, b, n, r: (0, head(g, r)))
    rspec = pl.BlockSpec((resp_rows, HEAD_DIM), lambda g, b, n, r: (0, head(g, r)))
    in_specs = [qspec, qspec]
    in_specs += [piece_spec(p.shape[2], 0) for p in pieces] + [piece_spec(p.shape[2], 1) for p in pieces]
    in_specs += [rspec, rspec]
    operands = [blocks, length, place, q, do] + list(pieces) + list(pieces) + [kr, vr]
    aliases = {}
    if earlier is not None:
        in_specs += [pl.BlockSpec(memory_space=pl.ANY)] * 3
        aliases = {len(operands) + i: i for i in range(3)}
        operands += list(earlier)
    out_rows = [sum(rows for _, rows in ranges) for ranges in out_ranges]
    out_specs = [qspec, rspec, rspec] + [
        pl.BlockSpec((None, 2, rows, HEAD_DIM), lambda g, b, n, r: (g // per_chunk, 0, 0, g % per_chunk))
        for rows in out_rows]
    out_shape = [
        jax.ShapeDtypeStruct((resp_rows, q_width), jnp.bfloat16),
        jax.ShapeDtypeStruct((resp_rows, kv_width), jnp.bfloat16),
        jax.ShapeDtypeStruct((resp_rows, kv_width), jnp.bfloat16),
    ] + [jax.ShapeDtypeStruct((n_pair, 2, rows, chunk_feats), jnp.bfloat16) for rows in out_rows]
    layout = (len(pieces), n_slots, slot_rows, xor_slots, tuple(tuple(r) for r in out_ranges), earlier is not None)
    flops = 2 * 6 * resp_rows * GROUP * heads * (pre_rows + resp_rows) * HEAD_DIM
    return pl.pallas_call(
        functools.partial(attention_grad_kernel, layout),
        out_shape=tuple(out_shape),
        grid_spec=pltpu.PrefetchScalarGridSpec(
            num_scalar_prefetch=3,
            grid=(heads,),
            in_specs=in_specs,
            out_specs=out_specs,
        ),
        input_output_aliases=aliases,
        cost_estimate=pl.CostEstimate(
            flops=flops,
            transcendentals=resp_rows * GROUP * heads * (pre_rows + resp_rows),
            bytes_accessed=2 * heads * HEAD_DIM * (4 * resp_rows * GROUP + 4 * pre_rows + 4 * resp_rows),
        ),
    )(*operands)


def ring_shift(x, axis, n, d):
    return lax.ppermute(x, axis, [(i, (i + d) % n) for i in range(n)])


def pair_gather(planes, pair_prompt):
    n = lax.axis_size("pair")
    r = lax.axis_index("pair")
    held = [lax.dynamic_index_in_dim(planes, pair_prompt[r], 0, keepdims=False)]
    for d in range(1, n):
        chunk = lax.dynamic_index_in_dim(planes, pair_prompt[(r + d) % n], 0, keepdims=False)
        held.append(ring_shift(chunk, "pair", n, d))
    return jnp.stack(held)


def tree_ctx():
    return lax.axis_size("ctx") == 4


def ctx_gather(x):
    n = lax.axis_size("ctx")
    if not tree_ctx():
        got = lax.all_gather(x, "ctx", axis=0, tiled=False)
        return [got[j] for j in range(n)]
    along_x = [(i, i ^ 1) for i in range(n)]
    along_y = [(i, i ^ 2) for i in range(n)]
    from_x = lax.ppermute(x, "ctx", along_x)
    from_y = lax.ppermute(x, "ctx", along_y)
    half = x.shape[2] // 2
    far_a = lax.ppermute(from_y[:, :, :half], "ctx", along_x)
    far_b = lax.ppermute(from_x[:, :, half:], "ctx", along_y)
    return [x, from_x, from_y, far_a, far_b]


def ctx_out_ranges(slot_rows):
    n = lax.axis_size("ctx")
    if not tree_ctx():
        return [[(j * slot_rows, slot_rows)] for j in range(n)]
    half = slot_rows // 2
    return [[(0, slot_rows)],
            [(slot_rows, slot_rows), (3 * slot_rows, half)],
            [(2 * slot_rows, slot_rows), (3 * slot_rows + half, half)]]


def ctx_reduce(pieces):
    if not tree_ctx():
        got = lax.all_to_all(jnp.stack(pieces), "ctx", split_axis=0, concat_axis=0, tiled=True)
        return jnp.sum(got.astype(jnp.float32), axis=0).astype(jnp.bfloat16)
    n = lax.axis_size("ctx")
    along_x = [(i, i ^ 1) for i in range(n)]
    along_y = [(i, i ^ 2) for i in range(n)]
    mine, send_x, send_y = pieces
    rows = mine.shape[2]
    got_x = lax.ppermute(send_x, "ctx", along_x)
    got_y = lax.ppermute(send_y, "ctx", along_y)
    far_a = lax.ppermute(got_x[:, :, rows:], "ctx", along_y)
    far_b = lax.ppermute(got_y[:, :, rows:], "ctx", along_x)
    far = jnp.concatenate([far_a, far_b], 2)
    total = (mine.astype(jnp.float32) + got_x[:, :, :rows].astype(jnp.float32)) + (
        got_y[:, :, :rows].astype(jnp.float32) + far.astype(jnp.float32))
    return total.astype(jnp.bfloat16)


def pair_reduce(totals, pair_prompt, n_prompts):
    n = lax.axis_size("pair")
    r = lax.axis_index("pair")
    out = None
    for d in range(n):
        chunk = totals[(n - d) % n]
        got = chunk if d == 0 else ring_shift(chunk, "pair", n, d)
        source = (r - d) % n
        hits = (pair_prompt[source] == jnp.arange(n_prompts, dtype=jnp.int32)).astype(jnp.float32)
        term = hits[:, None, None, None] * jnp.transpose(got.astype(jnp.float32), (1, 0, 2))[None]
        out = term if out is None else out + term
    return out


def in_group(width, kv_heads, chunk_heads, group_heads, k):
    head = jnp.arange(width) // (width // kv_heads)
    return ((head % chunk_heads) // group_heads == k)[None]


def shards(
    queries, resp_keys, resp_values, d_out, prefix_kv, prefix_blocks, resp_lengths, pair_prompt
):
    n_prompts = prefix_kv.shape[0]
    planes = jnp.transpose(prefix_kv, (0, 2, 1, 3))
    slot_rows = planes.shape[2]
    chunk_feats = planes.shape[-1]
    n_groups = HEAD_GROUPS if chunk_feats % (HEAD_GROUPS * HEAD_DIM) == 0 else 1
    group_feats = chunk_feats // n_groups
    place = jnp.stack([lax.axis_index("pair"), lax.axis_index("ctx")]).astype(jnp.int32)
    kv_heads = resp_keys.shape[-1] // HEAD_DIM
    chunk_heads = chunk_feats // HEAD_DIM
    group_heads = group_feats // HEAD_DIM
    earlier = None
    parts = []
    for k in range(n_groups):
        cols = slice(k * group_feats, (k + 1) * group_feats)
        pieces = ctx_gather(pair_gather(planes[..., cols], pair_prompt))
        outs = attention_grads(
            prefix_blocks[0, 0], resp_lengths[0, 0].reshape(1), place, queries[0, 0], d_out[0, 0], pieces,
            tree_ctx(), ctx_out_ranges(slot_rows), resp_keys[0, 0], resp_values[0, 0],
            k * (group_feats // HEAD_DIM), None)
        if earlier is None:
            earlier = outs[:3]
        else:
            earlier = tuple(jnp.where(in_group(o.shape[1], kv_heads, chunk_heads, group_heads, k), o, e)
                            for o, e in zip(outs[:3], earlier))
        parts.append(pair_reduce(ctx_reduce(list(outs[3:])), pair_prompt, n_prompts))
    dq, dkr, dvr = earlier
    d_prefix = parts[0] if n_groups == 1 else jnp.concatenate(parts, -1)
    return (dq[None, None], dkr[None, None], dvr[None, None], d_prefix)


def solution(mesh):
    placed = (
        P(("dp", "ctx"), "pair", None, None),
        P(("dp", "ctx"), "pair", None, None),
        P(("dp", "ctx"), "pair", None, None),
        P(("dp", "ctx"), "pair", None, None),
        P("dp", "ctx", None, "pair"),
        P(("dp", "ctx"), "pair", None),
        P(("dp", "ctx"), "pair"),
        P("dp"),
    )
    return jax.shard_map(
        shards,
        mesh=mesh,
        in_specs=placed,
        out_specs=(
            P(("dp", "ctx"), "pair", None, None),
            P(("dp", "ctx"), "pair", None, None),
            P(("dp", "ctx"), "pair", None, None),
            P("dp", "ctx", None, "pair"),
        ),
        check_vma=False,
    )
```

```python
import functools

import jax
import jax.numpy as jnp
from jax import lax
from jax.experimental import pallas as pl
from jax.experimental.pallas import tpu as pltpu
from jax.sharding import PartitionSpec as P

KV_HEADS = 8
GROUP = 2
HEAD_DIM = 128
BLOCK = 128
HEAD_GROUPS = 2


scale_factor = 144.0 ** (-0.5)
neg_big = -1e30

NT = (((1,), (1,)), ((), ()))
TN = (((0,), (0,)), ((), ()))


def attention_grad_kernel(layout, blocks_ref, length_ref, place_ref, q_ref, do_ref, *refs):
    n_in, n_slots, slot_rows, xor_slots, out_ranges, aliased = layout
    kp_refs, vp_refs = refs[:n_in], refs[n_in:2 * n_in]
    kr_ref, vr_ref = refs[2 * n_in:2 * n_in + 2]
    outs = refs[2 * n_in + 2 + (3 if aliased else 0):]
    dq_ref, dkr_ref, dvr_ref = outs[:3]
    piece_refs = outs[3:]
    resp_rows = q_ref.shape[0]
    kp = jnp.concatenate([r[...] for r in kp_refs], 0)
    vp = jnp.concatenate([r[...] for r in vp_refs], 0)
    pre_rows = kp.shape[0]
    kr = kr_ref[...]
    vr = vr_ref[...]

    slot_blocks = slot_rows // BLOCK
    c = place_ref[1]
    col_block = lax.broadcasted_iota(jnp.int32, (1, pre_rows), 1) // BLOCK
    flag = jnp.zeros((1, pre_rows), jnp.int32)
    for b in range(n_slots * slot_blocks):
        slot, sub = b // slot_blocks, b % slot_blocks
        source = jnp.bitwise_xor(c, slot) if xor_slots else slot
        flag = jnp.where(col_block == b, blocks_ref[source * slot_blocks + sub], flag)
    pre_ok = flag > 0
    rows = GROUP * resp_rows
    row_i = lax.broadcasted_iota(jnp.int32, (rows, resp_rows), 0) % resp_rows
    col_i = lax.broadcasted_iota(jnp.int32, (rows, resp_rows), 1)
    causal = row_i >= col_i
    live = lax.broadcasted_iota(jnp.int32, (rows, 1), 0) % resp_rows < length_ref[0]
    heads = [slice(j * HEAD_DIM, (j + 1) * HEAD_DIM) for j in range(GROUP)]
    q2 = jnp.concatenate([q_ref[:, cols] for cols in heads], 0)
    do2 = jnp.concatenate([do_ref[:, cols] for cols in heads], 0)
    do2 = jnp.where(live, do2, jnp.zeros_like(do2))

    sp = lax.dot_general(q2, kp, NT, preferred_element_type=jnp.float32) * scale_factor
    sr = lax.dot_general(q2, kr, NT, preferred_element_type=jnp.float32) * scale_factor
    sp = jnp.where(pre_ok, sp, neg_big)
    sr = jnp.where(causal, sr, neg_big)
    peak = jnp.maximum(jnp.max(sp, axis=-1, keepdims=True), jnp.max(sr, axis=-1, keepdims=True))
    ep = jnp.exp(sp - peak)
    er = jnp.exp(sr - peak)
    inv = 1.0 / (jnp.sum(ep, axis=-1, keepdims=True) + jnp.sum(er, axis=-1, keepdims=True))
    wp = ep * inv
    wr = er * inv
    pp = wp.astype(jnp.bfloat16)
    pr = wr.astype(jnp.bfloat16)
    att = jnp.dot(pp, vp, preferred_element_type=jnp.float32) + jnp.dot(pr, vr, preferred_element_type=jnp.float32)
    att = att.astype(jnp.bfloat16).astype(jnp.float32)
    delta = jnp.sum(do2.astype(jnp.float32) * att, axis=-1, keepdims=True)
    dpp = lax.dot_general(do2, vp, NT, preferred_element_type=jnp.float32)
    dpr = lax.dot_general(do2, vr, NT, preferred_element_type=jnp.float32)
    dsp = (wp * (dpp - delta)).astype(jnp.bfloat16)
    dsr = (wr * (dpr - delta)).astype(jnp.bfloat16)
    dq = (jnp.dot(dsp, kp, preferred_element_type=jnp.float32) + jnp.dot(
        dsr, kr, preferred_element_type=jnp.float32)) * scale_factor
    dq = dq.astype(dq_ref.dtype)
    for j, cols in enumerate(heads):
        dq_ref[:, cols] = dq[j * resp_rows:(j + 1) * resp_rows]
    dkp = lax.dot_general(dsp, q2, TN, preferred_element_type=jnp.float32)
    dkr = lax.dot_general(dsr, q2, TN, preferred_element_type=jnp.float32)
    dvp = lax.dot_general(pp, do2, TN, preferred_element_type=jnp.float32)
    dvr = lax.dot_general(pr, do2, TN, preferred_element_type=jnp.float32)
    dkr_ref[...] = (dkr * scale_factor).astype(dkr_ref.dtype)
    dvr_ref[...] = dvr.astype(dvr_ref.dtype)
    dkp = (dkp * scale_factor).astype(jnp.bfloat16)
    dvp = dvp.astype(jnp.bfloat16)
    for ref, ranges in zip(piece_refs, out_ranges):
        at = 0
        for start, rows in ranges:
            ref[0, at:at + rows] = dkp[start:start + rows]
            ref[1, at:at + rows] = dvp[start:start + rows]
            at += rows


def attention_grads(blocks, length, place, q, do, pieces, xor_slots, out_ranges, kr, vr, first_head, earlier):
    resp_rows, q_width = q.shape
    n_pair, _, _, chunk_feats = pieces[0].shape
    kv_width = kr.shape[1]
    pre_rows = sum(p.shape[2] for p in pieces)
    chunk_heads = kv_width // n_pair // HEAD_DIM
    per_chunk = chunk_feats // HEAD_DIM
    heads = n_pair * per_chunk
    n_slots = lax.axis_size("ctx")
    slot_rows = pre_rows // n_slots

    def head(g, r):
        return ((r[0] + n_pair - g // per_chunk) % n_pair) * chunk_heads + first_head + g % per_chunk

    def piece_spec(rows, kv):
        return pl.BlockSpec((None, None, rows, HEAD_DIM), lambda g, b, n, r: (g // per_chunk, kv, 0, g % per_chunk))

    qspec = pl.BlockSpec((resp_rows, GROUP * HEAD_DIM), lambda g, b, n, r: (0, head(g, r)))
    rspec = pl.BlockSpec((resp_rows, HEAD_DIM), lambda g, b, n, r: (0, head(g, r)))
    in_specs = [qspec, qspec]
    in_specs += [piece_spec(p.shape[2], 0) for p in pieces] + [piece_spec(p.shape[2], 1) for p in pieces]
    in_specs += [rspec, rspec]
    operands = [blocks, length, place, q, do] + list(pieces) + list(pieces) + [kr, vr]
    aliases = {}
    if earlier is not None:
        in_specs += [pl.BlockSpec(memory_space=pl.ANY)] * 3
        aliases = {len(operands) + i: i for i in range(3)}
        operands += list(earlier)
    out_rows = [sum(rows for _, rows in ranges) for ranges in out_ranges]
    out_specs = [qspec, rspec, rspec] + [
        pl.BlockSpec((None, 2, rows, HEAD_DIM), lambda g, b, n, r: (g // per_chunk, 0, 0, g % per_chunk))
        for rows in out_rows]
    out_shape = [
        jax.ShapeDtypeStruct((resp_rows, q_width), jnp.bfloat16),
        jax.ShapeDtypeStruct((resp_rows, kv_width), jnp.bfloat16),
        jax.ShapeDtypeStruct((resp_rows, kv_width), jnp.bfloat16),
    ] + [jax.ShapeDtypeStruct((n_pair, 2, rows, chunk_feats), jnp.bfloat16) for rows in out_rows]
    layout = (len(pieces), n_slots, slot_rows, xor_slots, tuple(tuple(r) for r in out_ranges), earlier is not None)
    flops = 2 * 6 * resp_rows * GROUP * heads * (pre_rows + resp_rows) * HEAD_DIM
    return pl.pallas_call(
        functools.partial(attention_grad_kernel, layout),
        out_shape=tuple(out_shape),
        grid_spec=pltpu.PrefetchScalarGridSpec(
            num_scalar_prefetch=3,
            grid=(heads,),
            in_specs=in_specs,
            out_specs=out_specs,
        ),
        input_output_aliases=aliases,
        cost_estimate=pl.CostEstimate(
            flops=flops,
            transcendentals=resp_rows * GROUP * heads * (pre_rows + resp_rows),
            bytes_accessed=2 * heads * HEAD_DIM * (4 * resp_rows * GROUP + 4 * pre_rows + 4 * resp_rows),
        ),
    )(*operands)


def ring_shift(x, axis, n, d):
    return lax.ppermute(x, axis, [(i, (i + d) % n) for i in range(n)])


def pair_gather(planes, pair_prompt):
    n = lax.axis_size("pair")
    r = lax.axis_index("pair")
    held = [lax.dynamic_index_in_dim(planes, pair_prompt[r], 0, keepdims=False)]
    for d in range(1, n):
        chunk = lax.dynamic_index_in_dim(planes, pair_prompt[(r + d) % n], 0, keepdims=False)
        held.append(ring_shift(chunk, "pair", n, d))
    return jnp.stack(held)


def tree_ctx():
    return lax.axis_size("ctx") == 4


def ctx_gather(x):
    n = lax.axis_size("ctx")
    if not tree_ctx():
        got = lax.all_gather(x, "ctx", axis=0, tiled=False)
        return [got[j] for j in range(n)]
    along_x = [(i, i ^ 1) for i in range(n)]
    along_y = [(i, i ^ 2) for i in range(n)]
    from_x = lax.ppermute(x, "ctx", along_x)
    from_y = lax.ppermute(x, "ctx", along_y)
    half = x.shape[2] // 2
    far_a = lax.ppermute(from_y[:, :, :half], "ctx", along_x)
    far_b = lax.ppermute(from_x[:, :, half:], "ctx", along_y)
    return [x, from_x, from_y, far_a, far_b]


def ctx_out_ranges(slot_rows):
    n = lax.axis_size("ctx")
    if not tree_ctx():
        return [[(j * slot_rows, slot_rows)] for j in range(n)]
    half = slot_rows // 2
    return [[(0, slot_rows)],
            [(slot_rows, slot_rows), (3 * slot_rows, half)],
            [(2 * slot_rows, slot_rows), (3 * slot_rows + half, half)]]


def ctx_reduce(pieces):
    if not tree_ctx():
        got = lax.all_to_all(jnp.stack(pieces), "ctx", split_axis=0, concat_axis=0, tiled=True)
        return jnp.sum(got.astype(jnp.float32), axis=0).astype(jnp.bfloat16)
    n = lax.axis_size("ctx")
    along_x = [(i, i ^ 1) for i in range(n)]
    along_y = [(i, i ^ 2) for i in range(n)]
    mine, send_x, send_y = pieces
    rows = mine.shape[2]
    got_x = lax.ppermute(send_x, "ctx", along_x)
    got_y = lax.ppermute(send_y, "ctx", along_y)
    far_a = lax.ppermute(got_x[:, :, rows:], "ctx", along_y)
    far_b = lax.ppermute(got_y[:, :, rows:], "ctx", along_x)
    far = jnp.concatenate([far_a, far_b], 2)
    total = (mine.astype(jnp.float32) + got_x[:, :, :rows].astype(jnp.float32)) + (
        got_y[:, :, :rows].astype(jnp.float32) + far.astype(jnp.float32))
    return total.astype(jnp.bfloat16)


def pair_reduce(totals, pair_prompt, n_prompts):
    n = lax.axis_size("pair")
    r = lax.axis_index("pair")
    out = None
    for d in range(n):
        chunk = totals[(n - d) % n]
        got = chunk if d == 0 else ring_shift(chunk, "pair", n, d)
        source = (r - d) % n
        hits = (pair_prompt[source] == jnp.arange(n_prompts, dtype=jnp.int32)).astype(jnp.float32)
        term = hits[:, None, None, None] * jnp.transpose(got.astype(jnp.float32), (1, 0, 2))[None]
        out = term if out is None else out + term
    return out


def in_group(width, kv_heads, chunk_heads, group_heads, k):
    head = jnp.arange(width) // (width // kv_heads)
    return ((head % chunk_heads) // group_heads == k)[None]


def shards(
    queries, resp_keys, resp_values, d_out, prefix_kv, prefix_blocks, resp_lengths, pair_prompt
):
    n_prompts = prefix_kv.shape[0]
    planes = jnp.transpose(prefix_kv, (0, 2, 1, 3))
    slot_rows = planes.shape[2]
    chunk_feats = planes.shape[-1]
    n_groups = HEAD_GROUPS if chunk_feats % (HEAD_GROUPS * HEAD_DIM) == 0 else 1
    group_feats = chunk_feats // n_groups
    place = jnp.stack([lax.axis_index("pair"), lax.axis_index("ctx")]).astype(jnp.int32)
    kv_heads = resp_keys.shape[-1] // HEAD_DIM
    chunk_heads = chunk_feats // HEAD_DIM
    group_heads = group_feats // HEAD_DIM
    earlier = None
    parts = []
    for k in range(n_groups):
        cols = slice(k * group_feats, (k + 1) * group_feats)
        pieces = ctx_gather(pair_gather(planes[..., cols], pair_prompt))
        outs = attention_grads(
            prefix_blocks[0, 0], resp_lengths[0, 0].reshape(1), place, queries[0, 0], d_out[0, 0], pieces,
            tree_ctx(), ctx_out_ranges(slot_rows), resp_keys[0, 0], resp_values[0, 0],
            k * (group_feats // HEAD_DIM), None)
        if earlier is None:
            earlier = outs[:3]
        else:
            earlier = tuple(jnp.where(in_group(o.shape[1], kv_heads, chunk_heads, group_heads, k), o, e)
                            for o, e in zip(outs[:3], earlier))
        parts.append(ctx_reduce(list(outs[3:])))
    dq, dkr, dvr = earlier
    d_prefix = pair_reduce(parts[0] if n_groups == 1 else jnp.concatenate(parts, -1), pair_prompt, n_prompts)
    return (dq[None, None], dkr[None, None], dvr[None, None], d_prefix)


def solution(mesh):
    placed = (
        P(("dp", "ctx"), "pair", None, None),
        P(("dp", "ctx"), "pair", None, None),
        P(("dp", "ctx"), "pair", None, None),
        P(("dp", "ctx"), "pair", None, None),
        P("dp", "ctx", None, "pair"),
        P(("dp", "ctx"), "pair", None),
        P(("dp", "ctx"), "pair"),
        P("dp"),
    )
    return jax.shard_map(
        shards,
        mesh=mesh,
        in_specs=placed,
        out_specs=(
            P(("dp", "ctx"), "pair", None, None),
            P(("dp", "ctx"), "pair", None, None),
            P(("dp", "ctx"), "pair", None, None),
            P("dp", "ctx", None, "pair"),
        ),
        check_vma=False,
    )
```

```python
import functools

import jax
import jax.numpy as jnp
from jax import lax
from jax.experimental import pallas as pl
from jax.experimental.pallas import tpu as pltpu
from jax.sharding import PartitionSpec as P

KV_HEADS = 8
GROUP = 2
HEAD_DIM = 128
BLOCK = 128
HEAD_GROUPS = 2


scale_factor = 144.0 ** (-0.5)
neg_big = -1e30

NT = (((1,), (1,)), ((), ()))
TN = (((0,), (0,)), ((), ()))


def attention_grad_kernel(layout, blocks_ref, length_ref, place_ref, q_ref, do_ref, *refs):
    n_in, n_slots, slot_rows, xor_slots, out_ranges, aliased = layout
    kp_refs, vp_refs = refs[:n_in], refs[n_in:2 * n_in]
    kr_ref, vr_ref = refs[2 * n_in:2 * n_in + 2]
    outs = refs[2 * n_in + 2 + (3 if aliased else 0):]
    dq_ref, dkr_ref, dvr_ref = outs[:3]
    piece_refs = outs[3:]
    resp_rows = q_ref.shape[0]
    kp = jnp.concatenate([r[...] for r in kp_refs], 0)
    vp = jnp.concatenate([r[...] for r in vp_refs], 0)
    pre_rows = kp.shape[0]
    kr = kr_ref[...]
    vr = vr_ref[...]

    slot_blocks = slot_rows // BLOCK
    c = place_ref[1]
    col_block = lax.broadcasted_iota(jnp.int32, (1, pre_rows), 1) // BLOCK
    flag = jnp.zeros((1, pre_rows), jnp.int32)
    for b in range(n_slots * slot_blocks):
        slot, sub = b // slot_blocks, b % slot_blocks
        source = jnp.bitwise_xor(c, slot) if xor_slots else slot
        flag = jnp.where(col_block == b, blocks_ref[source * slot_blocks + sub], flag)
    pre_ok = flag > 0
    rows = GROUP * resp_rows
    row_i = lax.broadcasted_iota(jnp.int32, (rows, resp_rows), 0) % resp_rows
    col_i = lax.broadcasted_iota(jnp.int32, (rows, resp_rows), 1)
    causal = row_i >= col_i
    live = lax.broadcasted_iota(jnp.int32, (rows, 1), 0) % resp_rows < length_ref[0]
    heads = [slice(j * HEAD_DIM, (j + 1) * HEAD_DIM) for j in range(GROUP)]
    q2 = jnp.concatenate([q_ref[:, cols] for cols in heads], 0)
    do2 = jnp.concatenate([do_ref[:, cols] for cols in heads], 0)
    do2 = jnp.where(live, do2, jnp.zeros_like(do2))

    sp = lax.dot_general(q2, kp, NT, preferred_element_type=jnp.float32) * scale_factor
    sr = lax.dot_general(q2, kr, NT, preferred_element_type=jnp.float32) * scale_factor
    sp = jnp.where(pre_ok, sp, neg_big)
    sr = jnp.where(causal, sr, neg_big)
    peak = jnp.maximum(jnp.max(sp, axis=-1, keepdims=True), jnp.max(sr, axis=-1, keepdims=True))
    ep = jnp.exp(sp - peak)
    er = jnp.exp(sr - peak)
    inv = 1.0 / (jnp.sum(ep, axis=-1, keepdims=True) + jnp.sum(er, axis=-1, keepdims=True))
    wp = ep * inv
    wr = er * inv
    pp = wp.astype(jnp.bfloat16)
    pr = wr.astype(jnp.bfloat16)
    att = jnp.dot(pp, vp, preferred_element_type=jnp.float32) + jnp.dot(pr, vr, preferred_element_type=jnp.float32)
    att = att.astype(jnp.bfloat16).astype(jnp.float32)
    delta = jnp.sum(do2.astype(jnp.float32) * att, axis=-1, keepdims=True)
    dpp = lax.dot_general(do2, vp, NT, preferred_element_type=jnp.float32)
    dpr = lax.dot_general(do2, vr, NT, preferred_element_type=jnp.float32)
    dsp = (wp * (dpp - delta)).astype(jnp.bfloat16)
    dsr = (wr * (dpr - delta)).astype(jnp.bfloat16)
    dq = (jnp.dot(dsp, kp, preferred_element_type=jnp.float32) + jnp.dot(
        dsr, kr, preferred_element_type=jnp.float32)) * scale_factor
    dq = dq.astype(dq_ref.dtype)
    for j, cols in enumerate(heads):
        dq_ref[:, cols] = dq[j * resp_rows:(j + 1) * resp_rows]
    dkp = lax.dot_general(dsp, q2, TN, preferred_element_type=jnp.float32)
    dkr = lax.dot_general(dsr, q2, TN, preferred_element_type=jnp.float32)
    dvp = lax.dot_general(pp, do2, TN, preferred_element_type=jnp.float32)
    dvr = lax.dot_general(pr, do2, TN, preferred_element_type=jnp.float32)
    dkr_ref[...] = (dkr * scale_factor).astype(dkr_ref.dtype)
    dvr_ref[...] = dvr.astype(dvr_ref.dtype)
    dkp = (dkp * scale_factor).astype(jnp.bfloat16)
    dvp = dvp.astype(jnp.bfloat16)
    for ref, ranges in zip(piece_refs, out_ranges):
        at = 0
        for start, rows in ranges:
            ref[0, at:at + rows] = dkp[start:start + rows]
            ref[1, at:at + rows] = dvp[start:start + rows]
            at += rows


def attention_grads(blocks, length, place, q, do, pieces, xor_slots, out_ranges, kr, vr, first_head, earlier):
    resp_rows, q_width = q.shape
    n_pair, _, _, chunk_feats = pieces[0].shape
    kv_width = kr.shape[1]
    pre_rows = sum(p.shape[2] for p in pieces)
    chunk_heads = kv_width // n_pair // HEAD_DIM
    per_chunk = chunk_feats // HEAD_DIM
    heads = n_pair * per_chunk
    n_slots = lax.axis_size("ctx")
    slot_rows = pre_rows // n_slots

    def head(g, r):
        return ((r[0] + n_pair - g // per_chunk) % n_pair) * chunk_heads + first_head + g % per_chunk

    def piece_spec(rows, kv):
        return pl.BlockSpec((None, None, rows, HEAD_DIM), lambda g, b, n, r: (g // per_chunk, kv, 0, g % per_chunk))

    qspec = pl.BlockSpec((resp_rows, GROUP * HEAD_DIM), lambda g, b, n, r: (0, head(g, r)))
    rspec = pl.BlockSpec((resp_rows, HEAD_DIM), lambda g, b, n, r: (0, head(g, r)))
    in_specs = [qspec, qspec]
    in_specs += [piece_spec(p.shape[2], 0) for p in pieces] + [piece_spec(p.shape[2], 1) for p in pieces]
    in_specs += [rspec, rspec]
    operands = [blocks, length, place, q, do] + list(pieces) + list(pieces) + [kr, vr]
    aliases = {}
    if earlier is not None:
        in_specs += [pl.BlockSpec(memory_space=pl.ANY)] * 3
        aliases = {len(operands) + i: i for i in range(3)}
        operands += list(earlier)
    out_rows = [sum(rows for _, rows in ranges) for ranges in out_ranges]
    out_specs = [qspec, rspec, rspec] + [
        pl.BlockSpec((None, 2, rows, HEAD_DIM), lambda g, b, n, r: (g // per_chunk, 0, 0, g % per_chunk))
        for rows in out_rows]
    out_shape = [
        jax.ShapeDtypeStruct((resp_rows, q_width), jnp.bfloat16),
        jax.ShapeDtypeStruct((resp_rows, kv_width), jnp.bfloat16),
        jax.ShapeDtypeStruct((resp_rows, kv_width), jnp.bfloat16),
    ] + [jax.ShapeDtypeStruct((n_pair, 2, rows, chunk_feats), jnp.bfloat16) for rows in out_rows]
    layout = (len(pieces), n_slots, slot_rows, xor_slots, tuple(tuple(r) for r in out_ranges), earlier is not None)
    flops = 2 * 6 * resp_rows * GROUP * heads * (pre_rows + resp_rows) * HEAD_DIM
    return pl.pallas_call(
        functools.partial(attention_grad_kernel, layout),
        out_shape=tuple(out_shape),
        grid_spec=pltpu.PrefetchScalarGridSpec(
            num_scalar_prefetch=3,
            grid=(heads,),
            in_specs=in_specs,
            out_specs=out_specs,
        ),
        input_output_aliases=aliases,
        cost_estimate=pl.CostEstimate(
            flops=flops,
            transcendentals=resp_rows * GROUP * heads * (pre_rows + resp_rows),
            bytes_accessed=2 * heads * HEAD_DIM * (4 * resp_rows * GROUP + 4 * pre_rows + 4 * resp_rows),
        ),
    )(*operands)


def ring_shift(x, axis, n, d):
    return lax.ppermute(x, axis, [(i, (i + d) % n) for i in range(n)])


def pair_gather(planes, pair_prompt):
    n = lax.axis_size("pair")
    r = lax.axis_index("pair")
    held = [lax.dynamic_index_in_dim(planes, pair_prompt[r], 0, keepdims=False)]
    for d in range(1, n):
        chunk = lax.dynamic_index_in_dim(planes, pair_prompt[(r + d) % n], 0, keepdims=False)
        held.append(ring_shift(chunk, "pair", n, d))
    return jnp.stack(held)


def tree_ctx():
    return lax.axis_size("ctx") == 4


def ctx_gather(x):
    n = lax.axis_size("ctx")
    if not tree_ctx():
        got = lax.all_gather(x, "ctx", axis=0, tiled=False)
        return [got[j] for j in range(n)]
    return [x] + [lax.ppermute(x, "ctx", [(i, i ^ j) for i in range(n)]) for j in range(1, n)]


def ctx_out_ranges(slot_rows):
    n = lax.axis_size("ctx")
    return [[(j * slot_rows, slot_rows)] for j in range(n)]


def ctx_reduce(pieces):
    n = lax.axis_size("ctx")
    if not tree_ctx():
        got = lax.all_to_all(jnp.stack(pieces), "ctx", split_axis=0, concat_axis=0, tiled=True)
        return jnp.sum(got.astype(jnp.float32), axis=0).astype(jnp.bfloat16)
    got = [pieces[0]] + [lax.ppermute(pieces[j], "ctx", [(i, i ^ j) for i in range(n)]) for j in range(1, n)]
    total = (got[0].astype(jnp.float32) + got[1].astype(jnp.float32)) + (
        got[2].astype(jnp.float32) + got[3].astype(jnp.float32))
    return total.astype(jnp.bfloat16)


def pair_reduce(totals, pair_prompt, n_prompts):
    n = lax.axis_size("pair")
    r = lax.axis_index("pair")
    out = None
    for d in range(n):
        chunk = totals[(n - d) % n]
        got = chunk if d == 0 else ring_shift(chunk, "pair", n, d)
        source = (r - d) % n
        hits = (pair_prompt[source] == jnp.arange(n_prompts, dtype=jnp.int32)).astype(jnp.float32)
        term = hits[:, None, None, None] * jnp.transpose(got.astype(jnp.float32), (1, 0, 2))[None]
        out = term if out is None else out + term
    return out


def in_group(width, kv_heads, chunk_heads, group_heads, k):
    head = jnp.arange(width) // (width // kv_heads)
    return ((head % chunk_heads) // group_heads == k)[None]


def shards(
    queries, resp_keys, resp_values, d_out, prefix_kv, prefix_blocks, resp_lengths, pair_prompt
):
    n_prompts = prefix_kv.shape[0]
    planes = jnp.transpose(prefix_kv, (0, 2, 1, 3))
    slot_rows = planes.shape[2]
    chunk_feats = planes.shape[-1]
    n_groups = HEAD_GROUPS if chunk_feats % (HEAD_GROUPS * HEAD_DIM) == 0 else 1
    group_feats = chunk_feats // n_groups
    place = jnp.stack([lax.axis_index("pair"), lax.axis_index("ctx")]).astype(jnp.int32)
    kv_heads = resp_keys.shape[-1] // HEAD_DIM
    chunk_heads = chunk_feats // HEAD_DIM
    group_heads = group_feats // HEAD_DIM
    earlier = None
    parts = []
    for k in range(n_groups):
        cols = slice(k * group_feats, (k + 1) * group_feats)
        pieces = ctx_gather(pair_gather(planes[..., cols], pair_prompt))
        outs = attention_grads(
            prefix_blocks[0, 0], resp_lengths[0, 0].reshape(1), place, queries[0, 0], d_out[0, 0], pieces,
            tree_ctx(), ctx_out_ranges(slot_rows), resp_keys[0, 0], resp_values[0, 0],
            k * (group_feats // HEAD_DIM), None)
        if earlier is None:
            earlier = outs[:3]
        else:
            earlier = tuple(jnp.where(in_group(o.shape[1], kv_heads, chunk_heads, group_heads, k), o, e)
                            for o, e in zip(outs[:3], earlier))
        parts.append(pair_reduce(ctx_reduce(list(outs[3:])), pair_prompt, n_prompts))
    dq, dkr, dvr = earlier
    d_prefix = parts[0] if n_groups == 1 else jnp.concatenate(parts, -1)
    return (dq[None, None], dkr[None, None], dvr[None, None], d_prefix)


def solution(mesh):
    placed = (
        P(("dp", "ctx"), "pair", None, None),
        P(("dp", "ctx"), "pair", None, None),
        P(("dp", "ctx"), "pair", None, None),
        P(("dp", "ctx"), "pair", None, None),
        P("dp", "ctx", None, "pair"),
        P(("dp", "ctx"), "pair", None),
        P(("dp", "ctx"), "pair"),
        P("dp"),
    )
    return jax.shard_map(
        shards,
        mesh=mesh,
        in_specs=placed,
        out_specs=(
            P(("dp", "ctx"), "pair", None, None),
            P(("dp", "ctx"), "pair", None, None),
            P(("dp", "ctx"), "pair", None, None),
            P("dp", "ctx", None, "pair"),
        ),
        check_vma=False,
    )
```

```python
import functools

import jax
import jax.numpy as jnp
from jax import lax
from jax.experimental import pallas as pl
from jax.experimental.pallas import tpu as pltpu
from jax.sharding import PartitionSpec as P

KV_HEADS = 8
GROUP = 2
HEAD_DIM = 128
BLOCK = 128
HEAD_GROUPS = 2


scale_factor = 144.0 ** (-0.5)
neg_big = -1e30

NT = (((1,), (1,)), ((), ()))
TN = (((0,), (0,)), ((), ()))


def attention_grad_kernel(layout, blocks_ref, length_ref, place_ref, q_ref, do_ref, *refs):
    n_in, n_slots, slot_rows, xor_slots, out_ranges, aliased = layout
    kp_refs, vp_refs = refs[:n_in], refs[n_in:2 * n_in]
    kr_ref, vr_ref = refs[2 * n_in:2 * n_in + 2]
    outs = refs[2 * n_in + 2 + (3 if aliased else 0):]
    dq_ref, dkr_ref, dvr_ref = outs[:3]
    piece_refs = outs[3:]
    resp_rows = q_ref.shape[0]
    kp = jnp.concatenate([r[...] for r in kp_refs], 0)
    vp = jnp.concatenate([r[...] for r in vp_refs], 0)
    pre_rows = kp.shape[0]
    kr = kr_ref[...]
    vr = vr_ref[...]

    slot_blocks = slot_rows // BLOCK
    c = place_ref[1]
    col_block = lax.broadcasted_iota(jnp.int32, (1, pre_rows), 1) // BLOCK
    flag = jnp.zeros((1, pre_rows), jnp.int32)
    for b in range(n_slots * slot_blocks):
        slot, sub = b // slot_blocks, b % slot_blocks
        source = jnp.bitwise_xor(c, slot) if xor_slots else slot
        flag = jnp.where(col_block == b, blocks_ref[source * slot_blocks + sub], flag)
    pre_ok = flag > 0
    rows = GROUP * resp_rows
    row_i = lax.broadcasted_iota(jnp.int32, (rows, resp_rows), 0) % resp_rows
    col_i = lax.broadcasted_iota(jnp.int32, (rows, resp_rows), 1)
    causal = row_i >= col_i
    live = lax.broadcasted_iota(jnp.int32, (rows, 1), 0) % resp_rows < length_ref[0]
    heads = [slice(j * HEAD_DIM, (j + 1) * HEAD_DIM) for j in range(GROUP)]
    q2 = jnp.concatenate([q_ref[:, cols] for cols in heads], 0)
    do2 = jnp.concatenate([do_ref[:, cols] for cols in heads], 0)
    do2 = jnp.where(live, do2, jnp.zeros_like(do2))

    sp = lax.dot_general(q2, kp, NT, preferred_element_type=jnp.float32) * scale_factor
    sr = lax.dot_general(q2, kr, NT, preferred_element_type=jnp.float32) * scale_factor
    sp = jnp.where(pre_ok, sp, neg_big)
    sr = jnp.where(causal, sr, neg_big)
    peak = jnp.maximum(jnp.max(sp, axis=-1, keepdims=True), jnp.max(sr, axis=-1, keepdims=True))
    ep = jnp.exp(sp - peak)
    er = jnp.exp(sr - peak)
    inv = 1.0 / (jnp.sum(ep, axis=-1, keepdims=True) + jnp.sum(er, axis=-1, keepdims=True))
    wp = ep * inv
    wr = er * inv
    pp = wp.astype(jnp.bfloat16)
    pr = wr.astype(jnp.bfloat16)
    att = jnp.dot(pp, vp, preferred_element_type=jnp.float32) + jnp.dot(pr, vr, preferred_element_type=jnp.float32)
    att = att.astype(jnp.bfloat16).astype(jnp.float32)
    delta = jnp.sum(do2.astype(jnp.float32) * att, axis=-1, keepdims=True)
    dpp = lax.dot_general(do2, vp, NT, preferred_element_type=jnp.float32)
    dpr = lax.dot_general(do2, vr, NT, preferred_element_type=jnp.float32)
    dsp = (wp * (dpp - delta)).astype(jnp.bfloat16)
    dsr = (wr * (dpr - delta)).astype(jnp.bfloat16)
    dq = (jnp.dot(dsp, kp, preferred_element_type=jnp.float32) + jnp.dot(
        dsr, kr, preferred_element_type=jnp.float32)) * scale_factor
    dq = dq.astype(dq_ref.dtype)
    for j, cols in enumerate(heads):
        dq_ref[:, cols] = dq[j * resp_rows:(j + 1) * resp_rows]
    dkp = lax.dot_general(dsp, q2, TN, preferred_element_type=jnp.float32)
    dkr = lax.dot_general(dsr, q2, TN, preferred_element_type=jnp.float32)
    dvp = lax.dot_general(pp, do2, TN, preferred_element_type=jnp.float32)
    dvr = lax.dot_general(pr, do2, TN, preferred_element_type=jnp.float32)
    dkr_ref[...] = (dkr * scale_factor).astype(dkr_ref.dtype)
    dvr_ref[...] = dvr.astype(dvr_ref.dtype)
    dkp = (dkp * scale_factor).astype(jnp.bfloat16)
    dvp = dvp.astype(jnp.bfloat16)
    for ref, ranges in zip(piece_refs, out_ranges):
        at = 0
        for start, rows in ranges:
            ref[0, at:at + rows] = dkp[start:start + rows]
            ref[1, at:at + rows] = dvp[start:start + rows]
            at += rows


def attention_grads(blocks, length, place, q, do, pieces, xor_slots, out_ranges, kr, vr, first_head, earlier):
    resp_rows, q_width = q.shape
    n_pair, _, _, chunk_feats = pieces[0].shape
    kv_width = kr.shape[1]
    pre_rows = sum(p.shape[2] for p in pieces)
    chunk_heads = kv_width // n_pair // HEAD_DIM
    per_chunk = chunk_feats // HEAD_DIM
    heads = n_pair * per_chunk
    n_slots = lax.axis_size("ctx")
    slot_rows = pre_rows // n_slots

    def head(g, r):
        return ((r[0] + n_pair - g // per_chunk) % n_pair) * chunk_heads + first_head + g % per_chunk

    def piece_spec(rows, kv):
        return pl.BlockSpec((None, None, rows, HEAD_DIM), lambda g, b, n, r: (g // per_chunk, kv, 0, g % per_chunk))

    qspec = pl.BlockSpec((resp_rows, GROUP * HEAD_DIM), lambda g, b, n, r: (0, head(g, r)))
    rspec = pl.BlockSpec((resp_rows, HEAD_DIM), lambda g, b, n, r: (0, head(g, r)))
    in_specs = [qspec, qspec]
    in_specs += [piece_spec(p.shape[2], 0) for p in pieces] + [piece_spec(p.shape[2], 1) for p in pieces]
    in_specs += [rspec, rspec]
    operands = [blocks, length, place, q, do] + list(pieces) + list(pieces) + [kr, vr]
    aliases = {}
    if earlier is not None:
        in_specs += [pl.BlockSpec(memory_space=pl.ANY)] * 3
        aliases = {len(operands) + i: i for i in range(3)}
        operands += list(earlier)
    out_rows = [sum(rows for _, rows in ranges) for ranges in out_ranges]
    out_specs = [qspec, rspec, rspec] + [
        pl.BlockSpec((None, 2, rows, HEAD_DIM), lambda g, b, n, r: (g // per_chunk, 0, 0, g % per_chunk))
        for rows in out_rows]
    out_shape = [
        jax.ShapeDtypeStruct((resp_rows, q_width), jnp.bfloat16),
        jax.ShapeDtypeStruct((resp_rows, kv_width), jnp.bfloat16),
        jax.ShapeDtypeStruct((resp_rows, kv_width), jnp.bfloat16),
    ] + [jax.ShapeDtypeStruct((n_pair, 2, rows, chunk_feats), jnp.bfloat16) for rows in out_rows]
    layout = (len(pieces), n_slots, slot_rows, xor_slots, tuple(tuple(r) for r in out_ranges), earlier is not None)
    flops = 2 * 6 * resp_rows * GROUP * heads * (pre_rows + resp_rows) * HEAD_DIM
    return pl.pallas_call(
        functools.partial(attention_grad_kernel, layout),
        out_shape=tuple(out_shape),
        grid_spec=pltpu.PrefetchScalarGridSpec(
            num_scalar_prefetch=3,
            grid=(heads,),
            in_specs=in_specs,
            out_specs=out_specs,
        ),
        input_output_aliases=aliases,
        cost_estimate=pl.CostEstimate(
            flops=flops,
            transcendentals=resp_rows * GROUP * heads * (pre_rows + resp_rows),
            bytes_accessed=2 * heads * HEAD_DIM * (4 * resp_rows * GROUP + 4 * pre_rows + 4 * resp_rows),
        ),
    )(*operands)


def ring_shift(x, axis, n, d):
    return lax.ppermute(x, axis, [(i, (i + d) % n) for i in range(n)])


def pair_gather(planes, pair_prompt):
    n = lax.axis_size("pair")
    r = lax.axis_index("pair")
    held = [lax.dynamic_index_in_dim(planes, pair_prompt[r], 0, keepdims=False)]
    for d in range(1, n):
        chunk = lax.dynamic_index_in_dim(planes, pair_prompt[(r + d) % n], 0, keepdims=False)
        held.append(ring_shift(chunk, "pair", n, d))
    return jnp.stack(held)


def tree_ctx():
    return lax.axis_size("ctx") == 4


def ctx_gather(x):
    n = lax.axis_size("ctx")
    if not tree_ctx():
        got = lax.all_gather(x, "ctx", axis=0, tiled=False)
        return [got[j] for j in range(n)]
    along_x = [(i, i ^ 1) for i in range(n)]
    along_y = [(i, i ^ 2) for i in range(n)]
    from_x = lax.ppermute(x, "ctx", along_x)
    from_y = lax.ppermute(x, "ctx", along_y)
    half = x.shape[2] // 2
    far_a = lax.ppermute(from_y[:, :, :half], "ctx", along_x)
    far_b = lax.ppermute(from_x[:, :, half:], "ctx", along_y)
    return [x, from_x, from_y, far_a, far_b]


def ctx_out_ranges(slot_rows):
    n = lax.axis_size("ctx")
    if not tree_ctx():
        return [[(j * slot_rows, slot_rows)] for j in range(n)]
    half = slot_rows // 2
    return [[(0, slot_rows)],
            [(slot_rows, slot_rows), (3 * slot_rows, half)],
            [(2 * slot_rows, slot_rows), (3 * slot_rows + half, half)]]


def ctx_reduce(pieces):
    if not tree_ctx():
        got = lax.all_to_all(jnp.stack(pieces), "ctx", split_axis=0, concat_axis=0, tiled=True)
        return jnp.sum(got.astype(jnp.float32), axis=0).astype(jnp.bfloat16)
    n = lax.axis_size("ctx")
    along_x = [(i, i ^ 1) for i in range(n)]
    along_y = [(i, i ^ 2) for i in range(n)]
    mine, send_x, send_y = pieces
    rows = mine.shape[2]
    got_x = lax.ppermute(send_x, "ctx", along_x)
    got_y = lax.ppermute(send_y, "ctx", along_y)
    far_a = lax.ppermute(got_x[:, :, rows:], "ctx", along_y)
    far_b = lax.ppermute(got_y[:, :, rows:], "ctx", along_x)
    far = jnp.concatenate([far_a, far_b], 2)
    total = (mine.astype(jnp.float32) + got_x[:, :, :rows].astype(jnp.float32)) + (
        got_y[:, :, :rows].astype(jnp.float32) + far.astype(jnp.float32))
    return total.astype(jnp.bfloat16)


def pair_reduce(totals, pair_prompt, n_prompts):
    n = lax.axis_size("pair")
    r = lax.axis_index("pair")
    out = None
    for d in range(n):
        chunk = totals[(n - d) % n]
        got = chunk if d == 0 else ring_shift(chunk, "pair", n, d)
        source = (r - d) % n
        hits = (pair_prompt[source] == jnp.arange(n_prompts, dtype=jnp.int32)).astype(jnp.float32)
        term = hits[:, None, None, None] * jnp.transpose(got.astype(jnp.float32), (1, 0, 2))[None]
        out = term if out is None else out + term
    return out


def in_group(width, kv_heads, chunk_heads, group_heads, k):
    head = jnp.arange(width) // (width // kv_heads)
    return ((head % chunk_heads) // group_heads == k)[None]


def shards(
    queries, resp_keys, resp_values, d_out, prefix_kv, prefix_blocks, resp_lengths, pair_prompt
):
    n_prompts = prefix_kv.shape[0]
    planes = jnp.transpose(prefix_kv, (0, 2, 1, 3))
    slot_rows = planes.shape[2]
    chunk_feats = planes.shape[-1]
    n_groups = HEAD_GROUPS if chunk_feats % (HEAD_GROUPS * HEAD_DIM) == 0 else 1
    group_feats = chunk_feats // n_groups
    place = jnp.stack([lax.axis_index("pair"), lax.axis_index("ctx")]).astype(jnp.int32)
    kv_heads = resp_keys.shape[-1] // HEAD_DIM
    chunk_heads = chunk_feats // HEAD_DIM
    group_heads = group_feats // HEAD_DIM
    earlier = None
    parts = []
    gathered = pair_gather(planes, pair_prompt)
    for k in range(n_groups):
        cols = slice(k * group_feats, (k + 1) * group_feats)
        pieces = ctx_gather(gathered[..., cols])
        outs = attention_grads(
            prefix_blocks[0, 0], resp_lengths[0, 0].reshape(1), place, queries[0, 0], d_out[0, 0], pieces,
            tree_ctx(), ctx_out_ranges(slot_rows), resp_keys[0, 0], resp_values[0, 0],
            k * (group_feats // HEAD_DIM), None)
        if earlier is None:
            earlier = outs[:3]
        else:
            earlier = tuple(jnp.where(in_group(o.shape[1], kv_heads, chunk_heads, group_heads, k), o, e)
                            for o, e in zip(outs[:3], earlier))
        parts.append(pair_reduce(ctx_reduce(list(outs[3:])), pair_prompt, n_prompts))
    dq, dkr, dvr = earlier
    d_prefix = parts[0] if n_groups == 1 else jnp.concatenate(parts, -1)
    return (dq[None, None], dkr[None, None], dvr[None, None], d_prefix)


def solution(mesh):
    placed = (
        P(("dp", "ctx"), "pair", None, None),
        P(("dp", "ctx"), "pair", None, None),
        P(("dp", "ctx"), "pair", None, None),
        P(("dp", "ctx"), "pair", None, None),
        P("dp", "ctx", None, "pair"),
        P(("dp", "ctx"), "pair", None),
        P(("dp", "ctx"), "pair"),
        P("dp"),
    )
    return jax.shard_map(
        shards,
        mesh=mesh,
        in_specs=placed,
        out_specs=(
            P(("dp", "ctx"), "pair", None, None),
            P(("dp", "ctx"), "pair", None, None),
            P(("dp", "ctx"), "pair", None, None),
            P("dp", "ctx", None, "pair"),
        ),
        check_vma=False,
    )
```

```python
import functools

import jax
import jax.numpy as jnp
from jax import lax
from jax.experimental import pallas as pl
from jax.experimental.pallas import tpu as pltpu
from jax.sharding import PartitionSpec as P

KV_HEADS = 8
GROUP = 2
HEAD_DIM = 128
BLOCK = 128
HEAD_GROUPS = 2


scale_factor = 144.0 ** (-0.5)
neg_big = -1e30

NT = (((1,), (1,)), ((), ()))
TN = (((0,), (0,)), ((), ()))


def attention_grad_kernel(layout, blocks_ref, length_ref, place_ref, q_ref, do_ref, *refs):
    n_in, n_slots, slot_rows, xor_slots, out_ranges, aliased = layout
    kp_refs, vp_refs = refs[:n_in], refs[n_in:2 * n_in]
    kr_ref, vr_ref = refs[2 * n_in:2 * n_in + 2]
    outs = refs[2 * n_in + 2 + (3 if aliased else 0):]
    dq_ref, dkr_ref, dvr_ref = outs[:3]
    piece_refs = outs[3:]
    resp_rows = q_ref.shape[0]
    kp = jnp.concatenate([r[...] for r in kp_refs], 0)
    vp = jnp.concatenate([r[...] for r in vp_refs], 0)
    pre_rows = kp.shape[0]
    kr = kr_ref[...]
    vr = vr_ref[...]

    slot_blocks = slot_rows // BLOCK
    c = place_ref[1]
    col_block = lax.broadcasted_iota(jnp.int32, (1, pre_rows), 1) // BLOCK
    flag = jnp.zeros((1, pre_rows), jnp.int32)
    for b in range(n_slots * slot_blocks):
        slot, sub = b // slot_blocks, b % slot_blocks
        source = jnp.bitwise_xor(c, slot) if xor_slots else slot
        flag = jnp.where(col_block == b, blocks_ref[source * slot_blocks + sub], flag)
    pre_ok = flag > 0
    rows = GROUP * resp_rows
    row_i = lax.broadcasted_iota(jnp.int32, (rows, resp_rows), 0) % resp_rows
    col_i = lax.broadcasted_iota(jnp.int32, (rows, resp_rows), 1)
    causal = row_i >= col_i
    live = lax.broadcasted_iota(jnp.int32, (rows, 1), 0) % resp_rows < length_ref[0]
    heads = [slice(j * HEAD_DIM, (j + 1) * HEAD_DIM) for j in range(GROUP)]
    q2 = jnp.concatenate([q_ref[:, cols] for cols in heads], 0)
    do2 = jnp.concatenate([do_ref[:, cols] for cols in heads], 0)
    do2 = jnp.where(live, do2, jnp.zeros_like(do2))

    sp = lax.dot_general(q2, kp, NT, preferred_element_type=jnp.float32) * scale_factor
    sr = lax.dot_general(q2, kr, NT, preferred_element_type=jnp.float32) * scale_factor
    sp = jnp.where(pre_ok, sp, neg_big)
    sr = jnp.where(causal, sr, neg_big)
    peak = jnp.maximum(jnp.max(sp, axis=-1, keepdims=True), jnp.max(sr, axis=-1, keepdims=True))
    ep = jnp.exp(sp - peak)
    er = jnp.exp(sr - peak)
    inv = 1.0 / (jnp.sum(ep, axis=-1, keepdims=True) + jnp.sum(er, axis=-1, keepdims=True))
    wp = ep * inv
    wr = er * inv
    pp = wp.astype(jnp.bfloat16)
    pr = wr.astype(jnp.bfloat16)
    att = jnp.dot(pp, vp, preferred_element_type=jnp.float32) + jnp.dot(pr, vr, preferred_element_type=jnp.float32)
    att = att.astype(jnp.bfloat16).astype(jnp.float32)
    delta = jnp.sum(do2.astype(jnp.float32) * att, axis=-1, keepdims=True)
    dpp = lax.dot_general(do2, vp, NT, preferred_element_type=jnp.float32)
    dpr = lax.dot_general(do2, vr, NT, preferred_element_type=jnp.float32)
    dsp = (wp * (dpp - delta)).astype(jnp.bfloat16)
    dsr = (wr * (dpr - delta)).astype(jnp.bfloat16)
    dq = (jnp.dot(dsp, kp, preferred_element_type=jnp.float32) + jnp.dot(
        dsr, kr, preferred_element_type=jnp.float32)) * scale_factor
    dq = dq.astype(dq_ref.dtype)
    for j, cols in enumerate(heads):
        dq_ref[:, cols] = dq[j * resp_rows:(j + 1) * resp_rows]
    dkp = lax.dot_general(dsp, q2, TN, preferred_element_type=jnp.float32)
    dkr = lax.dot_general(dsr, q2, TN, preferred_element_type=jnp.float32)
    dvp = lax.dot_general(pp, do2, TN, preferred_element_type=jnp.float32)
    dvr = lax.dot_general(pr, do2, TN, preferred_element_type=jnp.float32)
    dkr_ref[...] = (dkr * scale_factor).astype(dkr_ref.dtype)
    dvr_ref[...] = dvr.astype(dvr_ref.dtype)
    dkp = (dkp * scale_factor).astype(jnp.bfloat16)
    dvp = dvp.astype(jnp.bfloat16)
    for ref, ranges in zip(piece_refs, out_ranges):
        at = 0
        for start, rows in ranges:
            ref[0, at:at + rows] = dkp[start:start + rows]
            ref[1, at:at + rows] = dvp[start:start + rows]
            at += rows


def attention_grads(blocks, length, place, q, do, pieces, xor_slots, out_ranges, kr, vr, first_head, earlier):
    resp_rows, q_width = q.shape
    n_pair, _, _, chunk_feats = pieces[0].shape
    kv_width = kr.shape[1]
    pre_rows = sum(p.shape[2] for p in pieces)
    chunk_heads = kv_width // n_pair // HEAD_DIM
    per_chunk = chunk_feats // HEAD_DIM
    heads = n_pair * per_chunk
    n_slots = lax.axis_size("ctx")
    slot_rows = pre_rows // n_slots

    def head(g, r):
        return ((r[0] + n_pair - g // per_chunk) % n_pair) * chunk_heads + first_head + g % per_chunk

    def piece_spec(rows, kv):
        return pl.BlockSpec((None, None, rows, HEAD_DIM), lambda g, b, n, r: (g // per_chunk, kv, 0, g % per_chunk))

    qspec = pl.BlockSpec((resp_rows, GROUP * HEAD_DIM), lambda g, b, n, r: (0, head(g, r)))
    rspec = pl.BlockSpec((resp_rows, HEAD_DIM), lambda g, b, n, r: (0, head(g, r)))
    in_specs = [qspec, qspec]
    in_specs += [piece_spec(p.shape[2], 0) for p in pieces] + [piece_spec(p.shape[2], 1) for p in pieces]
    in_specs += [rspec, rspec]
    operands = [blocks, length, place, q, do] + list(pieces) + list(pieces) + [kr, vr]
    aliases = {}
    if earlier is not None:
        in_specs += [pl.BlockSpec(memory_space=pl.ANY)] * 3
        aliases = {len(operands) + i: i for i in range(3)}
        operands += list(earlier)
    out_rows = [sum(rows for _, rows in ranges) for ranges in out_ranges]
    out_specs = [qspec, rspec, rspec] + [
        pl.BlockSpec((None, 2, rows, HEAD_DIM), lambda g, b, n, r: (g // per_chunk, 0, 0, g % per_chunk))
        for rows in out_rows]
    out_shape = [
        jax.ShapeDtypeStruct((resp_rows, q_width), jnp.bfloat16),
        jax.ShapeDtypeStruct((resp_rows, kv_width), jnp.bfloat16),
        jax.ShapeDtypeStruct((resp_rows, kv_width), jnp.bfloat16),
    ] + [jax.ShapeDtypeStruct((n_pair, 2, rows, chunk_feats), jnp.bfloat16) for rows in out_rows]
    layout = (len(pieces), n_slots, slot_rows, xor_slots, tuple(tuple(r) for r in out_ranges), earlier is not None)
    flops = 2 * 6 * resp_rows * GROUP * heads * (pre_rows + resp_rows) * HEAD_DIM
    return pl.pallas_call(
        functools.partial(attention_grad_kernel, layout),
        out_shape=tuple(out_shape),
        grid_spec=pltpu.PrefetchScalarGridSpec(
            num_scalar_prefetch=3,
            grid=(heads,),
            in_specs=in_specs,
            out_specs=out_specs,
        ),
        input_output_aliases=aliases,
        cost_estimate=pl.CostEstimate(
            flops=flops,
            transcendentals=resp_rows * GROUP * heads * (pre_rows + resp_rows),
            bytes_accessed=2 * heads * HEAD_DIM * (4 * resp_rows * GROUP + 4 * pre_rows + 4 * resp_rows),
        ),
    )(*operands)


def ring_shift(x, axis, n, d):
    return lax.ppermute(x, axis, [(i, (i + d) % n) for i in range(n)])


def pair_gather(planes, pair_prompt):
    n = lax.axis_size("pair")
    r = lax.axis_index("pair")
    held = [lax.dynamic_index_in_dim(planes, pair_prompt[r], 0, keepdims=False)]
    for d in range(1, n):
        chunk = lax.dynamic_index_in_dim(planes, pair_prompt[(r + d) % n], 0, keepdims=False)
        held.append(ring_shift(chunk, "pair", n, d))
    return jnp.stack(held)


def tree_ctx():
    return lax.axis_size("ctx") == 4


def ctx_gather(x):
    n = lax.axis_size("ctx")
    if not tree_ctx():
        got = lax.all_gather(x, "ctx", axis=0, tiled=False)
        return [got[j] for j in range(n)]
    along_x = [(i, i ^ 1) for i in range(n)]
    along_y = [(i, i ^ 2) for i in range(n)]
    from_x = lax.ppermute(x, "ctx", along_x)
    from_y = lax.ppermute(x, "ctx", along_y)
    half = x.shape[2] // 2
    far_a = lax.ppermute(from_y[:, :, :half], "ctx", along_x)
    far_b = lax.ppermute(from_x[:, :, half:], "ctx", along_y)
    return [x, from_x, from_y, far_a, far_b]


def ctx_out_ranges(slot_rows):
    n = lax.axis_size("ctx")
    if not tree_ctx():
        return [[(j * slot_rows, slot_rows)] for j in range(n)]
    half = slot_rows // 2
    return [[(0, slot_rows)],
            [(slot_rows, slot_rows), (3 * slot_rows, half)],
            [(2 * slot_rows, slot_rows), (3 * slot_rows + half, half)]]


def ctx_reduce(pieces):
    if not tree_ctx():
        got = lax.all_to_all(jnp.stack(pieces), "ctx", split_axis=0, concat_axis=0, tiled=True)
        return jnp.sum(got.astype(jnp.float32), axis=0).astype(jnp.bfloat16)
    n = lax.axis_size("ctx")
    along_x = [(i, i ^ 1) for i in range(n)]
    along_y = [(i, i ^ 2) for i in range(n)]
    mine, send_x, send_y = pieces
    rows = mine.shape[2]
    got_x = lax.ppermute(send_x, "ctx", along_x)
    got_y = lax.ppermute(send_y, "ctx", along_y)
    far_a = lax.ppermute(got_x[:, :, rows:], "ctx", along_y)
    far_b = lax.ppermute(got_y[:, :, rows:], "ctx", along_x)
    far = jnp.concatenate([far_a, far_b], 2)
    total = (mine.astype(jnp.float32) + got_x[:, :, :rows].astype(jnp.float32)) + (
        got_y[:, :, :rows].astype(jnp.float32) + far.astype(jnp.float32))
    return total.astype(jnp.bfloat16)


def pair_exchange(totals):
    n = lax.axis_size("pair")
    return [totals[0]] + [ring_shift(totals[(n - d) % n], "pair", n, d) for d in range(1, n)]


def prompt_weights(pair_prompt, n_prompts):
    n = lax.axis_size("pair")
    r = lax.axis_index("pair")
    source = jnp.take(pair_prompt, (r - jnp.arange(n)) % n, mode="clip")
    return (source[:, None] == jnp.arange(n_prompts, dtype=jnp.int32)[None, :]).astype(jnp.float32)


def in_group(width, kv_heads, chunk_heads, group_heads, k):
    head = jnp.arange(width) // (width // kv_heads)
    return ((head % chunk_heads) // group_heads == k)[None]


def shards(
    queries, resp_keys, resp_values, d_out, prefix_kv, prefix_blocks, resp_lengths, pair_prompt
):
    n_prompts = prefix_kv.shape[0]
    planes = jnp.transpose(prefix_kv, (0, 2, 1, 3))
    slot_rows = planes.shape[2]
    chunk_feats = planes.shape[-1]
    n_groups = HEAD_GROUPS if chunk_feats % (HEAD_GROUPS * HEAD_DIM) == 0 else 1
    group_feats = chunk_feats // n_groups
    place = jnp.stack([lax.axis_index("pair"), lax.axis_index("ctx")]).astype(jnp.int32)
    kv_heads = resp_keys.shape[-1] // HEAD_DIM
    chunk_heads = chunk_feats // HEAD_DIM
    group_heads = group_feats // HEAD_DIM
    earlier = None
    parts = []
    for k in range(n_groups):
        cols = slice(k * group_feats, (k + 1) * group_feats)
        pieces = ctx_gather(pair_gather(planes[..., cols], pair_prompt))
        outs = attention_grads(
            prefix_blocks[0, 0], resp_lengths[0, 0].reshape(1), place, queries[0, 0], d_out[0, 0], pieces,
            tree_ctx(), ctx_out_ranges(slot_rows), resp_keys[0, 0], resp_values[0, 0],
            k * (group_feats // HEAD_DIM), None)
        if earlier is None:
            earlier = outs[:3]
        else:
            earlier = tuple(jnp.where(in_group(o.shape[1], kv_heads, chunk_heads, group_heads, k), o, e)
                            for o, e in zip(outs[:3], earlier))
        parts.append(pair_exchange(ctx_reduce(list(outs[3:]))))
    dq, dkr, dvr = earlier
    weights = prompt_weights(pair_prompt, n_prompts)
    d_prefix = jnp.concatenate([
        sum(weights[d][:, None, None, None] * jnp.transpose(got.astype(jnp.float32), (1, 0, 2))[None]
            for d, got in enumerate(part))
        for part in parts], -1)
    return (dq[None, None], dkr[None, None], dvr[None, None], d_prefix)


def solution(mesh):
    placed = (
        P(("dp", "ctx"), "pair", None, None),
        P(("dp", "ctx"), "pair", None, None),
        P(("dp", "ctx"), "pair", None, None),
        P(("dp", "ctx"), "pair", None, None),
        P("dp", "ctx", None, "pair"),
        P(("dp", "ctx"), "pair", None),
        P(("dp", "ctx"), "pair"),
        P("dp"),
    )
    return jax.shard_map(
        shards,
        mesh=mesh,
        in_specs=placed,
        out_specs=(
            P(("dp", "ctx"), "pair", None, None),
            P(("dp", "ctx"), "pair", None, None),
            P(("dp", "ctx"), "pair", None, None),
            P("dp", "ctx", None, "pair"),
        ),
        check_vma=False,
    )
```

```python
import functools

import jax
import jax.numpy as jnp
from jax import lax
from jax.experimental import pallas as pl
from jax.experimental.pallas import tpu as pltpu
from jax.sharding import PartitionSpec as P

KV_HEADS = 8
GROUP = 2
HEAD_DIM = 128
BLOCK = 128
HEAD_GROUPS = 2


scale_factor = 144.0 ** (-0.5)
neg_big = -1e30

NT = (((1,), (1,)), ((), ()))
TN = (((0,), (0,)), ((), ()))


def attention_grad_kernel(layout, blocks_ref, length_ref, place_ref, q_ref, do_ref, *refs):
    n_in, n_slots, slot_rows, xor_slots, out_ranges, aliased = layout
    kp_refs, vp_refs = refs[:n_in], refs[n_in:2 * n_in]
    kr_ref, vr_ref = refs[2 * n_in:2 * n_in + 2]
    outs = refs[2 * n_in + 2 + (3 if aliased else 0):]
    dq_ref, dkr_ref, dvr_ref = outs[:3]
    piece_refs = outs[3:]
    resp_rows = q_ref.shape[0]
    kp = jnp.concatenate([r[...] for r in kp_refs], 0)
    vp = jnp.concatenate([r[...] for r in vp_refs], 0)
    pre_rows = kp.shape[0]
    kr = kr_ref[...]
    vr = vr_ref[...]

    slot_blocks = slot_rows // BLOCK
    c = place_ref[1]
    col_block = lax.broadcasted_iota(jnp.int32, (1, pre_rows), 1) // BLOCK
    flag = jnp.zeros((1, pre_rows), jnp.int32)
    for b in range(n_slots * slot_blocks):
        slot, sub = b // slot_blocks, b % slot_blocks
        source = jnp.bitwise_xor(c, slot) if xor_slots else slot
        flag = jnp.where(col_block == b, blocks_ref[source * slot_blocks + sub], flag)
    pre_ok = flag > 0
    rows = GROUP * resp_rows
    row_i = lax.broadcasted_iota(jnp.int32, (rows, resp_rows), 0) % resp_rows
    col_i = lax.broadcasted_iota(jnp.int32, (rows, resp_rows), 1)
    causal = row_i >= col_i
    live = lax.broadcasted_iota(jnp.int32, (rows, 1), 0) % resp_rows < length_ref[0]
    heads = [slice(j * HEAD_DIM, (j + 1) * HEAD_DIM) for j in range(GROUP)]
    q2 = jnp.concatenate([q_ref[:, cols] for cols in heads], 0)
    do2 = jnp.concatenate([do_ref[:, cols] for cols in heads], 0)
    do2 = jnp.where(live, do2, jnp.zeros_like(do2))

    sp = lax.dot_general(q2, kp, NT, preferred_element_type=jnp.float32) * scale_factor
    sr = lax.dot_general(q2, kr, NT, preferred_element_type=jnp.float32) * scale_factor
    sp = jnp.where(pre_ok, sp, neg_big)
    sr = jnp.where(causal, sr, neg_big)
    peak = jnp.maximum(jnp.max(sp, axis=-1, keepdims=True), jnp.max(sr, axis=-1, keepdims=True))
    ep = jnp.exp(sp - peak)
    er = jnp.exp(sr - peak)
    inv = 1.0 / (jnp.sum(ep, axis=-1, keepdims=True) + jnp.sum(er, axis=-1, keepdims=True))
    wp = ep * inv
    wr = er * inv
    pp = wp.astype(jnp.bfloat16)
    pr = wr.astype(jnp.bfloat16)
    att = jnp.dot(pp, vp, preferred_element_type=jnp.float32) + jnp.dot(pr, vr, preferred_element_type=jnp.float32)
    att = att.astype(jnp.bfloat16).astype(jnp.float32)
    delta = jnp.sum(do2.astype(jnp.float32) * att, axis=-1, keepdims=True)
    dpp = lax.dot_general(do2, vp, NT, preferred_element_type=jnp.float32)
    dpr = lax.dot_general(do2, vr, NT, preferred_element_type=jnp.float32)
    dsp = (wp * (dpp - delta)).astype(jnp.bfloat16)
    dsr = (wr * (dpr - delta)).astype(jnp.bfloat16)
    dq = (jnp.dot(dsp, kp, preferred_element_type=jnp.float32) + jnp.dot(
        dsr, kr, preferred_element_type=jnp.float32)) * scale_factor
    dq = dq.astype(dq_ref.dtype)
    for j, cols in enumerate(heads):
        dq_ref[:, cols] = dq[j * resp_rows:(j + 1) * resp_rows]
    dkp = lax.dot_general(dsp, q2, TN, preferred_element_type=jnp.float32)
    dkr = lax.dot_general(dsr, q2, TN, preferred_element_type=jnp.float32)
    dvp = lax.dot_general(pp, do2, TN, preferred_element_type=jnp.float32)
    dvr = lax.dot_general(pr, do2, TN, preferred_element_type=jnp.float32)
    dkr_ref[...] = (dkr * scale_factor).astype(dkr_ref.dtype)
    dvr_ref[...] = dvr.astype(dvr_ref.dtype)
    dkp = (dkp * scale_factor).astype(jnp.bfloat16)
    dvp = dvp.astype(jnp.bfloat16)
    for ref, ranges in zip(piece_refs, out_ranges):
        at = 0
        for start, rows in ranges:
            ref[0, at:at + rows] = dkp[start:start + rows]
            ref[1, at:at + rows] = dvp[start:start + rows]
            at += rows


def attention_grads(blocks, length, place, q, do, pieces, xor_slots, out_ranges, kr, vr, first_head, earlier):
    resp_rows, q_width = q.shape
    n_pair, _, _, chunk_feats = pieces[0].shape
    kv_width = kr.shape[1]
    pre_rows = sum(p.shape[2] for p in pieces)
    chunk_heads = kv_width // n_pair // HEAD_DIM
    per_chunk = chunk_feats // HEAD_DIM
    heads = n_pair * per_chunk
    n_slots = lax.axis_size("ctx")
    slot_rows = pre_rows // n_slots

    def head(g, r):
        return ((r[0] + n_pair - g // per_chunk) % n_pair) * chunk_heads + first_head + g % per_chunk

    def piece_spec(rows, kv):
        return pl.BlockSpec((None, None, rows, HEAD_DIM), lambda g, b, n, r: (g // per_chunk, kv, 0, g % per_chunk))

    qspec = pl.BlockSpec((resp_rows, GROUP * HEAD_DIM), lambda g, b, n, r: (0, head(g, r)))
    rspec = pl.BlockSpec((resp_rows, HEAD_DIM), lambda g, b, n, r: (0, head(g, r)))
    in_specs = [qspec, qspec]
    in_specs += [piece_spec(p.shape[2], 0) for p in pieces] + [piece_spec(p.shape[2], 1) for p in pieces]
    in_specs += [rspec, rspec]
    operands = [blocks, length, place, q, do] + list(pieces) + list(pieces) + [kr, vr]
    aliases = {}
    if earlier is not None:
        in_specs += [pl.BlockSpec(memory_space=pl.ANY)] * 3
        aliases = {len(operands) + i: i for i in range(3)}
        operands += list(earlier)
    out_rows = [sum(rows for _, rows in ranges) for ranges in out_ranges]
    out_specs = [qspec, rspec, rspec] + [
        pl.BlockSpec((None, 2, rows, HEAD_DIM), lambda g, b, n, r: (g // per_chunk, 0, 0, g % per_chunk))
        for rows in out_rows]
    out_shape = [
        jax.ShapeDtypeStruct((resp_rows, q_width), jnp.bfloat16),
        jax.ShapeDtypeStruct((resp_rows, kv_width), jnp.bfloat16),
        jax.ShapeDtypeStruct((resp_rows, kv_width), jnp.bfloat16),
    ] + [jax.ShapeDtypeStruct((n_pair, 2, rows, chunk_feats), jnp.bfloat16) for rows in out_rows]
    layout = (len(pieces), n_slots, slot_rows, xor_slots, tuple(tuple(r) for r in out_ranges), earlier is not None)
    flops = 2 * 6 * resp_rows * GROUP * heads * (pre_rows + resp_rows) * HEAD_DIM
    return pl.pallas_call(
        functools.partial(attention_grad_kernel, layout),
        out_shape=tuple(out_shape),
        grid_spec=pltpu.PrefetchScalarGridSpec(
            num_scalar_prefetch=3,
            grid=(heads,),
            in_specs=in_specs,
            out_specs=out_specs,
        ),
        input_output_aliases=aliases,
        cost_estimate=pl.CostEstimate(
            flops=flops,
            transcendentals=resp_rows * GROUP * heads * (pre_rows + resp_rows),
            bytes_accessed=2 * heads * HEAD_DIM * (4 * resp_rows * GROUP + 4 * pre_rows + 4 * resp_rows),
        ),
    )(*operands)


def ring_shift(x, axis, n, d):
    return lax.ppermute(x, axis, [(i, (i + d) % n) for i in range(n)])


def pair_gather(planes, pair_prompt):
    n = lax.axis_size("pair")
    r = lax.axis_index("pair")
    held = [lax.dynamic_index_in_dim(planes, pair_prompt[r], 0, keepdims=False)]
    for d in range(1, n):
        chunk = lax.dynamic_index_in_dim(planes, pair_prompt[(r + d) % n], 0, keepdims=False)
        held.append(ring_shift(chunk, "pair", n, d))
    return jnp.stack(held)


def tree_ctx():
    return lax.axis_size("ctx") == 4


def ctx_gather(x):
    n = lax.axis_size("ctx")
    if not tree_ctx():
        got = lax.all_gather(x, "ctx", axis=0, tiled=False)
        return [got[j] for j in range(n)]
    along_x = [(i, i ^ 1) for i in range(n)]
    along_y = [(i, i ^ 2) for i in range(n)]
    from_x = lax.ppermute(x, "ctx", along_x)
    from_y = lax.ppermute(x, "ctx", along_y)
    half = x.shape[2] // 2
    far_a = lax.ppermute(from_y[:, :, :half], "ctx", along_x)
    far_b = lax.ppermute(from_x[:, :, half:], "ctx", along_y)
    return [x, from_x, from_y, far_a, far_b]


def ctx_out_ranges(slot_rows):
    n = lax.axis_size("ctx")
    return [[(j * slot_rows, slot_rows)] for j in range(n)]


def ctx_reduce(pieces):
    n = lax.axis_size("ctx")
    if not tree_ctx():
        got = lax.all_to_all(jnp.stack(pieces), "ctx", split_axis=0, concat_axis=0, tiled=True)
        return jnp.sum(got.astype(jnp.float32), axis=0).astype(jnp.bfloat16)
    got = [pieces[0]] + [lax.ppermute(pieces[j], "ctx", [(i, i ^ j) for i in range(n)]) for j in range(1, n)]
    total = (got[0].astype(jnp.float32) + got[1].astype(jnp.float32)) + (
        got[2].astype(jnp.float32) + got[3].astype(jnp.float32))
    return total.astype(jnp.bfloat16)


def pair_exchange(totals):
    n = lax.axis_size("pair")
    return [totals[0]] + [ring_shift(totals[(n - d) % n], "pair", n, d) for d in range(1, n)]


def prompt_weights(pair_prompt, n_prompts):
    n = lax.axis_size("pair")
    r = lax.axis_index("pair")
    source = jnp.take(pair_prompt, (r - jnp.arange(n)) % n, mode="clip")
    return (source[:, None] == jnp.arange(n_prompts, dtype=jnp.int32)[None, :]).astype(jnp.float32)


def in_group(width, kv_heads, chunk_heads, group_heads, k):
    head = jnp.arange(width) // (width // kv_heads)
    return ((head % chunk_heads) // group_heads == k)[None]


def shards(
    queries, resp_keys, resp_values, d_out, prefix_kv, prefix_blocks, resp_lengths, pair_prompt
):
    n_prompts = prefix_kv.shape[0]
    planes = jnp.transpose(prefix_kv, (0, 2, 1, 3))
    slot_rows = planes.shape[2]
    chunk_feats = planes.shape[-1]
    n_groups = HEAD_GROUPS if chunk_feats % (HEAD_GROUPS * HEAD_DIM) == 0 else 1
    group_feats = chunk_feats // n_groups
    place = jnp.stack([lax.axis_index("pair"), lax.axis_index("ctx")]).astype(jnp.int32)
    kv_heads = resp_keys.shape[-1] // HEAD_DIM
    chunk_heads = chunk_feats // HEAD_DIM
    group_heads = group_feats // HEAD_DIM
    earlier = None
    parts = []
    for k in range(n_groups):
        cols = slice(k * group_feats, (k + 1) * group_feats)
        pieces = ctx_gather(pair_gather(planes[..., cols], pair_prompt))
        outs = attention_grads(
            prefix_blocks[0, 0], resp_lengths[0, 0].reshape(1), place, queries[0, 0], d_out[0, 0], pieces,
            tree_ctx(), ctx_out_ranges(slot_rows), resp_keys[0, 0], resp_values[0, 0],
            k * (group_feats // HEAD_DIM), None)
        if earlier is None:
            earlier = outs[:3]
        else:
            earlier = tuple(jnp.where(in_group(o.shape[1], kv_heads, chunk_heads, group_heads, k), o, e)
                            for o, e in zip(outs[:3], earlier))
        parts.append(pair_exchange(ctx_reduce(list(outs[3:]))))
    dq, dkr, dvr = earlier
    weights = prompt_weights(pair_prompt, n_prompts)
    d_prefix = jnp.concatenate([
        sum(weights[d][:, None, None, None] * jnp.transpose(got.astype(jnp.float32), (1, 0, 2))[None]
            for d, got in enumerate(part))
        for part in parts], -1)
    return (dq[None, None], dkr[None, None], dvr[None, None], d_prefix)


def solution(mesh):
    placed = (
        P(("dp", "ctx"), "pair", None, None),
        P(("dp", "ctx"), "pair", None, None),
        P(("dp", "ctx"), "pair", None, None),
        P(("dp", "ctx"), "pair", None, None),
        P("dp", "ctx", None, "pair"),
        P(("dp", "ctx"), "pair", None),
        P(("dp", "ctx"), "pair"),
        P("dp"),
    )
    return jax.shard_map(
        shards,
        mesh=mesh,
        in_specs=placed,
        out_specs=(
            P(("dp", "ctx"), "pair", None, None),
            P(("dp", "ctx"), "pair", None, None),
            P(("dp", "ctx"), "pair", None, None),
            P("dp", "ctx", None, "pair"),
        ),
        check_vma=False,
    )
```

```python
import functools

import jax
import jax.numpy as jnp
from jax import lax
from jax.experimental import pallas as pl
from jax.experimental.pallas import tpu as pltpu
from jax.sharding import PartitionSpec as P

KV_HEADS = 8
GROUP = 2
HEAD_DIM = 128
BLOCK = 128
HEAD_GROUPS = 2


scale_factor = 144.0 ** (-0.5)
neg_big = -1e30

NT = (((1,), (1,)), ((), ()))
TN = (((0,), (0,)), ((), ()))


def attention_grad_kernel(layout, blocks_ref, length_ref, place_ref, q_ref, do_ref, *refs):
    n_in, n_slots, slot_rows, xor_slots, out_ranges, aliased = layout
    kp_refs, vp_refs = refs[:n_in], refs[n_in:2 * n_in]
    kr_ref, vr_ref = refs[2 * n_in:2 * n_in + 2]
    outs = refs[2 * n_in + 2 + (3 if aliased else 0):]
    dq_ref, dkr_ref, dvr_ref = outs[:3]
    piece_refs = outs[3:]
    resp_rows = q_ref.shape[0]
    kp = jnp.concatenate([r[...] for r in kp_refs], 0)
    vp = jnp.concatenate([r[...] for r in vp_refs], 0)
    pre_rows = kp.shape[0]
    kr = kr_ref[...]
    vr = vr_ref[...]

    slot_blocks = slot_rows // BLOCK
    c = place_ref[1]
    col_block = lax.broadcasted_iota(jnp.int32, (1, pre_rows), 1) // BLOCK
    flag = jnp.zeros((1, pre_rows), jnp.int32)
    for b in range(n_slots * slot_blocks):
        slot, sub = b // slot_blocks, b % slot_blocks
        source = jnp.bitwise_xor(c, slot) if xor_slots else slot
        flag = jnp.where(col_block == b, blocks_ref[source * slot_blocks + sub], flag)
    pre_ok = flag > 0
    rows = GROUP * resp_rows
    row_i = lax.broadcasted_iota(jnp.int32, (rows, resp_rows), 0) % resp_rows
    col_i = lax.broadcasted_iota(jnp.int32, (rows, resp_rows), 1)
    causal = row_i >= col_i
    live = lax.broadcasted_iota(jnp.int32, (rows, 1), 0) % resp_rows < length_ref[0]
    heads = [slice(j * HEAD_DIM, (j + 1) * HEAD_DIM) for j in range(GROUP)]
    q2 = jnp.concatenate([q_ref[:, cols] for cols in heads], 0)
    do2 = jnp.concatenate([do_ref[:, cols] for cols in heads], 0)
    do2 = jnp.where(live, do2, jnp.zeros_like(do2))

    sp = lax.dot_general(q2, kp, NT, preferred_element_type=jnp.float32) * scale_factor
    sr = lax.dot_general(q2, kr, NT, preferred_element_type=jnp.float32) * scale_factor
    sp = jnp.where(pre_ok, sp, neg_big)
    sr = jnp.where(causal, sr, neg_big)
    peak = jnp.maximum(jnp.max(sp, axis=-1, keepdims=True), jnp.max(sr, axis=-1, keepdims=True))
    ep = jnp.exp(sp - peak)
    er = jnp.exp(sr - peak)
    inv = 1.0 / (jnp.sum(ep, axis=-1, keepdims=True) + jnp.sum(er, axis=-1, keepdims=True))
    wp = ep * inv
    wr = er * inv
    pp = wp.astype(jnp.bfloat16)
    pr = wr.astype(jnp.bfloat16)
    att = jnp.dot(pp, vp, preferred_element_type=jnp.float32) + jnp.dot(pr, vr, preferred_element_type=jnp.float32)
    att = att.astype(jnp.bfloat16).astype(jnp.float32)
    delta = jnp.sum(do2.astype(jnp.float32) * att, axis=-1, keepdims=True)
    dpp = lax.dot_general(do2, vp, NT, preferred_element_type=jnp.float32)
    dpr = lax.dot_general(do2, vr, NT, preferred_element_type=jnp.float32)
    dsp = (wp * (dpp - delta)).astype(jnp.bfloat16)
    dsr = (wr * (dpr - delta)).astype(jnp.bfloat16)
    dq = (jnp.dot(dsp, kp, preferred_element_type=jnp.float32) + jnp.dot(
        dsr, kr, preferred_element_type=jnp.float32)) * scale_factor
    dq = dq.astype(dq_ref.dtype)
    for j, cols in enumerate(heads):
        dq_ref[:, cols] = dq[j * resp_rows:(j + 1) * resp_rows]
    dkp = lax.dot_general(dsp, q2, TN, preferred_element_type=jnp.float32)
    dkr = lax.dot_general(dsr, q2, TN, preferred_element_type=jnp.float32)
    dvp = lax.dot_general(pp, do2, TN, preferred_element_type=jnp.float32)
    dvr = lax.dot_general(pr, do2, TN, preferred_element_type=jnp.float32)
    dkr_ref[...] = (dkr * scale_factor).astype(dkr_ref.dtype)
    dvr_ref[...] = dvr.astype(dvr_ref.dtype)
    dkp = (dkp * scale_factor).astype(jnp.bfloat16)
    dvp = dvp.astype(jnp.bfloat16)
    for ref, ranges in zip(piece_refs, out_ranges):
        at = 0
        for start, rows in ranges:
            ref[0, at:at + rows] = dkp[start:start + rows]
            ref[1, at:at + rows] = dvp[start:start + rows]
            at += rows


def attention_grads(blocks, length, place, q, do, pieces, xor_slots, out_ranges, kr, vr, first_head, earlier):
    resp_rows, q_width = q.shape
    n_pair, _, _, chunk_feats = pieces[0].shape
    kv_width = kr.shape[1]
    pre_rows = sum(p.shape[2] for p in pieces)
    chunk_heads = kv_width // n_pair // HEAD_DIM
    per_chunk = chunk_feats // HEAD_DIM
    heads = n_pair * per_chunk
    n_slots = lax.axis_size("ctx")
    slot_rows = pre_rows // n_slots

    def head(g, r):
        return ((r[0] + n_pair - g // per_chunk) % n_pair) * chunk_heads + first_head + g % per_chunk

    def piece_spec(rows, kv):
        return pl.BlockSpec((None, None, rows, HEAD_DIM), lambda g, b, n, r: (g // per_chunk, kv, 0, g % per_chunk))

    qspec = pl.BlockSpec((resp_rows, GROUP * HEAD_DIM), lambda g, b, n, r: (0, head(g, r)))
    rspec = pl.BlockSpec((resp_rows, HEAD_DIM), lambda g, b, n, r: (0, head(g, r)))
    in_specs = [qspec, qspec]
    in_specs += [piece_spec(p.shape[2], 0) for p in pieces] + [piece_spec(p.shape[2], 1) for p in pieces]
    in_specs += [rspec, rspec]
    operands = [blocks, length, place, q, do] + list(pieces) + list(pieces) + [kr, vr]
    aliases = {}
    if earlier is not None:
        in_specs += [pl.BlockSpec(memory_space=pl.ANY)] * 3
        aliases = {len(operands) + i: i for i in range(3)}
        operands += list(earlier)
    out_rows = [sum(rows for _, rows in ranges) for ranges in out_ranges]
    out_specs = [qspec, rspec, rspec] + [
        pl.BlockSpec((None, 2, rows, HEAD_DIM), lambda g, b, n, r: (g // per_chunk, 0, 0, g % per_chunk))
        for rows in out_rows]
    out_shape = [
        jax.ShapeDtypeStruct((resp_rows, q_width), jnp.bfloat16),
        jax.ShapeDtypeStruct((resp_rows, kv_width), jnp.bfloat16),
        jax.ShapeDtypeStruct((resp_rows, kv_width), jnp.bfloat16),
    ] + [jax.ShapeDtypeStruct((n_pair, 2, rows, chunk_feats), jnp.bfloat16) for rows in out_rows]
    layout = (len(pieces), n_slots, slot_rows, xor_slots, tuple(tuple(r) for r in out_ranges), earlier is not None)
    flops = 2 * 6 * resp_rows * GROUP * heads * (pre_rows + resp_rows) * HEAD_DIM
    return pl.pallas_call(
        functools.partial(attention_grad_kernel, layout),
        out_shape=tuple(out_shape),
        grid_spec=pltpu.PrefetchScalarGridSpec(
            num_scalar_prefetch=3,
            grid=(heads,),
            in_specs=in_specs,
            out_specs=out_specs,
        ),
        input_output_aliases=aliases,
        cost_estimate=pl.CostEstimate(
            flops=flops,
            transcendentals=resp_rows * GROUP * heads * (pre_rows + resp_rows),
            bytes_accessed=2 * heads * HEAD_DIM * (4 * resp_rows * GROUP + 4 * pre_rows + 4 * resp_rows),
        ),
    )(*operands)


def copy_blocks_kernel(*refs):
    n = len(refs) // 3
    for src, dst in zip(refs[n:2 * n], refs[2 * n:]):
        dst[...] = src[...]


def merge_heads(earlier, later, n_heads, heads):
    resp_rows = earlier[0].shape[0]
    kv_heads = later[1].shape[1] // HEAD_DIM
    widths = [x.shape[1] // kv_heads for x in later]
    specs = [pl.BlockSpec((resp_rows, w), lambda g: (0, heads(g))) for w in widths]
    return pl.pallas_call(
        copy_blocks_kernel,
        out_shape=tuple(jax.ShapeDtypeStruct(x.shape, x.dtype) for x in earlier),
        grid=(n_heads,),
        in_specs=[pl.BlockSpec(memory_space=pl.ANY)] * len(earlier) + specs,
        out_specs=specs,
        input_output_aliases={i: i for i in range(len(earlier))},
    )(*earlier, *later)


def ring_shift(x, axis, n, d):
    return lax.ppermute(x, axis, [(i, (i + d) % n) for i in range(n)])


def pair_gather(planes, pair_prompt):
    n = lax.axis_size("pair")
    r = lax.axis_index("pair")
    held = [lax.dynamic_index_in_dim(planes, pair_prompt[r], 0, keepdims=False)]
    for d in range(1, n):
        chunk = lax.dynamic_index_in_dim(planes, pair_prompt[(r + d) % n], 0, keepdims=False)
        held.append(ring_shift(chunk, "pair", n, d))
    return jnp.stack(held)


def tree_ctx():
    return lax.axis_size("ctx") == 4


def ctx_gather(x):
    n = lax.axis_size("ctx")
    if not tree_ctx():
        got = lax.all_gather(x, "ctx", axis=0, tiled=False)
        return [got[j] for j in range(n)]
    along_x = [(i, i ^ 1) for i in range(n)]
    along_y = [(i, i ^ 2) for i in range(n)]
    from_x = lax.ppermute(x, "ctx", along_x)
    from_y = lax.ppermute(x, "ctx", along_y)
    half = x.shape[2] // 2
    far_a = lax.ppermute(from_y[:, :, :half], "ctx", along_x)
    far_b = lax.ppermute(from_x[:, :, half:], "ctx", along_y)
    return [x, from_x, from_y, far_a, far_b]


def ctx_out_ranges(slot_rows):
    n = lax.axis_size("ctx")
    return [[(j * slot_rows, slot_rows)] for j in range(n)]


def ctx_reduce(pieces):
    n = lax.axis_size("ctx")
    if not tree_ctx():
        got = lax.all_to_all(jnp.stack(pieces), "ctx", split_axis=0, concat_axis=0, tiled=True)
        return jnp.sum(got.astype(jnp.float32), axis=0).astype(jnp.bfloat16)
    got = [pieces[0]] + [lax.ppermute(pieces[j], "ctx", [(i, i ^ j) for i in range(n)]) for j in range(1, n)]
    total = (got[0].astype(jnp.float32) + got[1].astype(jnp.float32)) + (
        got[2].astype(jnp.float32) + got[3].astype(jnp.float32))
    return total.astype(jnp.bfloat16)


def pair_exchange(totals):
    n = lax.axis_size("pair")
    return [totals[0]] + [ring_shift(totals[(n - d) % n], "pair", n, d) for d in range(1, n)]


def prompt_weights(pair_prompt, n_prompts):
    n = lax.axis_size("pair")
    r = lax.axis_index("pair")
    source = jnp.take(pair_prompt, (r - jnp.arange(n)) % n, mode="clip")
    return (source[:, None] == jnp.arange(n_prompts, dtype=jnp.int32)[None, :]).astype(jnp.float32)


def group_head(chunk_heads, group_heads, k, g):
    return (g // group_heads) * chunk_heads + k * group_heads + g % group_heads


def shards(
    queries, resp_keys, resp_values, d_out, prefix_kv, prefix_blocks, resp_lengths, pair_prompt
):
    n_prompts = prefix_kv.shape[0]
    planes = jnp.transpose(prefix_kv, (0, 2, 1, 3))
    slot_rows = planes.shape[2]
    chunk_feats = planes.shape[-1]
    n_groups = HEAD_GROUPS if chunk_feats % (HEAD_GROUPS * HEAD_DIM) == 0 else 1
    group_feats = chunk_feats // n_groups
    place = jnp.stack([lax.axis_index("pair"), lax.axis_index("ctx")]).astype(jnp.int32)
    kv_heads = resp_keys.shape[-1] // HEAD_DIM
    chunk_heads = chunk_feats // HEAD_DIM
    group_heads = group_feats // HEAD_DIM
    earlier = None
    parts = []
    for k in range(n_groups):
        cols = slice(k * group_feats, (k + 1) * group_feats)
        pieces = ctx_gather(pair_gather(planes[..., cols], pair_prompt))
        outs = attention_grads(
            prefix_blocks[0, 0], resp_lengths[0, 0].reshape(1), place, queries[0, 0], d_out[0, 0], pieces,
            tree_ctx(), ctx_out_ranges(slot_rows), resp_keys[0, 0], resp_values[0, 0],
            k * (group_feats // HEAD_DIM), None)
        if earlier is None:
            earlier = outs[:3]
        else:
            earlier = merge_heads(
                earlier, outs[:3], kv_heads // chunk_heads * group_heads,
                functools.partial(group_head, chunk_heads, group_heads, k))
        parts.append(pair_exchange(ctx_reduce(list(outs[3:]))))
    dq, dkr, dvr = earlier
    weights = prompt_weights(pair_prompt, n_prompts)
    d_prefix = jnp.concatenate([
        sum(weights[d][:, None, None, None] * jnp.transpose(got.astype(jnp.float32), (1, 0, 2))[None]
            for d, got in enumerate(part))
        for part in parts], -1)
    return (dq[None, None], dkr[None, None], dvr[None, None], d_prefix)


def solution(mesh):
    placed = (
        P(("dp", "ctx"), "pair", None, None),
        P(("dp", "ctx"), "pair", None, None),
        P(("dp", "ctx"), "pair", None, None),
        P(("dp", "ctx"), "pair", None, None),
        P("dp", "ctx", None, "pair"),
        P(("dp", "ctx"), "pair", None),
        P(("dp", "ctx"), "pair"),
        P("dp"),
    )
    return jax.shard_map(
        shards,
        mesh=mesh,
        in_specs=placed,
        out_specs=(
            P(("dp", "ctx"), "pair", None, None),
            P(("dp", "ctx"), "pair", None, None),
            P(("dp", "ctx"), "pair", None, None),
            P("dp", "ctx", None, "pair"),
        ),
        check_vma=False,
    )
```

```python
import functools

import jax
import jax.numpy as jnp
from jax import lax
from jax.experimental import pallas as pl
from jax.experimental.pallas import tpu as pltpu
from jax.sharding import PartitionSpec as P

KV_HEADS = 8
GROUP = 2
HEAD_DIM = 128
BLOCK = 128
HEAD_GROUPS = 2


scale_factor = 144.0 ** (-0.5)
neg_big = -1e30

NT = (((1,), (1,)), ((), ()))
TN = (((0,), (0,)), ((), ()))


def attention_grad_kernel(layout, blocks_ref, length_ref, place_ref, q_ref, do_ref, *refs):
    n_in, n_slots, slot_rows, xor_slots, out_ranges, aliased = layout
    kp_refs, vp_refs = refs[:n_in], refs[n_in:2 * n_in]
    kr_ref, vr_ref = refs[2 * n_in:2 * n_in + 2]
    outs = refs[2 * n_in + 2 + (3 if aliased else 0):]
    dq_ref, dkr_ref, dvr_ref = outs[:3]
    piece_refs = outs[3:]
    resp_rows = q_ref.shape[0]
    kp = jnp.concatenate([r[...] for r in kp_refs], 0)
    vp = jnp.concatenate([r[...] for r in vp_refs], 0)
    pre_rows = kp.shape[0]
    kr = kr_ref[...]
    vr = vr_ref[...]

    slot_blocks = slot_rows // BLOCK
    c = place_ref[1]
    col_block = lax.broadcasted_iota(jnp.int32, (1, pre_rows), 1) // BLOCK
    flag = jnp.zeros((1, pre_rows), jnp.int32)
    for b in range(n_slots * slot_blocks):
        slot, sub = b // slot_blocks, b % slot_blocks
        source = jnp.bitwise_xor(c, slot) if xor_slots else slot
        flag = jnp.where(col_block == b, blocks_ref[source * slot_blocks + sub], flag)
    pre_ok = flag > 0
    rows = GROUP * resp_rows
    row_i = lax.broadcasted_iota(jnp.int32, (rows, resp_rows), 0) % resp_rows
    col_i = lax.broadcasted_iota(jnp.int32, (rows, resp_rows), 1)
    causal = row_i >= col_i
    live = lax.broadcasted_iota(jnp.int32, (rows, 1), 0) % resp_rows < length_ref[0]
    heads = [slice(j * HEAD_DIM, (j + 1) * HEAD_DIM) for j in range(GROUP)]
    q2 = jnp.concatenate([q_ref[:, cols] for cols in heads], 0)
    do2 = jnp.concatenate([do_ref[:, cols] for cols in heads], 0)
    do2 = jnp.where(live, do2, jnp.zeros_like(do2))

    sp = lax.dot_general(q2, kp, NT, preferred_element_type=jnp.float32) * scale_factor
    sr = lax.dot_general(q2, kr, NT, preferred_element_type=jnp.float32) * scale_factor
    sp = jnp.where(pre_ok, sp, neg_big)
    sr = jnp.where(causal, sr, neg_big)
    peak = jnp.maximum(jnp.max(sp, axis=-1, keepdims=True), jnp.max(sr, axis=-1, keepdims=True))
    ep = jnp.exp(sp - peak)
    er = jnp.exp(sr - peak)
    inv = 1.0 / (jnp.sum(ep, axis=-1, keepdims=True) + jnp.sum(er, axis=-1, keepdims=True))
    wp = ep * inv
    wr = er * inv
    pp = wp.astype(jnp.bfloat16)
    pr = wr.astype(jnp.bfloat16)
    att = jnp.dot(pp, vp, preferred_element_type=jnp.float32) + jnp.dot(pr, vr, preferred_element_type=jnp.float32)
    att = att.astype(jnp.bfloat16).astype(jnp.float32)
    delta = jnp.sum(do2.astype(jnp.float32) * att, axis=-1, keepdims=True)
    dpp = lax.dot_general(do2, vp, NT, preferred_element_type=jnp.float32)
    dpr = lax.dot_general(do2, vr, NT, preferred_element_type=jnp.float32)
    dsp = (wp * (dpp - delta)).astype(jnp.bfloat16)
    dsr = (wr * (dpr - delta)).astype(jnp.bfloat16)
    dq = (jnp.dot(dsp, kp, preferred_element_type=jnp.float32) + jnp.dot(
        dsr, kr, preferred_element_type=jnp.float32)) * scale_factor
    dq = dq.astype(dq_ref.dtype)
    for j, cols in enumerate(heads):
        dq_ref[:, cols] = dq[j * resp_rows:(j + 1) * resp_rows]
    dkp = lax.dot_general(dsp, q2, TN, preferred_element_type=jnp.float32)
    dkr = lax.dot_general(dsr, q2, TN, preferred_element_type=jnp.float32)
    dvp = lax.dot_general(pp, do2, TN, preferred_element_type=jnp.float32)
    dvr = lax.dot_general(pr, do2, TN, preferred_element_type=jnp.float32)
    dkr_ref[...] = (dkr * scale_factor).astype(dkr_ref.dtype)
    dvr_ref[...] = dvr.astype(dvr_ref.dtype)
    dkp = (dkp * scale_factor).astype(jnp.bfloat16)
    dvp = dvp.astype(jnp.bfloat16)
    for ref, ranges in zip(piece_refs, out_ranges):
        at = 0
        for start, rows in ranges:
            ref[0, at:at + rows] = dkp[start:start + rows]
            ref[1, at:at + rows] = dvp[start:start + rows]
            at += rows


def attention_grads(blocks, length, place, q, do, pieces, xor_slots, out_ranges, kr, vr, first_head, earlier):
    resp_rows, q_width = q.shape
    n_pair, _, _, chunk_feats = pieces[0].shape
    kv_width = kr.shape[1]
    pre_rows = sum(p.shape[2] for p in pieces)
    chunk_heads = kv_width // n_pair // HEAD_DIM
    per_chunk = chunk_feats // HEAD_DIM
    heads = n_pair * per_chunk
    n_slots = lax.axis_size("ctx")
    slot_rows = pre_rows // n_slots

    def head(g, r):
        return ((r[0] + n_pair - g // per_chunk) % n_pair) * chunk_heads + first_head + g % per_chunk

    def piece_spec(rows, kv):
        return pl.BlockSpec((None, None, rows, HEAD_DIM), lambda g, b, n, r: (g // per_chunk, kv, 0, g % per_chunk))

    qspec = pl.BlockSpec((resp_rows, GROUP * HEAD_DIM), lambda g, b, n, r: (0, head(g, r)))
    rspec = pl.BlockSpec((resp_rows, HEAD_DIM), lambda g, b, n, r: (0, head(g, r)))
    in_specs = [qspec, qspec]
    in_specs += [piece_spec(p.shape[2], 0) for p in pieces] + [piece_spec(p.shape[2], 1) for p in pieces]
    in_specs += [rspec, rspec]
    operands = [blocks, length, place, q, do] + list(pieces) + list(pieces) + [kr, vr]
    aliases = {}
    if earlier is not None:
        in_specs += [pl.BlockSpec(memory_space=pl.ANY)] * 3
        aliases = {len(operands) + i: i for i in range(3)}
        operands += list(earlier)
    out_rows = [sum(rows for _, rows in ranges) for ranges in out_ranges]
    out_specs = [qspec, rspec, rspec] + [
        pl.BlockSpec((None, 2, rows, HEAD_DIM), lambda g, b, n, r: (g // per_chunk, 0, 0, g % per_chunk))
        for rows in out_rows]
    out_shape = [
        jax.ShapeDtypeStruct((resp_rows, q_width), jnp.bfloat16),
        jax.ShapeDtypeStruct((resp_rows, kv_width), jnp.bfloat16),
        jax.ShapeDtypeStruct((resp_rows, kv_width), jnp.bfloat16),
    ] + [jax.ShapeDtypeStruct((n_pair, 2, rows, chunk_feats), jnp.bfloat16) for rows in out_rows]
    layout = (len(pieces), n_slots, slot_rows, xor_slots, tuple(tuple(r) for r in out_ranges), earlier is not None)
    flops = 2 * 6 * resp_rows * GROUP * heads * (pre_rows + resp_rows) * HEAD_DIM
    return pl.pallas_call(
        functools.partial(attention_grad_kernel, layout),
        out_shape=tuple(out_shape),
        grid_spec=pltpu.PrefetchScalarGridSpec(
            num_scalar_prefetch=3,
            grid=(heads,),
            in_specs=in_specs,
            out_specs=out_specs,
        ),
        input_output_aliases=aliases,
        cost_estimate=pl.CostEstimate(
            flops=flops,
            transcendentals=resp_rows * GROUP * heads * (pre_rows + resp_rows),
            bytes_accessed=2 * heads * HEAD_DIM * (4 * resp_rows * GROUP + 4 * pre_rows + 4 * resp_rows),
        ),
    )(*operands)


def ring_shift(x, axis, n, d):
    return lax.ppermute(x, axis, [(i, (i + d) % n) for i in range(n)])


def pair_gather(planes, pair_prompt):
    n = lax.axis_size("pair")
    r = lax.axis_index("pair")
    held = [lax.dynamic_index_in_dim(planes, pair_prompt[r], 0, keepdims=False)]
    for d in range(1, n):
        chunk = lax.dynamic_index_in_dim(planes, pair_prompt[(r + d) % n], 0, keepdims=False)
        held.append(ring_shift(chunk, "pair", n, d))
    return jnp.stack(held)


def tree_ctx():
    return lax.axis_size("ctx") == 4


def ctx_gather(x):
    n = lax.axis_size("ctx")
    if not tree_ctx():
        got = lax.all_gather(x, "ctx", axis=0, tiled=False)
        return [got[j] for j in range(n)]
    along_x = [(i, i ^ 1) for i in range(n)]
    along_y = [(i, i ^ 2) for i in range(n)]
    from_x = lax.ppermute(x, "ctx", along_x)
    from_y = lax.ppermute(x, "ctx", along_y)
    half = x.shape[2] // 2
    far_a = lax.ppermute(from_y[:, :, :half], "ctx", along_x)
    far_b = lax.ppermute(from_x[:, :, half:], "ctx", along_y)
    return [x, from_x, from_y, far_a, far_b]


def ctx_out_ranges(slot_rows):
    n = lax.axis_size("ctx")
    return [[(j * slot_rows, slot_rows)] for j in range(n)]


def ctx_reduce(pieces):
    n = lax.axis_size("ctx")
    if not tree_ctx():
        got = lax.all_to_all(jnp.stack(pieces), "ctx", split_axis=0, concat_axis=0, tiled=True)
        return jnp.sum(got.astype(jnp.float32), axis=0).astype(jnp.bfloat16)
    got = [pieces[0]] + [lax.ppermute(pieces[j], "ctx", [(i, i ^ j) for i in range(n)]) for j in range(1, n)]
    total = (got[0].astype(jnp.float32) + got[1].astype(jnp.float32)) + (
        got[2].astype(jnp.float32) + got[3].astype(jnp.float32))
    return total.astype(jnp.bfloat16)


def pair_exchange(totals):
    n = lax.axis_size("pair")
    return [totals[0]] + [ring_shift(totals[(n - d) % n], "pair", n, d) for d in range(1, n)]


def prompt_weights(pair_prompt, n_prompts):
    n = lax.axis_size("pair")
    r = lax.axis_index("pair")
    source = jnp.take(pair_prompt, (r - jnp.arange(n)) % n, mode="clip")
    return (source[:, None] == jnp.arange(n_prompts, dtype=jnp.int32)[None, :]).astype(jnp.float32)


def in_group(width, kv_heads, chunk_heads, group_heads, k):
    head = jnp.arange(width) // (width // kv_heads)
    return ((head % chunk_heads) // group_heads == k)[None]


def shards(
    queries, resp_keys, resp_values, d_out, prefix_kv, prefix_blocks, resp_lengths, pair_prompt
):
    n_prompts = prefix_kv.shape[0]
    planes = jnp.transpose(prefix_kv, (0, 2, 1, 3))
    slot_rows = planes.shape[2]
    chunk_feats = planes.shape[-1]
    n_groups = HEAD_GROUPS if chunk_feats % (HEAD_GROUPS * HEAD_DIM) == 0 else 1
    group_feats = chunk_feats // n_groups
    place = jnp.stack([lax.axis_index("pair"), lax.axis_index("ctx")]).astype(jnp.int32)
    kv_heads = resp_keys.shape[-1] // HEAD_DIM
    chunk_heads = chunk_feats // HEAD_DIM
    group_heads = group_feats // HEAD_DIM
    earlier = None
    parts = []
    for k in range(n_groups):
        cols = slice(k * group_feats, (k + 1) * group_feats)
        pieces = ctx_gather(pair_gather(planes[..., cols], pair_prompt))
        outs = attention_grads(
            prefix_blocks[0, 0], resp_lengths[0, 0].reshape(1), place, queries[0, 0], d_out[0, 0], pieces,
            tree_ctx(), ctx_out_ranges(slot_rows), resp_keys[0, 0], resp_values[0, 0],
            k * (group_feats // HEAD_DIM), None)
        if earlier is None:
            earlier = outs[:3]
        else:
            earlier = tuple(jnp.where(in_group(o.shape[1], kv_heads, chunk_heads, group_heads, k), o, e)
                            for o, e in zip(outs[:3], earlier))
        parts.append(pair_exchange(ctx_reduce(list(outs[3:]))))
    dq, dkr, dvr = earlier
    weights = prompt_weights(pair_prompt, n_prompts)
    d_prefix = sum(
        weights[d][:, None, None, None] * jnp.transpose(
            jnp.concatenate([part[d] for part in parts], -1).astype(jnp.float32), (1, 0, 2))[None]
        for d in range(len(parts[0])))
    return (dq[None, None], dkr[None, None], dvr[None, None], d_prefix)


def solution(mesh):
    placed = (
        P(("dp", "ctx"), "pair", None, None),
        P(("dp", "ctx"), "pair", None, None),
        P(("dp", "ctx"), "pair", None, None),
        P(("dp", "ctx"), "pair", None, None),
        P("dp", "ctx", None, "pair"),
        P(("dp", "ctx"), "pair", None),
        P(("dp", "ctx"), "pair"),
        P("dp"),
    )
    return jax.shard_map(
        shards,
        mesh=mesh,
        in_specs=placed,
        out_specs=(
            P(("dp", "ctx"), "pair", None, None),
            P(("dp", "ctx"), "pair", None, None),
            P(("dp", "ctx"), "pair", None, None),
            P("dp", "ctx", None, "pair"),
        ),
        check_vma=False,
    )
```

```python
import functools

import jax
import jax.numpy as jnp
from jax import lax
from jax.experimental import pallas as pl
from jax.experimental.pallas import tpu as pltpu
from jax.sharding import PartitionSpec as P

KV_HEADS = 8
GROUP = 2
HEAD_DIM = 128
BLOCK = 128
HEAD_GROUPS = 2


scale_factor = 144.0 ** (-0.5)
neg_big = -1e30

NT = (((1,), (1,)), ((), ()))
TN = (((0,), (0,)), ((), ()))


def attention_grad_kernel(layout, blocks_ref, length_ref, place_ref, q_ref, do_ref, *refs):
    n_in, n_slots, slot_rows, xor_slots, out_ranges, aliased = layout
    kv_refs = refs[:n_in]
    kr_ref, vr_ref = refs[n_in:n_in + 2]
    outs = refs[n_in + 2 + (3 if aliased else 0):]
    dq_ref, dkr_ref, dvr_ref = outs[:3]
    piece_refs = outs[3:]
    resp_rows = q_ref.shape[0]
    kp = jnp.concatenate([r[0] for r in kv_refs], 0)
    vp = jnp.concatenate([r[1] for r in kv_refs], 0)
    pre_rows = kp.shape[0]
    kr = kr_ref[...]
    vr = vr_ref[...]

    slot_blocks = slot_rows // BLOCK
    c = place_ref[1]
    col_block = lax.broadcasted_iota(jnp.int32, (1, pre_rows), 1) // BLOCK
    flag = jnp.zeros((1, pre_rows), jnp.int32)
    for b in range(n_slots * slot_blocks):
        slot, sub = b // slot_blocks, b % slot_blocks
        source = jnp.bitwise_xor(c, slot) if xor_slots else slot
        flag = jnp.where(col_block == b, blocks_ref[source * slot_blocks + sub], flag)
    pre_ok = flag > 0
    rows = GROUP * resp_rows
    row_i = lax.broadcasted_iota(jnp.int32, (rows, resp_rows), 0) % resp_rows
    col_i = lax.broadcasted_iota(jnp.int32, (rows, resp_rows), 1)
    causal = row_i >= col_i
    live = lax.broadcasted_iota(jnp.int32, (rows, 1), 0) % resp_rows < length_ref[0]
    heads = [slice(j * HEAD_DIM, (j + 1) * HEAD_DIM) for j in range(GROUP)]
    q2 = jnp.concatenate([q_ref[:, cols] for cols in heads], 0)
    do2 = jnp.concatenate([do_ref[:, cols] for cols in heads], 0)
    do2 = jnp.where(live, do2, jnp.zeros_like(do2))

    sp = lax.dot_general(q2, kp, NT, preferred_element_type=jnp.float32) * scale_factor
    sr = lax.dot_general(q2, kr, NT, preferred_element_type=jnp.float32) * scale_factor
    sp = jnp.where(pre_ok, sp, neg_big)
    sr = jnp.where(causal, sr, neg_big)
    peak = jnp.maximum(jnp.max(sp, axis=-1, keepdims=True), jnp.max(sr, axis=-1, keepdims=True))
    ep = jnp.exp(sp - peak)
    er = jnp.exp(sr - peak)
    inv = 1.0 / (jnp.sum(ep, axis=-1, keepdims=True) + jnp.sum(er, axis=-1, keepdims=True))
    wp = ep * inv
    wr = er * inv
    pp = wp.astype(jnp.bfloat16)
    pr = wr.astype(jnp.bfloat16)
    att = jnp.dot(pp, vp, preferred_element_type=jnp.float32) + jnp.dot(pr, vr, preferred_element_type=jnp.float32)
    att = att.astype(jnp.bfloat16).astype(jnp.float32)
    delta = jnp.sum(do2.astype(jnp.float32) * att, axis=-1, keepdims=True)
    dpp = lax.dot_general(do2, vp, NT, preferred_element_type=jnp.float32)
    dpr = lax.dot_general(do2, vr, NT, preferred_element_type=jnp.float32)
    dsp = (wp * (dpp - delta)).astype(jnp.bfloat16)
    dsr = (wr * (dpr - delta)).astype(jnp.bfloat16)
    dq = (jnp.dot(dsp, kp, preferred_element_type=jnp.float32) + jnp.dot(
        dsr, kr, preferred_element_type=jnp.float32)) * scale_factor
    dq = dq.astype(dq_ref.dtype)
    for j, cols in enumerate(heads):
        dq_ref[:, cols] = dq[j * resp_rows:(j + 1) * resp_rows]
    dkp = lax.dot_general(dsp, q2, TN, preferred_element_type=jnp.float32)
    dkr = lax.dot_general(dsr, q2, TN, preferred_element_type=jnp.float32)
    dvp = lax.dot_general(pp, do2, TN, preferred_element_type=jnp.float32)
    dvr = lax.dot_general(pr, do2, TN, preferred_element_type=jnp.float32)
    dkr_ref[...] = (dkr * scale_factor).astype(dkr_ref.dtype)
    dvr_ref[...] = dvr.astype(dvr_ref.dtype)
    dkp = (dkp * scale_factor).astype(jnp.bfloat16)
    dvp = dvp.astype(jnp.bfloat16)
    for ref, ranges in zip(piece_refs, out_ranges):
        at = 0
        for start, rows in ranges:
            ref[0, at:at + rows] = dkp[start:start + rows]
            ref[1, at:at + rows] = dvp[start:start + rows]
            at += rows


def attention_grads(blocks, length, place, q, do, pieces, xor_slots, out_ranges, kr, vr, first_head, earlier):
    resp_rows, q_width = q.shape
    n_pair, _, _, chunk_feats = pieces[0].shape
    kv_width = kr.shape[1]
    pre_rows = sum(p.shape[2] for p in pieces)
    chunk_heads = kv_width // n_pair // HEAD_DIM
    per_chunk = chunk_feats // HEAD_DIM
    heads = n_pair * per_chunk
    n_slots = lax.axis_size("ctx")
    slot_rows = pre_rows // n_slots

    def head(g, r):
        return ((r[0] + n_pair - g // per_chunk) % n_pair) * chunk_heads + first_head + g % per_chunk

    def piece_spec(rows):
        return pl.BlockSpec((None, 2, rows, HEAD_DIM), lambda g, b, n, r: (g // per_chunk, 0, 0, g % per_chunk))

    qspec = pl.BlockSpec((resp_rows, GROUP * HEAD_DIM), lambda g, b, n, r: (0, head(g, r)))
    rspec = pl.BlockSpec((resp_rows, HEAD_DIM), lambda g, b, n, r: (0, head(g, r)))
    in_specs = [qspec, qspec]
    in_specs += [piece_spec(p.shape[2]) for p in pieces]
    in_specs += [rspec, rspec]
    operands = [blocks, length, place, q, do] + list(pieces) + [kr, vr]
    aliases = {}
    if earlier is not None:
        in_specs += [pl.BlockSpec(memory_space=pl.ANY)] * 3
        aliases = {len(operands) + i: i for i in range(3)}
        operands += list(earlier)
    out_rows = [sum(rows for _, rows in ranges) for ranges in out_ranges]
    out_specs = [qspec, rspec, rspec] + [
        pl.BlockSpec((None, 2, rows, HEAD_DIM), lambda g, b, n, r: (g // per_chunk, 0, 0, g % per_chunk))
        for rows in out_rows]
    out_shape = [
        jax.ShapeDtypeStruct((resp_rows, q_width), jnp.bfloat16),
        jax.ShapeDtypeStruct((resp_rows, kv_width), jnp.bfloat16),
        jax.ShapeDtypeStruct((resp_rows, kv_width), jnp.bfloat16),
    ] + [jax.ShapeDtypeStruct((n_pair, 2, rows, chunk_feats), jnp.bfloat16) for rows in out_rows]
    layout = (len(pieces), n_slots, slot_rows, xor_slots, tuple(tuple(r) for r in out_ranges), earlier is not None)
    flops = 2 * 6 * resp_rows * GROUP * heads * (pre_rows + resp_rows) * HEAD_DIM
    return pl.pallas_call(
        functools.partial(attention_grad_kernel, layout),
        out_shape=tuple(out_shape),
        grid_spec=pltpu.PrefetchScalarGridSpec(
            num_scalar_prefetch=3,
            grid=(heads,),
            in_specs=in_specs,
            out_specs=out_specs,
        ),
        input_output_aliases=aliases,
        cost_estimate=pl.CostEstimate(
            flops=flops,
            transcendentals=resp_rows * GROUP * heads * (pre_rows + resp_rows),
            bytes_accessed=2 * heads * HEAD_DIM * (4 * resp_rows * GROUP + 4 * pre_rows + 4 * resp_rows),
        ),
    )(*operands)


def ring_shift(x, axis, n, d):
    return lax.ppermute(x, axis, [(i, (i + d) % n) for i in range(n)])


def pair_gather(planes, pair_prompt):
    n = lax.axis_size("pair")
    r = lax.axis_index("pair")
    held = [lax.dynamic_index_in_dim(planes, pair_prompt[r], 0, keepdims=False)]
    for d in range(1, n):
        chunk = lax.dynamic_index_in_dim(planes, pair_prompt[(r + d) % n], 0, keepdims=False)
        held.append(ring_shift(chunk, "pair", n, d))
    return jnp.stack(held)


def tree_ctx():
    return lax.axis_size("ctx") == 4


def ctx_gather(x):
    n = lax.axis_size("ctx")
    if not tree_ctx():
        got = lax.all_gather(x, "ctx", axis=0, tiled=False)
        return [got[j] for j in range(n)]
    along_x = [(i, i ^ 1) for i in range(n)]
    along_y = [(i, i ^ 2) for i in range(n)]
    from_x = lax.ppermute(x, "ctx", along_x)
    from_y = lax.ppermute(x, "ctx", along_y)
    half = x.shape[2] // 2
    far_a = lax.ppermute(from_y[:, :, :half], "ctx", along_x)
    far_b = lax.ppermute(from_x[:, :, half:], "ctx", along_y)
    return [x, from_x, from_y, far_a, far_b]


def ctx_out_ranges(slot_rows):
    n = lax.axis_size("ctx")
    return [[(j * slot_rows, slot_rows)] for j in range(n)]


def ctx_reduce(pieces):
    n = lax.axis_size("ctx")
    if not tree_ctx():
        got = lax.all_to_all(jnp.stack(pieces), "ctx", split_axis=0, concat_axis=0, tiled=True)
        return jnp.sum(got.astype(jnp.float32), axis=0).astype(jnp.bfloat16)
    got = [pieces[0]] + [lax.ppermute(pieces[j], "ctx", [(i, i ^ j) for i in range(n)]) for j in range(1, n)]
    total = (got[0].astype(jnp.float32) + got[1].astype(jnp.float32)) + (
        got[2].astype(jnp.float32) + got[3].astype(jnp.float32))
    return total.astype(jnp.bfloat16)


def pair_exchange(totals):
    n = lax.axis_size("pair")
    return [totals[0]] + [ring_shift(totals[(n - d) % n], "pair", n, d) for d in range(1, n)]


def prompt_weights(pair_prompt, n_prompts):
    n = lax.axis_size("pair")
    r = lax.axis_index("pair")
    source = jnp.take(pair_prompt, (r - jnp.arange(n)) % n, mode="clip")
    return (source[:, None] == jnp.arange(n_prompts, dtype=jnp.int32)[None, :]).astype(jnp.float32)


def in_group(width, kv_heads, chunk_heads, group_heads, k):
    head = jnp.arange(width) // (width // kv_heads)
    return ((head % chunk_heads) // group_heads == k)[None]


def shards(
    queries, resp_keys, resp_values, d_out, prefix_kv, prefix_blocks, resp_lengths, pair_prompt
):
    n_prompts = prefix_kv.shape[0]
    planes = jnp.transpose(prefix_kv, (0, 2, 1, 3))
    slot_rows = planes.shape[2]
    chunk_feats = planes.shape[-1]
    n_groups = HEAD_GROUPS if chunk_feats % (HEAD_GROUPS * HEAD_DIM) == 0 else 1
    group_feats = chunk_feats // n_groups
    place = jnp.stack([lax.axis_index("pair"), lax.axis_index("ctx")]).astype(jnp.int32)
    kv_heads = resp_keys.shape[-1] // HEAD_DIM
    chunk_heads = chunk_feats // HEAD_DIM
    group_heads = group_feats // HEAD_DIM
    earlier = None
    parts = []
    for k in range(n_groups):
        cols = slice(k * group_feats, (k + 1) * group_feats)
        pieces = ctx_gather(pair_gather(planes[..., cols], pair_prompt))
        outs = attention_grads(
            prefix_blocks[0, 0], resp_lengths[0, 0].reshape(1), place, queries[0, 0], d_out[0, 0], pieces,
            tree_ctx(), ctx_out_ranges(slot_rows), resp_keys[0, 0], resp_values[0, 0],
            k * (group_feats // HEAD_DIM), None)
        if earlier is None:
            earlier = outs[:3]
        else:
            earlier = tuple(jnp.where(in_group(o.shape[1], kv_heads, chunk_heads, group_heads, k), o, e)
                            for o, e in zip(outs[:3], earlier))
        parts.append(pair_exchange(ctx_reduce(list(outs[3:]))))
    dq, dkr, dvr = earlier
    weights = prompt_weights(pair_prompt, n_prompts)
    d_prefix = jnp.concatenate([
        sum(weights[d][:, None, None, None] * jnp.transpose(got.astype(jnp.float32), (1, 0, 2))[None]
            for d, got in enumerate(part))
        for part in parts], -1)
    return (dq[None, None], dkr[None, None], dvr[None, None], d_prefix)


def solution(mesh):
    placed = (
        P(("dp", "ctx"), "pair", None, None),
        P(("dp", "ctx"), "pair", None, None),
        P(("dp", "ctx"), "pair", None, None),
        P(("dp", "ctx"), "pair", None, None),
        P("dp", "ctx", None, "pair"),
        P(("dp", "ctx"), "pair", None),
        P(("dp", "ctx"), "pair"),
        P("dp"),
    )
    return jax.shard_map(
        shards,
        mesh=mesh,
        in_specs=placed,
        out_specs=(
            P(("dp", "ctx"), "pair", None, None),
            P(("dp", "ctx"), "pair", None, None),
            P(("dp", "ctx"), "pair", None, None),
            P("dp", "ctx", None, "pair"),
        ),
        check_vma=False,
    )
```

```python
import functools

import jax
import jax.numpy as jnp
from jax import lax
from jax.experimental import pallas as pl
from jax.experimental.pallas import tpu as pltpu
from jax.sharding import PartitionSpec as P

KV_HEADS = 8
GROUP = 2
HEAD_DIM = 128
BLOCK = 128
HEAD_GROUPS = 1


scale_factor = 144.0 ** (-0.5)
neg_big = -1e30

NT = (((1,), (1,)), ((), ()))
TN = (((0,), (0,)), ((), ()))


def attention_grad_kernel(layout, blocks_ref, length_ref, place_ref, q_ref, do_ref, *refs):
    n_in, n_slots, slot_rows, xor_slots, out_ranges, aliased = layout
    kv_refs = refs[:n_in]
    kr_ref, vr_ref = refs[n_in:n_in + 2]
    outs = refs[n_in + 2 + (3 if aliased else 0):]
    dq_ref, dkr_ref, dvr_ref = outs[:3]
    piece_refs = outs[3:]
    resp_rows = q_ref.shape[0]
    kp = jnp.concatenate([r[0] for r in kv_refs], 0)
    vp = jnp.concatenate([r[1] for r in kv_refs], 0)
    pre_rows = kp.shape[0]
    kr = kr_ref[...]
    vr = vr_ref[...]

    slot_blocks = slot_rows // BLOCK
    c = place_ref[1]
    col_block = lax.broadcasted_iota(jnp.int32, (1, pre_rows), 1) // BLOCK
    flag = jnp.zeros((1, pre_rows), jnp.int32)
    for b in range(n_slots * slot_blocks):
        slot, sub = b // slot_blocks, b % slot_blocks
        source = jnp.bitwise_xor(c, slot) if xor_slots else slot
        flag = jnp.where(col_block == b, blocks_ref[source * slot_blocks + sub], flag)
    pre_ok = flag > 0
    rows = GROUP * resp_rows
    row_i = lax.broadcasted_iota(jnp.int32, (rows, resp_rows), 0) % resp_rows
    col_i = lax.broadcasted_iota(jnp.int32, (rows, resp_rows), 1)
    causal = row_i >= col_i
    live = lax.broadcasted_iota(jnp.int32, (rows, 1), 0) % resp_rows < length_ref[0]
    heads = [slice(j * HEAD_DIM, (j + 1) * HEAD_DIM) for j in range(GROUP)]
    q2 = jnp.concatenate([q_ref[:, cols] for cols in heads], 0)
    do2 = jnp.concatenate([do_ref[:, cols] for cols in heads], 0)
    do2 = jnp.where(live, do2, jnp.zeros_like(do2))

    sp = lax.dot_general(q2, kp, NT, preferred_element_type=jnp.float32) * scale_factor
    sr = lax.dot_general(q2, kr, NT, preferred_element_type=jnp.float32) * scale_factor
    sp = jnp.where(pre_ok, sp, neg_big)
    sr = jnp.where(causal, sr, neg_big)
    peak = jnp.maximum(jnp.max(sp, axis=-1, keepdims=True), jnp.max(sr, axis=-1, keepdims=True))
    ep = jnp.exp(sp - peak)
    er = jnp.exp(sr - peak)
    inv = 1.0 / (jnp.sum(ep, axis=-1, keepdims=True) + jnp.sum(er, axis=-1, keepdims=True))
    wp = ep * inv
    wr = er * inv
    pp = wp.astype(jnp.bfloat16)
    pr = wr.astype(jnp.bfloat16)
    att = jnp.dot(pp, vp, preferred_element_type=jnp.float32) + jnp.dot(pr, vr, preferred_element_type=jnp.float32)
    att = att.astype(jnp.bfloat16).astype(jnp.float32)
    delta = jnp.sum(do2.astype(jnp.float32) * att, axis=-1, keepdims=True)
    dpp = lax.dot_general(do2, vp, NT, preferred_element_type=jnp.float32)
    dpr = lax.dot_general(do2, vr, NT, preferred_element_type=jnp.float32)
    dsp = (wp * (dpp - delta)).astype(jnp.bfloat16)
    dsr = (wr * (dpr - delta)).astype(jnp.bfloat16)
    dq = (jnp.dot(dsp, kp, preferred_element_type=jnp.float32) + jnp.dot(
        dsr, kr, preferred_element_type=jnp.float32)) * scale_factor
    dq = dq.astype(dq_ref.dtype)
    for j, cols in enumerate(heads):
        dq_ref[:, cols] = dq[j * resp_rows:(j + 1) * resp_rows]
    dkp = lax.dot_general(dsp, q2, TN, preferred_element_type=jnp.float32)
    dkr = lax.dot_general(dsr, q2, TN, preferred_element_type=jnp.float32)
    dvp = lax.dot_general(pp, do2, TN, preferred_element_type=jnp.float32)
    dvr = lax.dot_general(pr, do2, TN, preferred_element_type=jnp.float32)
    dkr_ref[...] = (dkr * scale_factor).astype(dkr_ref.dtype)
    dvr_ref[...] = dvr.astype(dvr_ref.dtype)
    dkp = (dkp * scale_factor).astype(jnp.bfloat16)
    dvp = dvp.astype(jnp.bfloat16)
    for ref, ranges in zip(piece_refs, out_ranges):
        at = 0
        for start, rows in ranges:
            ref[0, at:at + rows] = dkp[start:start + rows]
            ref[1, at:at + rows] = dvp[start:start + rows]
            at += rows


def attention_grads(blocks, length, place, q, do, pieces, xor_slots, out_ranges, kr, vr, first_head, earlier):
    resp_rows, q_width = q.shape
    n_pair, _, _, chunk_feats = pieces[0].shape
    kv_width = kr.shape[1]
    pre_rows = sum(p.shape[2] for p in pieces)
    chunk_heads = kv_width // n_pair // HEAD_DIM
    per_chunk = chunk_feats // HEAD_DIM
    heads = n_pair * per_chunk
    n_slots = lax.axis_size("ctx")
    slot_rows = pre_rows // n_slots

    def head(g, r):
        return ((r[0] + n_pair - g // per_chunk) % n_pair) * chunk_heads + first_head + g % per_chunk

    def piece_spec(rows):
        return pl.BlockSpec((None, 2, rows, HEAD_DIM), lambda g, b, n, r: (g // per_chunk, 0, 0, g % per_chunk))

    qspec = pl.BlockSpec((resp_rows, GROUP * HEAD_DIM), lambda g, b, n, r: (0, head(g, r)))
    rspec = pl.BlockSpec((resp_rows, HEAD_DIM), lambda g, b, n, r: (0, head(g, r)))
    in_specs = [qspec, qspec]
    in_specs += [piece_spec(p.shape[2]) for p in pieces]
    in_specs += [rspec, rspec]
    operands = [blocks, length, place, q, do] + list(pieces) + [kr, vr]
    aliases = {}
    if earlier is not None:
        in_specs += [pl.BlockSpec(memory_space=pl.ANY)] * 3
        aliases = {len(operands) + i: i for i in range(3)}
        operands += list(earlier)
    out_rows = [sum(rows for _, rows in ranges) for ranges in out_ranges]
    out_specs = [qspec, rspec, rspec] + [
        pl.BlockSpec((None, 2, rows, HEAD_DIM), lambda g, b, n, r: (g // per_chunk, 0, 0, g % per_chunk))
        for rows in out_rows]
    out_shape = [
        jax.ShapeDtypeStruct((resp_rows, q_width), jnp.bfloat16),
        jax.ShapeDtypeStruct((resp_rows, kv_width), jnp.bfloat16),
        jax.ShapeDtypeStruct((resp_rows, kv_width), jnp.bfloat16),
    ] + [jax.ShapeDtypeStruct((n_pair, 2, rows, chunk_feats), jnp.bfloat16) for rows in out_rows]
    layout = (len(pieces), n_slots, slot_rows, xor_slots, tuple(tuple(r) for r in out_ranges), earlier is not None)
    flops = 2 * 6 * resp_rows * GROUP * heads * (pre_rows + resp_rows) * HEAD_DIM
    return pl.pallas_call(
        functools.partial(attention_grad_kernel, layout),
        out_shape=tuple(out_shape),
        grid_spec=pltpu.PrefetchScalarGridSpec(
            num_scalar_prefetch=3,
            grid=(heads,),
            in_specs=in_specs,
            out_specs=out_specs,
        ),
        input_output_aliases=aliases,
        cost_estimate=pl.CostEstimate(
            flops=flops,
            transcendentals=resp_rows * GROUP * heads * (pre_rows + resp_rows),
            bytes_accessed=2 * heads * HEAD_DIM * (4 * resp_rows * GROUP + 4 * pre_rows + 4 * resp_rows),
        ),
    )(*operands)


def ring_shift(x, axis, n, d):
    return lax.ppermute(x, axis, [(i, (i + d) % n) for i in range(n)])


def pair_gather(planes, pair_prompt):
    n = lax.axis_size("pair")
    r = lax.axis_index("pair")
    held = [lax.dynamic_index_in_dim(planes, pair_prompt[r], 0, keepdims=False)]
    for d in range(1, n):
        chunk = lax.dynamic_index_in_dim(planes, pair_prompt[(r + d) % n], 0, keepdims=False)
        held.append(ring_shift(chunk, "pair", n, d))
    return jnp.stack(held)


def tree_ctx():
    return lax.axis_size("ctx") == 4


def ctx_gather(x):
    n = lax.axis_size("ctx")
    if not tree_ctx():
        got = lax.all_gather(x, "ctx", axis=0, tiled=False)
        return [got[j] for j in range(n)]
    along_x = [(i, i ^ 1) for i in range(n)]
    along_y = [(i, i ^ 2) for i in range(n)]
    from_x = lax.ppermute(x, "ctx", along_x)
    from_y = lax.ppermute(x, "ctx", along_y)
    half = x.shape[2] // 2
    far_a = lax.ppermute(from_y[:, :, :half], "ctx", along_x)
    far_b = lax.ppermute(from_x[:, :, half:], "ctx", along_y)
    return [x, from_x, from_y, far_a, far_b]


def ctx_out_ranges(slot_rows):
    n = lax.axis_size("ctx")
    return [[(j * slot_rows, slot_rows)] for j in range(n)]


def ctx_reduce(pieces):
    n = lax.axis_size("ctx")
    if not tree_ctx():
        got = lax.all_to_all(jnp.stack(pieces), "ctx", split_axis=0, concat_axis=0, tiled=True)
        return jnp.sum(got.astype(jnp.float32), axis=0).astype(jnp.bfloat16)
    got = [pieces[0]] + [lax.ppermute(pieces[j], "ctx", [(i, i ^ j) for i in range(n)]) for j in range(1, n)]
    total = (got[0].astype(jnp.float32) + got[1].astype(jnp.float32)) + (
        got[2].astype(jnp.float32) + got[3].astype(jnp.float32))
    return total.astype(jnp.bfloat16)


def pair_exchange(totals):
    n = lax.axis_size("pair")
    return [totals[0]] + [ring_shift(totals[(n - d) % n], "pair", n, d) for d in range(1, n)]


def prompt_weights(pair_prompt, n_prompts):
    n = lax.axis_size("pair")
    r = lax.axis_index("pair")
    source = jnp.take(pair_prompt, (r - jnp.arange(n)) % n, mode="clip")
    return (source[:, None] == jnp.arange(n_prompts, dtype=jnp.int32)[None, :]).astype(jnp.float32)


def in_group(width, kv_heads, chunk_heads, group_heads, k):
    head = jnp.arange(width) // (width // kv_heads)
    return ((head % chunk_heads) // group_heads == k)[None]


def shards(
    queries, resp_keys, resp_values, d_out, prefix_kv, prefix_blocks, resp_lengths, pair_prompt
):
    n_prompts = prefix_kv.shape[0]
    planes = jnp.transpose(prefix_kv, (0, 2, 1, 3))
    slot_rows = planes.shape[2]
    chunk_feats = planes.shape[-1]
    n_groups = HEAD_GROUPS if chunk_feats % (HEAD_GROUPS * HEAD_DIM) == 0 else 1
    group_feats = chunk_feats // n_groups
    place = jnp.stack([lax.axis_index("pair"), lax.axis_index("ctx")]).astype(jnp.int32)
    kv_heads = resp_keys.shape[-1] // HEAD_DIM
    chunk_heads = chunk_feats // HEAD_DIM
    group_heads = group_feats // HEAD_DIM
    earlier = None
    parts = []
    for k in range(n_groups):
        cols = slice(k * group_feats, (k + 1) * group_feats)
        pieces = ctx_gather(pair_gather(planes[..., cols], pair_prompt))
        outs = attention_grads(
            prefix_blocks[0, 0], resp_lengths[0, 0].reshape(1), place, queries[0, 0], d_out[0, 0], pieces,
            tree_ctx(), ctx_out_ranges(slot_rows), resp_keys[0, 0], resp_values[0, 0],
            k * (group_feats // HEAD_DIM), None)
        if earlier is None:
            earlier = outs[:3]
        else:
            earlier = tuple(jnp.where(in_group(o.shape[1], kv_heads, chunk_heads, group_heads, k), o, e)
                            for o, e in zip(outs[:3], earlier))
        parts.append(pair_exchange(ctx_reduce(list(outs[3:]))))
    dq, dkr, dvr = earlier
    weights = prompt_weights(pair_prompt, n_prompts)
    d_prefix = jnp.concatenate([
        sum(weights[d][:, None, None, None] * jnp.transpose(got.astype(jnp.float32), (1, 0, 2))[None]
            for d, got in enumerate(part))
        for part in parts], -1)
    return (dq[None, None], dkr[None, None], dvr[None, None], d_prefix)


def solution(mesh):
    placed = (
        P(("dp", "ctx"), "pair", None, None),
        P(("dp", "ctx"), "pair", None, None),
        P(("dp", "ctx"), "pair", None, None),
        P(("dp", "ctx"), "pair", None, None),
        P("dp", "ctx", None, "pair"),
        P(("dp", "ctx"), "pair", None),
        P(("dp", "ctx"), "pair"),
        P("dp"),
    )
    return jax.shard_map(
        shards,
        mesh=mesh,
        in_specs=placed,
        out_specs=(
            P(("dp", "ctx"), "pair", None, None),
            P(("dp", "ctx"), "pair", None, None),
            P(("dp", "ctx"), "pair", None, None),
            P("dp", "ctx", None, "pair"),
        ),
        check_vma=False,
    )
```

```python
import functools

import jax
import jax.numpy as jnp
from jax import lax
from jax.experimental import pallas as pl
from jax.experimental.pallas import tpu as pltpu
from jax.sharding import PartitionSpec as P

KV_HEADS = 8
GROUP = 2
HEAD_DIM = 128
BLOCK = 128
HEAD_GROUPS = 2


scale_factor = 144.0 ** (-0.5)
neg_big = -1e30

NT = (((1,), (1,)), ((), ()))
TN = (((0,), (0,)), ((), ()))


def attention_grad_kernel(layout, blocks_ref, length_ref, place_ref, q_ref, do_ref, *refs):
    n_in, n_slots, slot_rows, xor_slots, out_ranges, aliased = layout
    kv_refs = refs[:n_in]
    kr_ref, vr_ref = refs[n_in:n_in + 2]
    outs = refs[n_in + 2 + (3 if aliased else 0):]
    dq_ref, dkr_ref, dvr_ref = outs[:3]
    piece_refs = outs[3:]
    resp_rows = q_ref.shape[0]
    kp = jnp.concatenate([r[0] for r in kv_refs], 0)
    vp = jnp.concatenate([r[1] for r in kv_refs], 0)
    pre_rows = kp.shape[0]
    kr = kr_ref[...]
    vr = vr_ref[...]

    slot_blocks = slot_rows // BLOCK
    c = place_ref[1]
    col_block = lax.broadcasted_iota(jnp.int32, (1, pre_rows), 1) // BLOCK
    flag = jnp.zeros((1, pre_rows), jnp.int32)
    for b in range(n_slots * slot_blocks):
        slot, sub = b // slot_blocks, b % slot_blocks
        source = jnp.bitwise_xor(c, slot) if xor_slots else slot
        flag = jnp.where(col_block == b, blocks_ref[source * slot_blocks + sub], flag)
    pre_ok = flag > 0
    rows = GROUP * resp_rows
    row_i = lax.broadcasted_iota(jnp.int32, (rows, resp_rows), 0) % resp_rows
    col_i = lax.broadcasted_iota(jnp.int32, (rows, resp_rows), 1)
    causal = row_i >= col_i
    live = lax.broadcasted_iota(jnp.int32, (rows, 1), 0) % resp_rows < length_ref[0]
    heads = [slice(j * HEAD_DIM, (j + 1) * HEAD_DIM) for j in range(GROUP)]
    q2 = jnp.concatenate([q_ref[:, cols] for cols in heads], 0)
    do2 = jnp.concatenate([do_ref[:, cols] for cols in heads], 0)
    do2 = jnp.where(live, do2, jnp.zeros_like(do2))

    sp = lax.dot_general(q2, kp, NT, preferred_element_type=jnp.float32) * scale_factor
    sr = lax.dot_general(q2, kr, NT, preferred_element_type=jnp.float32) * scale_factor
    sp = jnp.where(pre_ok, sp, neg_big)
    sr = jnp.where(causal, sr, neg_big)
    peak = jnp.maximum(jnp.max(sp, axis=-1, keepdims=True), jnp.max(sr, axis=-1, keepdims=True))
    ep = jnp.exp(sp - peak)
    er = jnp.exp(sr - peak)
    inv = 1.0 / (jnp.sum(ep, axis=-1, keepdims=True) + jnp.sum(er, axis=-1, keepdims=True))
    wp = ep * inv
    wr = er * inv
    pp = wp.astype(jnp.bfloat16)
    pr = wr.astype(jnp.bfloat16)
    att = jnp.dot(pp, vp, preferred_element_type=jnp.float32) + jnp.dot(pr, vr, preferred_element_type=jnp.float32)
    att = att.astype(jnp.bfloat16).astype(jnp.float32)
    delta = jnp.sum(do2.astype(jnp.float32) * att, axis=-1, keepdims=True)
    dpp = lax.dot_general(do2, vp, NT, preferred_element_type=jnp.float32)
    dpr = lax.dot_general(do2, vr, NT, preferred_element_type=jnp.float32)
    dsp = (wp * (dpp - delta)).astype(jnp.bfloat16)
    dsr = (wr * (dpr - delta)).astype(jnp.bfloat16)
    dq = (jnp.dot(dsp, kp, preferred_element_type=jnp.float32) + jnp.dot(
        dsr, kr, preferred_element_type=jnp.float32)) * scale_factor
    dq = dq.astype(dq_ref.dtype)
    for j, cols in enumerate(heads):
        dq_ref[:, cols] = dq[j * resp_rows:(j + 1) * resp_rows]
    dkp = lax.dot_general(dsp, q2, TN, preferred_element_type=jnp.float32)
    dkr = lax.dot_general(dsr, q2, TN, preferred_element_type=jnp.float32)
    dvp = lax.dot_general(pp, do2, TN, preferred_element_type=jnp.float32)
    dvr = lax.dot_general(pr, do2, TN, preferred_element_type=jnp.float32)
    dkr_ref[...] = (dkr * scale_factor).astype(dkr_ref.dtype)
    dvr_ref[...] = dvr.astype(dvr_ref.dtype)
    dkp = (dkp * scale_factor).astype(jnp.bfloat16)
    dvp = dvp.astype(jnp.bfloat16)
    for ref, ranges in zip(piece_refs, out_ranges):
        at = 0
        for start, rows in ranges:
            ref[0, at:at + rows] = dkp[start:start + rows]
            ref[1, at:at + rows] = dvp[start:start + rows]
            at += rows


def attention_grads(blocks, length, place, q, do, pieces, xor_slots, out_ranges, kr, vr, first_head, earlier):
    resp_rows, q_width = q.shape
    n_pair, _, _, chunk_feats = pieces[0].shape
    kv_width = kr.shape[1]
    pre_rows = sum(p.shape[2] for p in pieces)
    chunk_heads = kv_width // n_pair // HEAD_DIM
    per_chunk = chunk_feats // HEAD_DIM
    heads = n_pair * per_chunk
    n_slots = lax.axis_size("ctx")
    slot_rows = pre_rows // n_slots

    def head(g, r):
        return ((r[0] + n_pair - g // per_chunk) % n_pair) * chunk_heads + first_head + g % per_chunk

    def piece_spec(rows):
        return pl.BlockSpec((None, 2, rows, HEAD_DIM), lambda g, b, n, r: (g // per_chunk, 0, 0, g % per_chunk))

    qspec = pl.BlockSpec((resp_rows, GROUP * HEAD_DIM), lambda g, b, n, r: (0, head(g, r)))
    rspec = pl.BlockSpec((resp_rows, HEAD_DIM), lambda g, b, n, r: (0, head(g, r)))
    in_specs = [qspec, qspec]
    in_specs += [piece_spec(p.shape[2]) for p in pieces]
    in_specs += [rspec, rspec]
    operands = [blocks, length, place, q, do] + list(pieces) + [kr, vr]
    aliases = {}
    if earlier is not None:
        in_specs += [pl.BlockSpec(memory_space=pl.ANY)] * 3
        aliases = {len(operands) + i: i for i in range(3)}
        operands += list(earlier)
    out_rows = [sum(rows for _, rows in ranges) for ranges in out_ranges]
    out_specs = [qspec, rspec, rspec] + [
        pl.BlockSpec((None, 2, rows, HEAD_DIM), lambda g, b, n, r: (g // per_chunk, 0, 0, g % per_chunk))
        for rows in out_rows]
    out_shape = [
        jax.ShapeDtypeStruct((resp_rows, q_width), jnp.bfloat16),
        jax.ShapeDtypeStruct((resp_rows, kv_width), jnp.bfloat16),
        jax.ShapeDtypeStruct((resp_rows, kv_width), jnp.bfloat16),
    ] + [jax.ShapeDtypeStruct((n_pair, 2, rows, chunk_feats), jnp.bfloat16) for rows in out_rows]
    layout = (len(pieces), n_slots, slot_rows, xor_slots, tuple(tuple(r) for r in out_ranges), earlier is not None)
    flops = 2 * 6 * resp_rows * GROUP * heads * (pre_rows + resp_rows) * HEAD_DIM
    return pl.pallas_call(
        functools.partial(attention_grad_kernel, layout),
        out_shape=tuple(out_shape),
        grid_spec=pltpu.PrefetchScalarGridSpec(
            num_scalar_prefetch=3,
            grid=(heads,),
            in_specs=in_specs,
            out_specs=out_specs,
        ),
        input_output_aliases=aliases,
        cost_estimate=pl.CostEstimate(
            flops=flops,
            transcendentals=resp_rows * GROUP * heads * (pre_rows + resp_rows),
            bytes_accessed=2 * heads * HEAD_DIM * (4 * resp_rows * GROUP + 4 * pre_rows + 4 * resp_rows),
        ),
    )(*operands)


def ring_shift(x, axis, n, d):
    return lax.ppermute(x, axis, [(i, (i + d) % n) for i in range(n)])


def pair_gather(planes, pair_prompt):
    n = lax.axis_size("pair")
    r = lax.axis_index("pair")
    held = [lax.dynamic_index_in_dim(planes, pair_prompt[r], 0, keepdims=False)]
    for d in range(1, n):
        chunk = lax.dynamic_index_in_dim(planes, pair_prompt[(r + d) % n], 0, keepdims=False)
        held.append(ring_shift(chunk, "pair", n, d))
    return jnp.stack(held)


def tree_ctx():
    return lax.axis_size("ctx") == 4


def ctx_gather(x):
    n = lax.axis_size("ctx")
    if not tree_ctx():
        got = lax.all_gather(x, "ctx", axis=0, tiled=False)
        return [got[j] for j in range(n)]
    along_x = [(i, i ^ 1) for i in range(n)]
    along_y = [(i, i ^ 2) for i in range(n)]
    from_x = lax.ppermute(x, "ctx", along_x)
    from_y = lax.ppermute(x, "ctx", along_y)
    half = x.shape[2] // 2
    far_a = lax.ppermute(from_y[:, :, :half], "ctx", along_x)
    far_b = lax.ppermute(from_x[:, :, half:], "ctx", along_y)
    return [x, from_x, from_y, far_a, far_b]


def ctx_out_ranges(slot_rows):
    n = lax.axis_size("ctx")
    return [[(j * slot_rows, slot_rows)] for j in range(n)]


def ctx_reduce(pieces):
    n = lax.axis_size("ctx")
    if not tree_ctx():
        got = lax.all_to_all(jnp.stack(pieces), "ctx", split_axis=0, concat_axis=0, tiled=True)
        return jnp.sum(got.astype(jnp.float32), axis=0).astype(jnp.bfloat16)
    got = [pieces[0]] + [lax.ppermute(pieces[j], "ctx", [(i, i ^ j) for i in range(n)]) for j in range(1, n)]
    total = (got[0].astype(jnp.float32) + got[1].astype(jnp.float32)) + (
        got[2].astype(jnp.float32) + got[3].astype(jnp.float32))
    return total.astype(jnp.bfloat16)


def pair_exchange(totals):
    n = lax.axis_size("pair")
    return [totals[0]] + [ring_shift(totals[(n - d) % n], "pair", n, d) for d in range(1, n)]


def prompt_weights(pair_prompt, n_prompts):
    n = lax.axis_size("pair")
    r = lax.axis_index("pair")
    source = jnp.take(pair_prompt, (r - jnp.arange(n)) % n, mode="clip")
    return (source[:, None] == jnp.arange(n_prompts, dtype=jnp.int32)[None, :]).astype(jnp.float32)


def in_group(width, kv_heads, chunk_heads, group_heads, k):
    head = jnp.arange(width) // (width // kv_heads)
    return ((head % chunk_heads) // group_heads == k)[None]


def shards(
    queries, resp_keys, resp_values, d_out, prefix_kv, prefix_blocks, resp_lengths, pair_prompt
):
    n_prompts = prefix_kv.shape[0]
    planes = jnp.transpose(prefix_kv, (0, 2, 1, 3))
    slot_rows = planes.shape[2]
    chunk_feats = planes.shape[-1]
    n_groups = HEAD_GROUPS if chunk_feats % (HEAD_GROUPS * HEAD_DIM) == 0 else 1
    group_feats = chunk_feats // n_groups
    place = jnp.stack([lax.axis_index("pair"), lax.axis_index("ctx")]).astype(jnp.int32)
    planes, place, blocks, length = lax.optimization_barrier(
        (planes, place, prefix_blocks[0, 0], resp_lengths[0, 0].reshape(1)))
    kv_heads = resp_keys.shape[-1] // HEAD_DIM
    chunk_heads = chunk_feats // HEAD_DIM
    group_heads = group_feats // HEAD_DIM
    earlier = None
    parts = []
    for k in range(n_groups):
        cols = slice(k * group_feats, (k + 1) * group_feats)
        pieces = ctx_gather(pair_gather(planes[..., cols], pair_prompt))
        outs = attention_grads(
            blocks, length, place, queries[0, 0], d_out[0, 0], pieces,
            tree_ctx(), ctx_out_ranges(slot_rows), resp_keys[0, 0], resp_values[0, 0],
            k * (group_feats // HEAD_DIM), None)
        if earlier is None:
            earlier = outs[:3]
        else:
            earlier = tuple(jnp.where(in_group(o.shape[1], kv_heads, chunk_heads, group_heads, k), o, e)
                            for o, e in zip(outs[:3], earlier))
        parts.append(pair_exchange(ctx_reduce(list(outs[3:]))))
    dq, dkr, dvr = earlier
    weights = prompt_weights(pair_prompt, n_prompts)
    d_prefix = jnp.concatenate([
        sum(weights[d][:, None, None, None] * jnp.transpose(got.astype(jnp.float32), (1, 0, 2))[None]
            for d, got in enumerate(part))
        for part in parts], -1)
    return (dq[None, None], dkr[None, None], dvr[None, None], d_prefix)


def solution(mesh):
    placed = (
        P(("dp", "ctx"), "pair", None, None),
        P(("dp", "ctx"), "pair", None, None),
        P(("dp", "ctx"), "pair", None, None),
        P(("dp", "ctx"), "pair", None, None),
        P("dp", "ctx", None, "pair"),
        P(("dp", "ctx"), "pair", None),
        P(("dp", "ctx"), "pair"),
        P("dp"),
    )
    return jax.shard_map(
        shards,
        mesh=mesh,
        in_specs=placed,
        out_specs=(
            P(("dp", "ctx"), "pair", None, None),
            P(("dp", "ctx"), "pair", None, None),
            P(("dp", "ctx"), "pair", None, None),
            P("dp", "ctx", None, "pair"),
        ),
        check_vma=False,
    )
```

```python
import functools

import jax
import jax.numpy as jnp
from jax import lax
from jax.experimental import pallas as pl
from jax.experimental.pallas import tpu as pltpu
from jax.sharding import PartitionSpec as P

KV_HEADS = 8
GROUP = 2
HEAD_DIM = 128
BLOCK = 128
HEAD_GROUPS = 2


scale_factor = 144.0 ** (-0.5)
neg_big = -1e30

NT = (((1,), (1,)), ((), ()))
TN = (((0,), (0,)), ((), ()))


def attention_grad_kernel(layout, blocks_ref, length_ref, place_ref, q_ref, do_ref, *refs):
    n_in, n_slots, slot_rows, xor_slots, out_ranges, aliased, per_chunk = layout
    g = pl.program_id(0)
    slot_in = g // per_chunk
    feat = slice(None) if per_chunk == 1 else pl.ds(pl.multiple_of((g % per_chunk) * HEAD_DIM, HEAD_DIM), HEAD_DIM)
    kv_refs = refs[:n_in]
    kr_ref, vr_ref = refs[n_in:n_in + 2]
    outs = refs[n_in + 2 + (3 if aliased else 0):]
    dq_ref, dkr_ref, dvr_ref = outs[:3]
    piece_refs = outs[3:]
    resp_rows = q_ref.shape[0]
    kp = jnp.concatenate([r[slot_in, 0, :, feat] for r in kv_refs], 0)
    vp = jnp.concatenate([r[slot_in, 1, :, feat] for r in kv_refs], 0)
    pre_rows = kp.shape[0]
    kr = kr_ref[...]
    vr = vr_ref[...]

    slot_blocks = slot_rows // BLOCK
    c = place_ref[1]
    col_block = lax.broadcasted_iota(jnp.int32, (1, pre_rows), 1) // BLOCK
    flag = jnp.zeros((1, pre_rows), jnp.int32)
    for b in range(n_slots * slot_blocks):
        slot, sub = b // slot_blocks, b % slot_blocks
        source = jnp.bitwise_xor(c, slot) if xor_slots else slot
        flag = jnp.where(col_block == b, blocks_ref[source * slot_blocks + sub], flag)
    pre_ok = flag > 0
    rows = GROUP * resp_rows
    row_i = lax.broadcasted_iota(jnp.int32, (rows, resp_rows), 0) % resp_rows
    col_i = lax.broadcasted_iota(jnp.int32, (rows, resp_rows), 1)
    causal = row_i >= col_i
    live = lax.broadcasted_iota(jnp.int32, (rows, 1), 0) % resp_rows < length_ref[0]
    heads = [slice(j * HEAD_DIM, (j + 1) * HEAD_DIM) for j in range(GROUP)]
    q2 = jnp.concatenate([q_ref[:, cols] for cols in heads], 0)
    do2 = jnp.concatenate([do_ref[:, cols] for cols in heads], 0)
    do2 = jnp.where(live, do2, jnp.zeros_like(do2))

    sp = lax.dot_general(q2, kp, NT, preferred_element_type=jnp.float32) * scale_factor
    sr = lax.dot_general(q2, kr, NT, preferred_element_type=jnp.float32) * scale_factor
    sp = jnp.where(pre_ok, sp, neg_big)
    sr = jnp.where(causal, sr, neg_big)
    peak = jnp.maximum(jnp.max(sp, axis=-1, keepdims=True), jnp.max(sr, axis=-1, keepdims=True))
    ep = jnp.exp(sp - peak)
    er = jnp.exp(sr - peak)
    inv = 1.0 / (jnp.sum(ep, axis=-1, keepdims=True) + jnp.sum(er, axis=-1, keepdims=True))
    wp = ep * inv
    wr = er * inv
    pp = wp.astype(jnp.bfloat16)
    pr = wr.astype(jnp.bfloat16)
    att = jnp.dot(pp, vp, preferred_element_type=jnp.float32) + jnp.dot(pr, vr, preferred_element_type=jnp.float32)
    att = att.astype(jnp.bfloat16).astype(jnp.float32)
    delta = jnp.sum(do2.astype(jnp.float32) * att, axis=-1, keepdims=True)
    dpp = lax.dot_general(do2, vp, NT, preferred_element_type=jnp.float32)
    dpr = lax.dot_general(do2, vr, NT, preferred_element_type=jnp.float32)
    dsp = (wp * (dpp - delta)).astype(jnp.bfloat16)
    dsr = (wr * (dpr - delta)).astype(jnp.bfloat16)
    dq = (jnp.dot(dsp, kp, preferred_element_type=jnp.float32) + jnp.dot(
        dsr, kr, preferred_element_type=jnp.float32)) * scale_factor
    dq = dq.astype(dq_ref.dtype)
    for j, cols in enumerate(heads):
        dq_ref[:, cols] = dq[j * resp_rows:(j + 1) * resp_rows]
    dkp = lax.dot_general(dsp, q2, TN, preferred_element_type=jnp.float32)
    dkr = lax.dot_general(dsr, q2, TN, preferred_element_type=jnp.float32)
    dvp = lax.dot_general(pp, do2, TN, preferred_element_type=jnp.float32)
    dvr = lax.dot_general(pr, do2, TN, preferred_element_type=jnp.float32)
    dkr_ref[...] = (dkr * scale_factor).astype(dkr_ref.dtype)
    dvr_ref[...] = dvr.astype(dvr_ref.dtype)
    dkp = (dkp * scale_factor).astype(jnp.bfloat16)
    dvp = dvp.astype(jnp.bfloat16)
    for ref, ranges in zip(piece_refs, out_ranges):
        at = 0
        for start, rows in ranges:
            ref[0, at:at + rows] = dkp[start:start + rows]
            ref[1, at:at + rows] = dvp[start:start + rows]
            at += rows


def attention_grads(blocks, length, place, q, do, pieces, xor_slots, out_ranges, kr, vr, first_head, earlier):
    resp_rows, q_width = q.shape
    n_pair, _, _, chunk_feats = pieces[0].shape
    kv_width = kr.shape[1]
    pre_rows = sum(p.shape[2] for p in pieces)
    chunk_heads = kv_width // n_pair // HEAD_DIM
    per_chunk = chunk_feats // HEAD_DIM
    heads = n_pair * per_chunk
    n_slots = lax.axis_size("ctx")
    slot_rows = pre_rows // n_slots

    def head(g, r):
        return ((r[0] + n_pair - g // per_chunk) % n_pair) * chunk_heads + first_head + g % per_chunk

    def piece_spec(rows):
        return pl.BlockSpec(memory_space=pltpu.VMEM)

    qspec = pl.BlockSpec((resp_rows, GROUP * HEAD_DIM), lambda g, b, n, r: (0, head(g, r)))
    rspec = pl.BlockSpec((resp_rows, HEAD_DIM), lambda g, b, n, r: (0, head(g, r)))
    in_specs = [qspec, qspec]
    in_specs += [piece_spec(p.shape[2]) for p in pieces]
    in_specs += [rspec, rspec]
    operands = [blocks, length, place, q, do] + list(pieces) + [kr, vr]
    aliases = {}
    if earlier is not None:
        in_specs += [pl.BlockSpec(memory_space=pl.ANY)] * 3
        aliases = {len(operands) + i: i for i in range(3)}
        operands += list(earlier)
    out_rows = [sum(rows for _, rows in ranges) for ranges in out_ranges]
    out_specs = [qspec, rspec, rspec] + [
        pl.BlockSpec((None, 2, rows, HEAD_DIM), lambda g, b, n, r: (g // per_chunk, 0, 0, g % per_chunk))
        for rows in out_rows]
    out_shape = [
        jax.ShapeDtypeStruct((resp_rows, q_width), jnp.bfloat16),
        jax.ShapeDtypeStruct((resp_rows, kv_width), jnp.bfloat16),
        jax.ShapeDtypeStruct((resp_rows, kv_width), jnp.bfloat16),
    ] + [jax.ShapeDtypeStruct((n_pair, 2, rows, chunk_feats), jnp.bfloat16) for rows in out_rows]
    layout = (len(pieces), n_slots, slot_rows, xor_slots, tuple(tuple(r) for r in out_ranges), earlier is not None,
              per_chunk)
    flops = 2 * 6 * resp_rows * GROUP * heads * (pre_rows + resp_rows) * HEAD_DIM
    return pl.pallas_call(
        functools.partial(attention_grad_kernel, layout),
        out_shape=tuple(out_shape),
        grid_spec=pltpu.PrefetchScalarGridSpec(
            num_scalar_prefetch=3,
            grid=(heads,),
            in_specs=in_specs,
            out_specs=out_specs,
        ),
        input_output_aliases=aliases,
        cost_estimate=pl.CostEstimate(
            flops=flops,
            transcendentals=resp_rows * GROUP * heads * (pre_rows + resp_rows),
            bytes_accessed=2 * heads * HEAD_DIM * (4 * resp_rows * GROUP + 4 * pre_rows + 4 * resp_rows),
        ),
    )(*operands)


def ring_shift(x, axis, n, d):
    return lax.ppermute(x, axis, [(i, (i + d) % n) for i in range(n)])


def pair_gather(planes, pair_prompt):
    n = lax.axis_size("pair")
    r = lax.axis_index("pair")
    held = [lax.dynamic_index_in_dim(planes, pair_prompt[r], 0, keepdims=False)]
    for d in range(1, n):
        chunk = lax.dynamic_index_in_dim(planes, pair_prompt[(r + d) % n], 0, keepdims=False)
        held.append(ring_shift(chunk, "pair", n, d))
    return jnp.stack(held)


def tree_ctx():
    return lax.axis_size("ctx") == 4


def ctx_gather(x):
    n = lax.axis_size("ctx")
    if not tree_ctx():
        got = lax.all_gather(x, "ctx", axis=0, tiled=False)
        return [got[j] for j in range(n)]
    along_x = [(i, i ^ 1) for i in range(n)]
    along_y = [(i, i ^ 2) for i in range(n)]
    from_x = lax.ppermute(x, "ctx", along_x)
    from_y = lax.ppermute(x, "ctx", along_y)
    half = x.shape[2] // 2
    far_a = lax.ppermute(from_y[:, :, :half], "ctx", along_x)
    far_b = lax.ppermute(from_x[:, :, half:], "ctx", along_y)
    return [x, from_x, from_y, far_a, far_b]


def ctx_out_ranges(slot_rows):
    n = lax.axis_size("ctx")
    return [[(j * slot_rows, slot_rows)] for j in range(n)]


def ctx_reduce(pieces):
    n = lax.axis_size("ctx")
    if not tree_ctx():
        got = lax.all_to_all(jnp.stack(pieces), "ctx", split_axis=0, concat_axis=0, tiled=True)
        return jnp.sum(got.astype(jnp.float32), axis=0).astype(jnp.bfloat16)
    got = [pieces[0]] + [lax.ppermute(pieces[j], "ctx", [(i, i ^ j) for i in range(n)]) for j in range(1, n)]
    total = (got[0].astype(jnp.float32) + got[1].astype(jnp.float32)) + (
        got[2].astype(jnp.float32) + got[3].astype(jnp.float32))
    return total.astype(jnp.bfloat16)


def pair_exchange(totals):
    n = lax.axis_size("pair")
    return [totals[0]] + [ring_shift(totals[(n - d) % n], "pair", n, d) for d in range(1, n)]


def prompt_weights(pair_prompt, n_prompts):
    n = lax.axis_size("pair")
    r = lax.axis_index("pair")
    source = jnp.take(pair_prompt, (r - jnp.arange(n)) % n, mode="clip")
    return (source[:, None] == jnp.arange(n_prompts, dtype=jnp.int32)[None, :]).astype(jnp.float32)


def in_group(width, kv_heads, chunk_heads, group_heads, k):
    head = jnp.arange(width) // (width // kv_heads)
    return ((head % chunk_heads) // group_heads == k)[None]


def shards(
    queries, resp_keys, resp_values, d_out, prefix_kv, prefix_blocks, resp_lengths, pair_prompt
):
    n_prompts = prefix_kv.shape[0]
    planes = jnp.transpose(prefix_kv, (0, 2, 1, 3))
    slot_rows = planes.shape[2]
    chunk_feats = planes.shape[-1]
    n_groups = HEAD_GROUPS if chunk_feats % (HEAD_GROUPS * HEAD_DIM) == 0 else 1
    group_feats = chunk_feats // n_groups
    place = jnp.stack([lax.axis_index("pair"), lax.axis_index("ctx")]).astype(jnp.int32)
    kv_heads = resp_keys.shape[-1] // HEAD_DIM
    chunk_heads = chunk_feats // HEAD_DIM
    group_heads = group_feats // HEAD_DIM
    earlier = None
    parts = []
    for k in range(n_groups):
        cols = slice(k * group_feats, (k + 1) * group_feats)
        pieces = ctx_gather(pair_gather(planes[..., cols], pair_prompt))
        outs = attention_grads(
            prefix_blocks[0, 0], resp_lengths[0, 0].reshape(1), place, queries[0, 0], d_out[0, 0], pieces,
            tree_ctx(), ctx_out_ranges(slot_rows), resp_keys[0, 0], resp_values[0, 0],
            k * (group_feats // HEAD_DIM), None)
        if earlier is None:
            earlier = outs[:3]
        else:
            earlier = tuple(jnp.where(in_group(o.shape[1], kv_heads, chunk_heads, group_heads, k), o, e)
                            for o, e in zip(outs[:3], earlier))
        parts.append(pair_exchange(ctx_reduce(list(outs[3:]))))
    dq, dkr, dvr = earlier
    weights = prompt_weights(pair_prompt, n_prompts)
    d_prefix = jnp.concatenate([
        sum(weights[d][:, None, None, None] * jnp.transpose(got.astype(jnp.float32), (1, 0, 2))[None]
            for d, got in enumerate(part))
        for part in parts], -1)
    return (dq[None, None], dkr[None, None], dvr[None, None], d_prefix)


def solution(mesh):
    placed = (
        P(("dp", "ctx"), "pair", None, None),
        P(("dp", "ctx"), "pair", None, None),
        P(("dp", "ctx"), "pair", None, None),
        P(("dp", "ctx"), "pair", None, None),
        P("dp", "ctx", None, "pair"),
        P(("dp", "ctx"), "pair", None),
        P(("dp", "ctx"), "pair"),
        P("dp"),
    )
    return jax.shard_map(
        shards,
        mesh=mesh,
        in_specs=placed,
        out_specs=(
            P(("dp", "ctx"), "pair", None, None),
            P(("dp", "ctx"), "pair", None, None),
            P(("dp", "ctx"), "pair", None, None),
            P("dp", "ctx", None, "pair"),
        ),
        check_vma=False,
    )
```

```python
import functools

import jax
import jax.numpy as jnp
from jax import lax
from jax.experimental import pallas as pl
from jax.experimental.pallas import tpu as pltpu
from jax.sharding import PartitionSpec as P

KV_HEADS = 8
GROUP = 2
HEAD_DIM = 128
BLOCK = 128
HEAD_GROUPS = 2


scale_factor = 144.0 ** (-0.5)
neg_big = -1e30

NT = (((1,), (1,)), ((), ()))
TN = (((0,), (0,)), ((), ()))


def attention_grad_kernel(layout, blocks_ref, length_ref, place_ref, q_ref, do_ref, *refs):
    n_in, n_slots, slot_rows, xor_slots, out_ranges, aliased = layout
    kv_refs = refs[:n_in]
    kr_ref, vr_ref = refs[n_in:n_in + 2]
    outs = refs[n_in + 2 + (3 if aliased else 0):]
    dq_ref, dkr_ref, dvr_ref = outs[:3]
    piece_refs = outs[3:]
    resp_rows = q_ref.shape[0]
    kp = jnp.concatenate([r[0] for r in kv_refs], 0)
    vp = jnp.concatenate([r[1] for r in kv_refs], 0)
    pre_rows = kp.shape[0]
    kr = kr_ref[...]
    vr = vr_ref[...]

    slot_blocks = slot_rows // BLOCK
    c = place_ref[1]
    col_block = lax.broadcasted_iota(jnp.int32, (1, pre_rows), 1) // BLOCK
    flag = jnp.zeros((1, pre_rows), jnp.int32)
    for b in range(n_slots * slot_blocks):
        slot, sub = b // slot_blocks, b % slot_blocks
        source = jnp.bitwise_xor(c, slot) if xor_slots else slot
        flag = jnp.where(col_block == b, blocks_ref[source * slot_blocks + sub], flag)
    pre_ok = flag > 0
    rows = GROUP * resp_rows
    row_i = lax.broadcasted_iota(jnp.int32, (rows, resp_rows), 0) % resp_rows
    col_i = lax.broadcasted_iota(jnp.int32, (rows, resp_rows), 1)
    causal = row_i >= col_i
    live = lax.broadcasted_iota(jnp.int32, (rows, 1), 0) % resp_rows < length_ref[0]
    heads = [slice(j * HEAD_DIM, (j + 1) * HEAD_DIM) for j in range(GROUP)]
    q2 = jnp.concatenate([q_ref[:, cols] for cols in heads], 0)
    do2 = jnp.concatenate([do_ref[:, cols] for cols in heads], 0)
    do2 = jnp.where(live, do2, jnp.zeros_like(do2))

    sp = lax.dot_general(q2, kp, NT, preferred_element_type=jnp.float32) * scale_factor
    sr = lax.dot_general(q2, kr, NT, preferred_element_type=jnp.float32) * scale_factor
    sp = jnp.where(pre_ok, sp, neg_big)
    sr = jnp.where(causal, sr, neg_big)
    peak = jnp.maximum(jnp.max(sp, axis=-1, keepdims=True), jnp.max(sr, axis=-1, keepdims=True))
    ep = jnp.exp(sp - peak)
    er = jnp.exp(sr - peak)
    inv = 1.0 / (jnp.sum(ep, axis=-1, keepdims=True) + jnp.sum(er, axis=-1, keepdims=True))
    wp = ep * inv
    wr = er * inv
    pp = wp.astype(jnp.bfloat16)
    pr = wr.astype(jnp.bfloat16)
    att = jnp.dot(pp, vp, preferred_element_type=jnp.float32) + jnp.dot(pr, vr, preferred_element_type=jnp.float32)
    att = att.astype(jnp.bfloat16).astype(jnp.float32)
    delta = jnp.sum(do2.astype(jnp.float32) * att, axis=-1, keepdims=True)
    dpp = lax.dot_general(do2, vp, NT, preferred_element_type=jnp.float32)
    dpr = lax.dot_general(do2, vr, NT, preferred_element_type=jnp.float32)
    dsp = (wp * (dpp - delta)).astype(jnp.bfloat16)
    dsr = (wr * (dpr - delta)).astype(jnp.bfloat16)
    dq = (jnp.dot(dsp, kp, preferred_element_type=jnp.float32) + jnp.dot(
        dsr, kr, preferred_element_type=jnp.float32)) * scale_factor
    dq = dq.astype(dq_ref.dtype)
    for j, cols in enumerate(heads):
        dq_ref[:, cols] = dq[j * resp_rows:(j + 1) * resp_rows]
    dkp = lax.dot_general(dsp, q2, TN, preferred_element_type=jnp.float32)
    dkr = lax.dot_general(dsr, q2, TN, preferred_element_type=jnp.float32)
    dvp = lax.dot_general(pp, do2, TN, preferred_element_type=jnp.float32)
    dvr = lax.dot_general(pr, do2, TN, preferred_element_type=jnp.float32)
    dkr_ref[...] = (dkr * scale_factor).astype(dkr_ref.dtype)
    dvr_ref[...] = dvr.astype(dvr_ref.dtype)
    dkp = (dkp * scale_factor).astype(jnp.bfloat16)
    dvp = dvp.astype(jnp.bfloat16)
    for ref, ranges in zip(piece_refs, out_ranges):
        at = 0
        for start, rows in ranges:
            ref[0, at:at + rows] = dkp[start:start + rows]
            ref[1, at:at + rows] = dvp[start:start + rows]
            at += rows


def attention_grads(blocks, length, place, q, do, pieces, xor_slots, out_ranges, kr, vr, first_head, earlier):
    resp_rows, q_width = q.shape
    n_pair, _, _, chunk_feats = pieces[0].shape
    kv_width = kr.shape[1]
    pre_rows = sum(p.shape[2] for p in pieces)
    chunk_heads = kv_width // n_pair // HEAD_DIM
    per_chunk = chunk_feats // HEAD_DIM
    heads = n_pair * per_chunk
    n_slots = lax.axis_size("ctx")
    slot_rows = pre_rows // n_slots

    def head(g, r):
        return ((r[0] + n_pair - g // per_chunk) % n_pair) * chunk_heads + first_head + g % per_chunk

    def piece_spec(rows):
        return pl.BlockSpec((None, 2, rows, HEAD_DIM), lambda g, b, n, r: (g // per_chunk, 0, 0, g % per_chunk))

    qspec = pl.BlockSpec((resp_rows, GROUP * HEAD_DIM), lambda g, b, n, r: (0, head(g, r)))
    rspec = pl.BlockSpec((resp_rows, HEAD_DIM), lambda g, b, n, r: (0, head(g, r)))
    in_specs = [qspec, qspec]
    in_specs += [piece_spec(p.shape[2]) for p in pieces]
    in_specs += [rspec, rspec]
    operands = [blocks, length, place, q, do] + list(pieces) + [kr, vr]
    aliases = {}
    if earlier is not None:
        in_specs += [pl.BlockSpec(memory_space=pl.ANY)] * 3
        aliases = {len(operands) + i: i for i in range(3)}
        operands += list(earlier)
    out_rows = [sum(rows for _, rows in ranges) for ranges in out_ranges]
    out_specs = [qspec, rspec, rspec] + [
        pl.BlockSpec((None, 2, rows, HEAD_DIM), lambda g, b, n, r: (g // per_chunk, 0, 0, g % per_chunk))
        for rows in out_rows]
    out_shape = [
        jax.ShapeDtypeStruct((resp_rows, q_width), jnp.bfloat16),
        jax.ShapeDtypeStruct((resp_rows, kv_width), jnp.bfloat16),
        jax.ShapeDtypeStruct((resp_rows, kv_width), jnp.bfloat16),
    ] + [jax.ShapeDtypeStruct((n_pair, 2, rows, chunk_feats), jnp.bfloat16) for rows in out_rows]
    layout = (len(pieces), n_slots, slot_rows, xor_slots, tuple(tuple(r) for r in out_ranges), earlier is not None)
    flops = 2 * 6 * resp_rows * GROUP * heads * (pre_rows + resp_rows) * HEAD_DIM
    return pl.pallas_call(
        functools.partial(attention_grad_kernel, layout),
        out_shape=tuple(out_shape),
        grid_spec=pltpu.PrefetchScalarGridSpec(
            num_scalar_prefetch=3,
            grid=(heads,),
            in_specs=in_specs,
            out_specs=out_specs,
        ),
        input_output_aliases=aliases,
        cost_estimate=pl.CostEstimate(
            flops=flops,
            transcendentals=resp_rows * GROUP * heads * (pre_rows + resp_rows),
            bytes_accessed=2 * heads * HEAD_DIM * (4 * resp_rows * GROUP + 4 * pre_rows + 4 * resp_rows),
        ),
    )(*operands)


def ring_shift(x, axis, n, d):
    return lax.ppermute(x, axis, [(i, (i + d) % n) for i in range(n)])


def pair_gather(planes, pair_prompt):
    n = lax.axis_size("pair")
    r = lax.axis_index("pair")
    held = [lax.dynamic_index_in_dim(planes, pair_prompt[r], 0, keepdims=False)]
    for d in range(1, n):
        chunk = lax.dynamic_index_in_dim(planes, pair_prompt[(r + d) % n], 0, keepdims=False)
        held.append(ring_shift(chunk, "pair", n, d))
    return jnp.stack(held)


def tree_ctx():
    return lax.axis_size("ctx") == 4


def ctx_gather(x, direct=False):
    n = lax.axis_size("ctx")
    if not tree_ctx():
        got = lax.all_gather(x, "ctx", axis=0, tiled=False)
        return [got[j] for j in range(n)]
    if direct:
        return [x] + [lax.ppermute(x, "ctx", [(i, i ^ j) for i in range(n)]) for j in range(1, n)]
    along_x = [(i, i ^ 1) for i in range(n)]
    along_y = [(i, i ^ 2) for i in range(n)]
    from_x = lax.ppermute(x, "ctx", along_x)
    from_y = lax.ppermute(x, "ctx", along_y)
    half = x.shape[2] // 2
    far_a = lax.ppermute(from_y[:, :, :half], "ctx", along_x)
    far_b = lax.ppermute(from_x[:, :, half:], "ctx", along_y)
    return [x, from_x, from_y, far_a, far_b]


def ctx_out_ranges(slot_rows):
    n = lax.axis_size("ctx")
    return [[(j * slot_rows, slot_rows)] for j in range(n)]


def ctx_reduce(pieces):
    n = lax.axis_size("ctx")
    if not tree_ctx():
        got = lax.all_to_all(jnp.stack(pieces), "ctx", split_axis=0, concat_axis=0, tiled=True)
        return jnp.sum(got.astype(jnp.float32), axis=0).astype(jnp.bfloat16)
    got = [pieces[0]] + [lax.ppermute(pieces[j], "ctx", [(i, i ^ j) for i in range(n)]) for j in range(1, n)]
    total = (got[0].astype(jnp.float32) + got[1].astype(jnp.float32)) + (
        got[2].astype(jnp.float32) + got[3].astype(jnp.float32))
    return total.astype(jnp.bfloat16)


def pair_exchange(totals):
    n = lax.axis_size("pair")
    return [totals[0]] + [ring_shift(totals[(n - d) % n], "pair", n, d) for d in range(1, n)]


def prompt_weights(pair_prompt, n_prompts):
    n = lax.axis_size("pair")
    r = lax.axis_index("pair")
    source = jnp.take(pair_prompt, (r - jnp.arange(n)) % n, mode="clip")
    return (source[:, None] == jnp.arange(n_prompts, dtype=jnp.int32)[None, :]).astype(jnp.float32)


def in_group(width, kv_heads, chunk_heads, group_heads, k):
    head = jnp.arange(width) // (width // kv_heads)
    return ((head % chunk_heads) // group_heads == k)[None]


def shards(
    queries, resp_keys, resp_values, d_out, prefix_kv, prefix_blocks, resp_lengths, pair_prompt
):
    n_prompts = prefix_kv.shape[0]
    planes = jnp.transpose(prefix_kv, (0, 2, 1, 3))
    slot_rows = planes.shape[2]
    chunk_feats = planes.shape[-1]
    n_groups = HEAD_GROUPS if chunk_feats % (HEAD_GROUPS * HEAD_DIM) == 0 else 1
    group_feats = chunk_feats // n_groups
    place = jnp.stack([lax.axis_index("pair"), lax.axis_index("ctx")]).astype(jnp.int32)
    kv_heads = resp_keys.shape[-1] // HEAD_DIM
    chunk_heads = chunk_feats // HEAD_DIM
    group_heads = group_feats // HEAD_DIM
    earlier = None
    parts = []
    for k in range(n_groups):
        cols = slice(k * group_feats, (k + 1) * group_feats)
        pieces = ctx_gather(pair_gather(planes[..., cols], pair_prompt), direct=k > 0)
        outs = attention_grads(
            prefix_blocks[0, 0], resp_lengths[0, 0].reshape(1), place, queries[0, 0], d_out[0, 0], pieces,
            tree_ctx(), ctx_out_ranges(slot_rows), resp_keys[0, 0], resp_values[0, 0],
            k * (group_feats // HEAD_DIM), None)
        if earlier is None:
            earlier = outs[:3]
        else:
            earlier = tuple(jnp.where(in_group(o.shape[1], kv_heads, chunk_heads, group_heads, k), o, e)
                            for o, e in zip(outs[:3], earlier))
        parts.append(pair_exchange(ctx_reduce(list(outs[3:]))))
    dq, dkr, dvr = earlier
    weights = prompt_weights(pair_prompt, n_prompts)
    d_prefix = jnp.concatenate([
        sum(weights[d][:, None, None, None] * jnp.transpose(got.astype(jnp.float32), (1, 0, 2))[None]
            for d, got in enumerate(part))
        for part in parts], -1)
    return (dq[None, None], dkr[None, None], dvr[None, None], d_prefix)


def solution(mesh):
    placed = (
        P(("dp", "ctx"), "pair", None, None),
        P(("dp", "ctx"), "pair", None, None),
        P(("dp", "ctx"), "pair", None, None),
        P(("dp", "ctx"), "pair", None, None),
        P("dp", "ctx", None, "pair"),
        P(("dp", "ctx"), "pair", None),
        P(("dp", "ctx"), "pair"),
        P("dp"),
    )
    return jax.shard_map(
        shards,
        mesh=mesh,
        in_specs=placed,
        out_specs=(
            P(("dp", "ctx"), "pair", None, None),
            P(("dp", "ctx"), "pair", None, None),
            P(("dp", "ctx"), "pair", None, None),
            P("dp", "ctx", None, "pair"),
        ),
        check_vma=False,
    )
```
